32 devices in a mesh: groups: 2 (over y), region: 4 (over z), seg: 2 (over x), tb: 2 (over core).
Axes of the slice: x: 2, y: 2, z: 4, core: 2. Of those that a mesh axis runs over, the one named last changes fastest.
Arguments:
- records: bfloat16 [16, 3, 1024], P(('groups', 'region'), None, 'seg'), parts along dimension 0, may hold values from -6 to 6
- templates: bfloat16 [4, 64, 16, 3, 512], P(('groups', 'tb'), None, 'region'), parts along dimension 0, may hold values from -6 to 6
- channel_mask: int32 [4, 64, 16, 3], P(('groups', 'tb'), None, 'region'), parts along dimension 0, may hold values 0 or 1
- station_region: int32 [16], P(('groups', 'region')), parts along dimension 0, may hold values from 0 to 3, as said below
Outputs:
- detect: float32 [4, 64, 1024], P(('groups', 'tb'), None, 'seg'), parts along dimension 0
The draws below stay inside these ranges and needn't reach their ends.
There are 2 independent parts, one for each index of `groups`. The reference program is written for one: setup_inputs(seed, part) draws one part's arguments, and reference() takes and returns one part's arrays. A program takes and returns all parts, laid end to end along the dimension named above; each array names one. Nothing has to cross between parts.
Inputs may be any that keep to these rules, and one draw needn't show every extreme that they name: `station_region`: the 2 stations of one device (aligned blocks of 2 station numbers) name distinct regions. No region is named by more than 4 stations, and one region by exactly 4.
All inputs are finite; a program needn't handle non-finite values. No bound on the sum of `channel_mask` on one device may be relied on, other than what follows from the above.
Results may differ from the reference program's by a relative error of at most 0.0041.
Values may be sent and summed in bfloat16 or wider, within the bound.
No kernel may reach another device: no remote copies, remote signals or barrier semaphores. Data moves between devices by JAX's collectives and lax.ppermute only.
A program may use at most 64 MiB of HBM per device.

```python
import jax
import jax.numpy as jnp
from jax import lax

TLEN = 512
K = 64
BATCHES = 2
REGIONS = 4
STA_DEV = 2
STATIONS = 8
CAP = 4
TOTAL_LEN = 1024


def draw_station_region(key, part):
    base_key = jax.random.fold_in(key, 11)
    key_regions, key_roles, key_local = jax.random.split(base_key, 3)
    region_order = jax.random.permutation(key_regions, REGIONS)
    sender_roles = jax.random.permutation(key_roles, REGIONS)
    local_scores = jax.random.randint(key_local, (REGIONS, STA_DEV), 0, 1 << 20) * STA_DEV
    local_scores = local_scores + jnp.arange(STA_DEV, dtype=jnp.int32)[None, :]
    position = jnp.argsort(jnp.argsort(local_scores, axis=1, stable=True), axis=1, stable=True)
    sender_role = sender_roles[:, None]
    cyclic = max(REGIONS - 1, 1)
    heavy_pick = jnp.where(position == 0, 0, (sender_role + position - 1) % cyclic + 1)
    light_pick = (sender_role + position) % cyclic + 1
    chosen = jnp.where(sender_role < CAP, heavy_pick, light_pick)
    return region_order[chosen].reshape(STATIONS).astype(jnp.int32)


def touch_ends(array, own_key, least, largest):
    spot = [jax.random.randint(jax.random.fold_in(own_key, axis), (), 0, length) for axis, length in enumerate(array.shape)]
    widest = array.shape.index(max(array.shape))
    neighbour = spot[:widest] + [(spot[widest] + 1) % array.shape[widest]] + spot[widest + 1:]
    return array.at[tuple(spot)].set(least).at[tuple(neighbour)].set(largest)


def block_levels(key, shape, cuts, low, top_value):
    level = 1.0
    for dim, blocks in cuts:
        heights = jax.random.uniform(jax.random.fold_in(jax.random.fold_in(key, 6), dim), (blocks,), jnp.float32, low / len(cuts), top_value / len(cuts))
        level = level * jnp.repeat(jnp.exp(heights), shape[dim] // blocks).reshape((-1,) + (1,) * (len(shape) - 1 - dim))
    return level


def noise(key, shape, deviation, bound, shards=(), kind=jnp.bfloat16):
    entries = deviation * jax.random.normal(key, shape, jnp.float32)
    if shards:
        entries = entries * block_levels(key, shape, shards, -0.22, 0.18)
    return jnp.clip(entries, -bound, bound).astype(kind)


def setup_inputs(seed: int = 0, part: int = 0) -> dict:
    seeds = jax.random.split(jax.random.key(seed), 5)
    part_keys = jax.random.split(jax.random.fold_in(seeds[4], part), 5)
    records = noise(part_keys[0], (STATIONS, 3, TOTAL_LEN), 1.0, 6.0, ((0, 4), (2, 2)))
    templates = noise(part_keys[1], (BATCHES, K, REGIONS * CAP, 3, TLEN), 1.0, 6.0, ((0, 2), (2, 4)))
    channel_mask = touch_ends((jax.random.randint(part_keys[2], (BATCHES, K, REGIONS * CAP, 3), 0, 4) < 3).astype(jnp.int32), jax.random.fold_in(part_keys[2], 1), 0, 1)
    station_region = draw_station_region(jax.random.fold_in(jax.random.fold_in(seeds[4], part), 71), part)
    return dict(records=records, templates=templates, channel_mask=channel_mask, station_region=station_region)


def window_rows(stretch, columns, filter_taps):
    channels, window_span = stretch.shape
    repeated = jnp.broadcast_to(stretch[:, None, :], (channels, columns + 1, window_span))
    repeated = repeated.reshape(channels, (columns + 1) * window_span)
    shifted = repeated[:, :columns * (window_span + 1)].reshape(channels, columns, window_span + 1)
    return shifted[:, :, :filter_taps]

def scaled_windows(stretch, columns, filter_taps):
    widened = window_rows(stretch, columns, filter_taps).astype(jnp.float32)
    energy = lax.optimization_barrier(jnp.sum(widened * widened, axis=2))
    return (widened / jnp.sqrt(jnp.maximum(energy, 1.0))[:, :, None]).astype(jnp.bfloat16)

def reference(records, templates, channel_mask, station_region):
    stations = records.shape[0]
    total_len = records.shape[2]
    station_ids = jnp.arange(stations, dtype=jnp.int32)
    earlier = (station_region[None, :] == station_region[:, None]) & (station_ids[None, :] < station_ids[:, None])
    slot_ranks = lax.optimization_barrier(jnp.sum(earlier.astype(jnp.int32), axis=1))
    slot_of = station_region * CAP + slot_ranks
    slot_index = jnp.arange(REGIONS * CAP, dtype=jnp.int32)
    placing = slot_index[:, None] == slot_of[None, :]
    owned_rows = jnp.dot(placing.astype(jnp.bfloat16), records.reshape(stations, -1), preferred_element_type=jnp.float32).astype(jnp.bfloat16)
    owned_rows = owned_rows.reshape(REGIONS * CAP, 3, total_len)
    filled = lax.optimization_barrier(jnp.sum(placing.astype(jnp.float32), axis=1))
    padding = jnp.zeros((REGIONS * CAP, 3, TLEN), jnp.bfloat16)
    flat_owned = jnp.concatenate([owned_rows, padding], axis=2).reshape(REGIONS * CAP * 3, total_len + TLEN)
    weight = channel_mask.astype(jnp.float32) * filled[None, None, :, None]
    widened_templates = templates.astype(jnp.float32)
    template_norm = jnp.sqrt(lax.optimization_barrier(jnp.sum(widened_templates * widened_templates, axis=4, keepdims=True)) + 1e-06)
    normed = (widened_templates * weight[..., None] / template_norm).astype(jnp.bfloat16)
    normed_wide = normed.reshape(BATCHES * K, REGIONS * CAP * 3, TLEN).astype(jnp.float32)
    columns = 128

    def one_block(block_index):
        offset = block_index * columns
        stretch = lax.dynamic_slice_in_dim(flat_owned, offset, columns + TLEN - 1, 1)
        scaled = scaled_windows(stretch, columns, TLEN).astype(jnp.float32)
        return jnp.einsum('rct,cut->ru', normed_wide, scaled)
    blocks = lax.map(one_block, jnp.arange(total_len // columns, dtype=jnp.int32))
    stacked = jnp.transpose(blocks, (1, 0, 2)).reshape(BATCHES * K, total_len)
    power_sum = lax.optimization_barrier(jnp.mean(stacked * stacked, axis=1))
    detect = stacked / jnp.sqrt(power_sum + 1e-06)[:, None]
    return detect.reshape(BATCHES, K, total_len)
```

```python
import jax
import jax.numpy as jnp
from jax import lax
from jax.sharding import PartitionSpec as P


def window_rows(stretch, columns, filter_taps):
    channels, window_span = stretch.shape
    repeated = jnp.broadcast_to(stretch[:, None, :], (channels, columns + 1, window_span))
    repeated = repeated.reshape(channels, (columns + 1) * window_span)
    shifted = repeated[:, : columns * (window_span + 1)].reshape(channels, columns, window_span + 1)
    return shifted[:, :, :filter_taps]


def scaled_windows(stretch, columns, filter_taps):
    widened = window_rows(stretch, columns, filter_taps).astype(jnp.float32)
    energy = jnp.sum(widened * widened, axis=2)
    return (widened / jnp.sqrt(jnp.maximum(energy, 1.0))[:, :, None]).astype(jnp.bfloat16)


def correlate(normed, flat_owned, seg_len):
    stacked_rows, channels, filter_taps = normed.shape
    columns = 128

    def one_block(block_index, stacked):
        offset = block_index * columns
        stretch = lax.dynamic_slice_in_dim(flat_owned, offset, columns + filter_taps - 1, 1)
        scaled = scaled_windows(stretch, columns, filter_taps)
        block_sum = lax.dot_general(
            normed, scaled, (((1, 2), (0, 2)), ((), ())), preferred_element_type=jnp.float32
        )
        return lax.dynamic_update_slice_in_dim(stacked, block_sum, offset, 1)

    return lax.fori_loop(
        0, seg_len // columns, one_block, jnp.zeros((stacked_rows, seg_len), jnp.float32)
    )


def ordered_sum(part, axis):
    size = lax.axis_size(axis)
    if size == 1:
        return part
    me = lax.axis_index(axis)
    received = [part] + [
        lax.ppermute(part, axis, [(i, (i + k) % size) for i in range(size)]) for k in range(1, size)
    ]
    stack = jnp.stack(received)
    order = (me - jnp.arange(size, dtype=jnp.int32)) % size
    return jnp.sum(jnp.take(stack, order, axis=0), axis=0)


def gather_owned(records, station_region, capacity, filter_taps):
    local_count, components, seg_len = records.shape
    regions = lax.axis_size("region")
    segs = lax.axis_size("seg")
    tag = jnp.broadcast_to(station_region.astype(jnp.bfloat16)[:, None, None], (local_count, 1, seg_len))
    payload = jnp.concatenate([records, tag], axis=1)
    axes = ("region", "seg")
    same_seg = [payload]
    for k in range(1, regions):
        pairs = [
            (r * segs + s, ((r + k) % regions) * segs + s) for r in range(regions) for s in range(segs)
        ]
        same_seg.append(lax.ppermute(payload, axes, pairs))
    next_seg = []
    for k in range(regions):
        pairs = [
            (r * segs + s + 1, ((r + k) % regions) * segs + s)
            for r in range(regions)
            for s in range(segs - 1)
        ]
        next_seg.append(lax.ppermute(records[:, :, :filter_taps], axes, pairs))
    me = lax.axis_index("region")
    order = (me - jnp.arange(regions, dtype=jnp.int32)) % regions
    here = jnp.take(jnp.stack(same_seg), order, axis=0)
    ahead = jnp.take(jnp.stack(next_seg), order, axis=0)
    stations = regions * local_count
    here = here.reshape(stations, components + 1, seg_len)
    ahead = ahead.reshape(stations, components, filter_taps)
    region_of = here[:, components, 0].astype(jnp.int32)
    rows = jnp.concatenate([here[:, :components, :], ahead], axis=2)
    station_ids = jnp.arange(stations, dtype=jnp.int32)
    earlier = (region_of[None, :] == region_of[:, None]) & (station_ids[None, :] < station_ids[:, None])
    ranks = jnp.sum(earlier.astype(jnp.int32), axis=1)
    slot_index = jnp.arange(capacity, dtype=jnp.int32)
    placing = (region_of[None, :] == me) & (ranks[None, :] == slot_index[:, None])
    owned_rows = jnp.dot(
        placing.astype(jnp.bfloat16), rows.reshape(stations, -1), preferred_element_type=jnp.float32
    ).astype(jnp.bfloat16)
    owned_rows = owned_rows.reshape(capacity, components, seg_len + filter_taps)
    filled = jnp.sum(placing.astype(jnp.float32), axis=1)
    return owned_rows, filled


def per_device(records, templates, channel_mask, station_region):
    local_batches, kept, capacity, components, filter_taps = templates.shape
    seg_len = records.shape[2]
    owned_rows, filled = gather_owned(records, station_region, capacity, filter_taps)
    flat_owned = owned_rows.reshape(capacity * components, seg_len + filter_taps)
    weight = channel_mask.astype(jnp.float32) * filled[None, None, :, None]
    widened_templates = templates.astype(jnp.float32)
    template_norm = jnp.sqrt(
        jnp.sum(widened_templates * widened_templates, axis=4, keepdims=True) + 1e-06
    )
    normed = (widened_templates * weight[..., None] / template_norm).astype(jnp.bfloat16)
    normed = normed.reshape(local_batches * kept, capacity * components, filter_taps)
    total_len = seg_len * lax.axis_size("seg")
    stacked = ordered_sum(correlate(normed, flat_owned, seg_len), "region")
    power_sum = ordered_sum(jnp.sum(stacked * stacked, axis=1), "seg")
    detect = stacked / jnp.sqrt(power_sum / total_len + 1e-06)[:, None]
    return detect.reshape(local_batches, kept, seg_len)


def solution(mesh):
    placed = (
        P(("groups", "region"), None, "seg"),
        P(("groups", "tb"), None, "region", None, None),
        P(("groups", "tb"), None, "region", None),
        P(("groups", "region")),
    )
    return jax.shard_map(
        per_device,
        mesh=mesh,
        in_specs=placed,
        out_specs=P(("groups", "tb"), None, "seg"),
        check_vma=False,
    )
```

```python
import jax
import jax.numpy as jnp
from jax import lax
from jax.sharding import PartitionSpec as P
from jax.experimental import pallas as pl
from jax.experimental.pallas import tpu as pltpu


def hankel_kernel(x_ref, n_ref, o_ref, h_ref):
    channels, rows, width = n_ref.shape
    taps_blocks = width // 128
    out_blocks = o_ref.shape[1] // 128
    blocks = taps_blocks + out_blocks
    row = lax.broadcasted_iota(jnp.int32, (128, 128), 0)
    lane = lax.broadcasted_iota(jnp.int32, (128, 128), 1)
    low = lane <= row

    def one_channel(c, acc):
        rolled = [
            pltpu.roll(x_ref[pl.ds(c * blocks + m, 128, stride=0), :], 1, 1, stride=1, stride_axis=0)
            for m in range(blocks)
        ]
        squares = []
        for m in range(blocks - 1):
            window = jnp.where(low, rolled[m], rolled[m + 1])
            squares.append(jnp.sum(window * window, axis=0, keepdims=True))
            window = window.astype(jnp.bfloat16)
            for p in range(taps_blocks):
                a = m - p
                if 0 <= a < out_blocks:
                    h_ref[p * 128 : (p + 1) * 128, a * 128 : (a + 1) * 128] = window
        energy = jnp.concatenate(
            [sum(squares[a + p] for p in range(taps_blocks)) for a in range(out_blocks)], axis=1
        )
        part = jnp.dot(n_ref[c], h_ref[...], preferred_element_type=jnp.float32)
        return acc + part * (1.0 / jnp.sqrt(jnp.maximum(energy, 1.0)))

    o_ref[...] = lax.fori_loop(0, channels, one_channel, jnp.zeros(o_ref.shape, jnp.float32))


def correlate(normed, flat_owned, seg_len):
    rows, channels, filter_taps = normed.shape
    flipped = normed.reshape(rows, channels, filter_taps // 128, 128)[..., ::-1]
    flipped = jnp.transpose(flipped.reshape(rows, channels, filter_taps), (1, 0, 2))
    blocks = flat_owned.astype(jnp.float32).reshape(channels * (flat_owned.shape[1] // 128), 128)
    return pl.pallas_call(
        hankel_kernel,
        out_shape=jax.ShapeDtypeStruct((rows, seg_len), jnp.float32),
        scratch_shapes=[pltpu.VMEM((filter_taps, seg_len), jnp.bfloat16)],
    )(blocks, flipped)


def ordered_sum(part, axis):
    size = lax.axis_size(axis)
    if size == 1:
        return part
    me = lax.axis_index(axis)
    received = [part] + [
        lax.ppermute(part, axis, [(i, (i + k) % size) for i in range(size)]) for k in range(1, size)
    ]
    stack = jnp.stack(received)
    order = (me - jnp.arange(size, dtype=jnp.int32)) % size
    return jnp.sum(jnp.take(stack, order, axis=0), axis=0)


def gather_owned(records, station_region, capacity, filter_taps):
    local_count, components, seg_len = records.shape
    regions = lax.axis_size("region")
    segs = lax.axis_size("seg")
    tag = jnp.broadcast_to(station_region.astype(jnp.bfloat16)[:, None, None], (local_count, 1, seg_len))
    payload = jnp.concatenate([records, tag], axis=1)
    axes = ("region", "seg")
    same_seg = [payload]
    for k in range(1, regions):
        pairs = [
            (r * segs + s, ((r + k) % regions) * segs + s) for r in range(regions) for s in range(segs)
        ]
        same_seg.append(lax.ppermute(payload, axes, pairs))
    next_seg = []
    for k in range(regions):
        pairs = [
            (r * segs + s + 1, ((r + k) % regions) * segs + s)
            for r in range(regions)
            for s in range(segs - 1)
        ]
        next_seg.append(lax.ppermute(records[:, :, :filter_taps], axes, pairs))
    me = lax.axis_index("region")
    order = (me - jnp.arange(regions, dtype=jnp.int32)) % regions
    here = jnp.take(jnp.stack(same_seg), order, axis=0)
    ahead = jnp.take(jnp.stack(next_seg), order, axis=0)
    stations = regions * local_count
    here = here.reshape(stations, components + 1, seg_len)
    ahead = ahead.reshape(stations, components, filter_taps)
    region_of = here[:, components, 0].astype(jnp.int32)
    rows = jnp.concatenate([here[:, :components, :], ahead], axis=2)
    station_ids = jnp.arange(stations, dtype=jnp.int32)
    earlier = (region_of[None, :] == region_of[:, None]) & (station_ids[None, :] < station_ids[:, None])
    ranks = jnp.sum(earlier.astype(jnp.int32), axis=1)
    slot_index = jnp.arange(capacity, dtype=jnp.int32)
    placing = (region_of[None, :] == me) & (ranks[None, :] == slot_index[:, None])
    owned_rows = jnp.dot(
        placing.astype(jnp.bfloat16), rows.reshape(stations, -1), preferred_element_type=jnp.float32
    ).astype(jnp.bfloat16)
    owned_rows = owned_rows.reshape(capacity, components, seg_len + filter_taps)
    filled = jnp.sum(placing.astype(jnp.float32), axis=1)
    return owned_rows, filled


def per_device(records, templates, channel_mask, station_region):
    local_batches, kept, capacity, components, filter_taps = templates.shape
    seg_len = records.shape[2]
    owned_rows, filled = gather_owned(records, station_region, capacity, filter_taps)
    flat_owned = owned_rows.reshape(capacity * components, seg_len + filter_taps)
    weight = channel_mask.astype(jnp.float32) * filled[None, None, :, None]
    widened_templates = templates.astype(jnp.float32)
    template_norm = jnp.sqrt(
        jnp.sum(widened_templates * widened_templates, axis=4, keepdims=True) + 1e-06
    )
    normed = (widened_templates * weight[..., None] / template_norm).astype(jnp.bfloat16)
    normed = normed.reshape(local_batches * kept, capacity * components, filter_taps)
    total_len = seg_len * lax.axis_size("seg")
    stacked = ordered_sum(correlate(normed, flat_owned, seg_len), "region")
    power_sum = ordered_sum(jnp.sum(stacked * stacked, axis=1), "seg")
    detect = stacked / jnp.sqrt(power_sum / total_len + 1e-06)[:, None]
    return detect.reshape(local_batches, kept, seg_len)


def solution(mesh):
    placed = (
        P(("groups", "region"), None, "seg"),
        P(("groups", "tb"), None, "region", None, None),
        P(("groups", "tb"), None, "region", None),
        P(("groups", "region")),
    )
    return jax.shard_map(
        per_device,
        mesh=mesh,
        in_specs=placed,
        out_specs=P(("groups", "tb"), None, "seg"),
        check_vma=False,
    )
```

```python
import jax
import jax.numpy as jnp
from jax import lax
from jax.sharding import PartitionSpec as P
from jax.experimental import pallas as pl
from jax.experimental.pallas import tpu as pltpu


def hankel_kernel(x_ref, n_ref, o_ref, h_ref):
    width = h_ref.shape[0]
    channels = n_ref.shape[1] // width
    taps_blocks = width // 128
    out_blocks = o_ref.shape[1] // 128
    blocks = taps_blocks + out_blocks
    row = lax.broadcasted_iota(jnp.int32, (128, 128), 0)
    lane = lax.broadcasted_iota(jnp.int32, (128, 128), 1)
    low = lane >= row

    def one_channel(c, acc):
        rolled = [
            pltpu.roll(x_ref[pl.ds(c * blocks + m, 128, stride=0), :], 0, 1, stride=1, stride_axis=0)
            for m in range(blocks)
        ]
        squares = []
        for m in range(blocks - 1):
            window = jnp.where(low, rolled[m], rolled[m + 1])
            squares.append(jnp.sum(window * window, axis=0, keepdims=True))
            window = window.astype(jnp.bfloat16)
            for p in range(taps_blocks):
                a = m - p
                if 0 <= a < out_blocks:
                    h_ref[p * 128 : (p + 1) * 128, a * 128 : (a + 1) * 128] = window
        energy = jnp.concatenate(
            [sum(squares[a + p] for p in range(taps_blocks)) for a in range(out_blocks)], axis=1
        )
        start = pl.multiple_of(c * width, 128)
        part = jnp.dot(n_ref[:, pl.ds(start, width)], h_ref[...], preferred_element_type=jnp.float32)
        return acc + part * (1.0 / jnp.sqrt(jnp.maximum(energy, 1.0)))

    o_ref[...] = lax.fori_loop(0, channels, one_channel, jnp.zeros(o_ref.shape, jnp.float32))


def unflip(stacked):
    rows, seg_len = stacked.shape
    return stacked.reshape(rows, seg_len // 128, 128)[..., ::-1].reshape(rows, seg_len)


def correlate(normed, flat_owned, seg_len):
    rows, channels, filter_taps = normed.shape
    blocks = flat_owned.reshape(channels * (flat_owned.shape[1] // 128), 128)[:, ::-1]
    return pl.pallas_call(
        hankel_kernel,
        out_shape=jax.ShapeDtypeStruct((rows, seg_len), jnp.float32),
        scratch_shapes=[pltpu.VMEM((filter_taps, seg_len), jnp.bfloat16)],
    )(blocks.astype(jnp.float32), normed.reshape(rows, channels * filter_taps))


def ordered_sum(part, axis):
    size = lax.axis_size(axis)
    if size == 1:
        return part
    me = lax.axis_index(axis)
    received = [part] + [
        lax.ppermute(part, axis, [(i, (i + k) % size) for i in range(size)]) for k in range(1, size)
    ]
    stack = jnp.stack(received)
    order = (me - jnp.arange(size, dtype=jnp.int32)) % size
    return jnp.sum(jnp.take(stack, order, axis=0), axis=0)


def gather_owned(records, station_region, capacity, filter_taps):
    local_count, components, seg_len = records.shape
    regions = lax.axis_size("region")
    segs = lax.axis_size("seg")
    tag = jnp.broadcast_to(station_region.astype(jnp.bfloat16)[:, None, None], (local_count, 1, seg_len))
    payload = jnp.concatenate([records, tag], axis=1)
    axes = ("region", "seg")
    same_seg = [payload]
    for k in range(1, regions):
        pairs = [
            (r * segs + s, ((r + k) % regions) * segs + s) for r in range(regions) for s in range(segs)
        ]
        same_seg.append(lax.ppermute(payload, axes, pairs))
    next_seg = []
    for k in range(regions):
        pairs = [
            (r * segs + s + 1, ((r + k) % regions) * segs + s)
            for r in range(regions)
            for s in range(segs - 1)
        ]
        next_seg.append(lax.ppermute(records[:, :, :filter_taps], axes, pairs))
    me = lax.axis_index("region")
    order = (me - jnp.arange(regions, dtype=jnp.int32)) % regions
    here = jnp.take(jnp.stack(same_seg), order, axis=0)
    ahead = jnp.take(jnp.stack(next_seg), order, axis=0)
    stations = regions * local_count
    here = here.reshape(stations, components + 1, seg_len)
    ahead = ahead.reshape(stations, components, filter_taps)
    region_of = here[:, components, 0].astype(jnp.int32)
    rows = jnp.concatenate([here[:, :components, :], ahead], axis=2)
    station_ids = jnp.arange(stations, dtype=jnp.int32)
    earlier = (region_of[None, :] == region_of[:, None]) & (station_ids[None, :] < station_ids[:, None])
    ranks = jnp.sum(earlier.astype(jnp.int32), axis=1)
    slot_index = jnp.arange(capacity, dtype=jnp.int32)
    placing = (region_of[None, :] == me) & (ranks[None, :] == slot_index[:, None])
    owned_rows = jnp.dot(
        placing.astype(jnp.bfloat16), rows.reshape(stations, -1), preferred_element_type=jnp.float32
    ).astype(jnp.bfloat16)
    owned_rows = owned_rows.reshape(capacity, components, seg_len + filter_taps)
    filled = jnp.sum(placing.astype(jnp.float32), axis=1)
    return owned_rows, filled


def per_device(records, templates, channel_mask, station_region):
    local_batches, kept, capacity, components, filter_taps = templates.shape
    seg_len = records.shape[2]
    owned_rows, filled = gather_owned(records, station_region, capacity, filter_taps)
    flat_owned = owned_rows.reshape(capacity * components, seg_len + filter_taps)
    weight = channel_mask.astype(jnp.float32) * filled[None, None, :, None]
    widened_templates = templates.astype(jnp.float32)
    template_norm = jnp.sqrt(
        jnp.sum(widened_templates * widened_templates, axis=4, keepdims=True) + 1e-06
    )
    normed = (widened_templates * weight[..., None] / template_norm).astype(jnp.bfloat16)
    normed = normed.reshape(local_batches * kept, capacity * components, filter_taps)
    total_len = seg_len * lax.axis_size("seg")
    stacked = ordered_sum(correlate(normed, flat_owned, seg_len), "region")
    power_sum = ordered_sum(jnp.sum(stacked * stacked, axis=1), "seg")
    detect = unflip(stacked) / jnp.sqrt(power_sum / total_len + 1e-06)[:, None]
    return detect.reshape(local_batches, kept, seg_len)


def solution(mesh):
    placed = (
        P(("groups", "region"), None, "seg"),
        P(("groups", "tb"), None, "region", None, None),
        P(("groups", "tb"), None, "region", None),
        P(("groups", "region")),
    )
    return jax.shard_map(
        per_device,
        mesh=mesh,
        in_specs=placed,
        out_specs=P(("groups", "tb"), None, "seg"),
        check_vma=False,
    )
```

```python
import jax
import jax.numpy as jnp
from jax import lax
from jax.sharding import PartitionSpec as P
from jax.experimental import pallas as pl
from jax.experimental.pallas import tpu as pltpu


def hankel_kernel(x_ref, n_ref, o_ref, h_ref):
    width = h_ref.shape[0]
    channels = n_ref.shape[1] // width
    taps_blocks = width // 128
    out_blocks = o_ref.shape[1] // 128
    blocks = taps_blocks + out_blocks
    row = lax.broadcasted_iota(jnp.int32, (128, 128), 0)
    lane = lax.broadcasted_iota(jnp.int32, (128, 128), 1)
    low = lane >= row

    def one_channel(c, acc):
        rolled = [
            pltpu.roll(x_ref[pl.ds(c * blocks + m, 128, stride=0), :], 0, 1, stride=1, stride_axis=0)
            for m in range(blocks)
        ]
        squares = []
        for m in range(blocks - 1):
            window = jnp.where(low, rolled[m], rolled[m + 1])
            squares.append(jnp.sum(window * window, axis=0, keepdims=True))
            window = window.astype(jnp.bfloat16)
            for p in range(taps_blocks):
                a = m - p
                if 0 <= a < out_blocks:
                    h_ref[p * 128 : (p + 1) * 128, a * 128 : (a + 1) * 128] = window
        energy = jnp.concatenate(
            [sum(squares[a + p] for p in range(taps_blocks)) for a in range(out_blocks)], axis=1
        )
        start = pl.multiple_of(c * width, 128)
        part = jnp.dot(n_ref[:, pl.ds(start, width)], h_ref[...], preferred_element_type=jnp.float32)
        return acc + part * (1.0 / jnp.sqrt(jnp.maximum(energy, 1.0)))

    o_ref[...] = lax.fori_loop(0, channels, one_channel, jnp.zeros(o_ref.shape, jnp.float32))


def unflip(stacked):
    rows, seg_len = stacked.shape
    return stacked.reshape(rows, seg_len // 128, 128)[..., ::-1].reshape(rows, seg_len)


def correlate(normed, flat_owned, seg_len):
    rows, channels, filter_taps = normed.shape
    blocks = flat_owned.reshape(channels * (flat_owned.shape[1] // 128), 128)[:, ::-1]
    return pl.pallas_call(
        hankel_kernel,
        out_shape=jax.ShapeDtypeStruct((rows, seg_len), jnp.float32),
        scratch_shapes=[pltpu.VMEM((filter_taps, seg_len), jnp.bfloat16)],
    )(blocks.astype(jnp.float32), normed.reshape(rows, channels * filter_taps))


def ordered_sum(part, axis):
    size = lax.axis_size(axis)
    received = [part] + [
        lax.ppermute(part, axis, [(i, (i + k) % size) for i in range(size)]) for k in range(1, size)
    ]
    if size & (size - 1) == 0:
        while len(received) > 1:
            half = len(received) // 2
            received = [received[k] + received[k + half] for k in range(half)]
        return received[0]
    me = lax.axis_index(axis)
    order = (me - jnp.arange(size, dtype=jnp.int32)) % size
    return jnp.sum(jnp.take(jnp.stack(received), order, axis=0), axis=0)


def gather_owned(records, station_region, capacity, filter_taps):
    local_count, components, seg_len = records.shape
    regions = lax.axis_size("region")
    segs = lax.axis_size("seg")
    tag = jnp.broadcast_to(station_region.astype(jnp.bfloat16)[:, None, None], (local_count, 1, seg_len))
    payload = jnp.concatenate([records, tag], axis=1)
    axes = ("region", "seg")
    same_seg = [payload]
    for k in range(1, regions):
        pairs = [
            (r * segs + s, ((r + k) % regions) * segs + s) for r in range(regions) for s in range(segs)
        ]
        same_seg.append(lax.ppermute(payload, axes, pairs))
    next_seg = []
    for k in range(regions):
        pairs = [
            (r * segs + s + 1, ((r + k) % regions) * segs + s)
            for r in range(regions)
            for s in range(segs - 1)
        ]
        next_seg.append(lax.ppermute(records[:, :, :filter_taps], axes, pairs))
    me = lax.axis_index("region")
    stations = regions * local_count
    shift = jnp.arange(regions, dtype=jnp.int32)[:, None]
    local = jnp.arange(local_count, dtype=jnp.int32)[None, :]
    station_ids = (((me - shift) % regions) * local_count + local).reshape(stations)
    here = jnp.concatenate(same_seg, axis=0)
    ahead = jnp.concatenate(next_seg, axis=0)
    region_of = here[:, components, 0].astype(jnp.int32)
    rows = jnp.concatenate([here[:, :components, :], ahead], axis=2)
    earlier = (region_of[None, :] == region_of[:, None]) & (station_ids[None, :] < station_ids[:, None])
    ranks = jnp.sum(earlier.astype(jnp.int32), axis=1)
    slot_index = jnp.arange(capacity, dtype=jnp.int32)
    placing = (region_of[None, :] == me) & (ranks[None, :] == slot_index[:, None])
    owned_rows = jnp.dot(
        placing.astype(jnp.bfloat16), rows.reshape(stations, -1), preferred_element_type=jnp.float32
    ).astype(jnp.bfloat16)
    owned_rows = owned_rows.reshape(capacity, components, seg_len + filter_taps)
    filled = jnp.sum(placing.astype(jnp.float32), axis=1)
    return owned_rows, filled


def per_device(records, templates, channel_mask, station_region):
    local_batches, kept, capacity, components, filter_taps = templates.shape
    seg_len = records.shape[2]
    owned_rows, filled = gather_owned(records, station_region, capacity, filter_taps)
    flat_owned = owned_rows.reshape(capacity * components, seg_len + filter_taps)
    weight = channel_mask.astype(jnp.float32) * filled[None, None, :, None]
    widened_templates = templates.astype(jnp.float32)
    template_norm = jnp.sqrt(
        jnp.sum(widened_templates * widened_templates, axis=4, keepdims=True) + 1e-06
    )
    normed = (widened_templates * weight[..., None] / template_norm).astype(jnp.bfloat16)
    normed = normed.reshape(local_batches * kept, capacity * components, filter_taps)
    total_len = seg_len * lax.axis_size("seg")
    stacked = ordered_sum(correlate(normed, flat_owned, seg_len), "region")
    power_sum = ordered_sum(jnp.sum(stacked * stacked, axis=1), "seg")
    detect = unflip(stacked) / jnp.sqrt(power_sum / total_len + 1e-06)[:, None]
    return detect.reshape(local_batches, kept, seg_len)


def solution(mesh):
    placed = (
        P(("groups", "region"), None, "seg"),
        P(("groups", "tb"), None, "region", None, None),
        P(("groups", "tb"), None, "region", None),
        P(("groups", "region")),
    )
    return jax.shard_map(
        per_device,
        mesh=mesh,
        in_specs=placed,
        out_specs=P(("groups", "tb"), None, "seg"),
        check_vma=False,
    )
```

```python
import jax
import jax.numpy as jnp
from jax import lax
from jax.sharding import PartitionSpec as P
from jax.experimental import pallas as pl
from jax.experimental.pallas import tpu as pltpu


def hankel_kernel(x_ref, n_ref, fill_ref, o_ref, h_ref):
    width = h_ref.shape[0]
    channels = n_ref.shape[1] // width
    taps_blocks = width // 128
    out_blocks = o_ref.shape[1] // 128
    blocks = taps_blocks + out_blocks
    row = lax.broadcasted_iota(jnp.int32, (128, 128), 0)
    lane = lax.broadcasted_iota(jnp.int32, (128, 128), 1)
    low = lane >= row

    def one_channel(c, acc):
        rolled = [
            pltpu.roll(x_ref[pl.ds(c * blocks + m, 128, stride=0), :], 0, 1, stride=1, stride_axis=0)
            for m in range(blocks)
        ]
        squares = []
        for m in range(blocks - 1):
            window = jnp.where(low, rolled[m], rolled[m + 1])
            squares.append(jnp.sum(window * window, axis=0, keepdims=True))
            window = window.astype(jnp.bfloat16)
            for p in range(taps_blocks):
                a = m - p
                if 0 <= a < out_blocks:
                    h_ref[p * 128 : (p + 1) * 128, a * 128 : (a + 1) * 128] = window
        energy = jnp.concatenate(
            [sum(squares[a + p] for p in range(taps_blocks)) for a in range(out_blocks)], axis=1
        )
        start = pl.multiple_of(c * width, 128)
        part = jnp.dot(n_ref[:, pl.ds(start, width)], h_ref[...], preferred_element_type=jnp.float32)
        return acc + part * (fill_ref[c] / jnp.sqrt(jnp.maximum(energy, 1.0)))

    o_ref[...] = lax.fori_loop(0, channels, one_channel, jnp.zeros(o_ref.shape, jnp.float32))


def unflip(stacked):
    rows, seg_len = stacked.shape
    return stacked.reshape(rows, seg_len // 128, 128)[..., ::-1].reshape(rows, seg_len)


def correlate(normed, flat_owned, filled, seg_len):
    rows, channels, filter_taps = normed.shape
    blocks = flat_owned.reshape(channels * (flat_owned.shape[1] // 128), 128)[:, ::-1]
    return pl.pallas_call(
        hankel_kernel,
        out_shape=jax.ShapeDtypeStruct((rows, seg_len), jnp.float32),
        in_specs=[
            pl.BlockSpec(memory_space=pltpu.VMEM),
            pl.BlockSpec(memory_space=pltpu.VMEM),
            pl.BlockSpec(memory_space=pltpu.SMEM),
        ],
        scratch_shapes=[pltpu.VMEM((filter_taps, seg_len), jnp.bfloat16)],
    )(blocks.astype(jnp.float32), normed.reshape(rows, channels * filter_taps), filled)


def ordered_sum(part, axis):
    size = lax.axis_size(axis)
    received = [part] + [
        lax.ppermute(part, axis, [(i, (i + k) % size) for i in range(size)]) for k in range(1, size)
    ]
    if size & (size - 1) == 0:
        while len(received) > 1:
            half = len(received) // 2
            received = [received[k] + received[k + half] for k in range(half)]
        return received[0]
    me = lax.axis_index(axis)
    order = (me - jnp.arange(size, dtype=jnp.int32)) % size
    return jnp.sum(jnp.take(jnp.stack(received), order, axis=0), axis=0)


def gather_owned(records, station_region, capacity, filter_taps):
    local_count, components, seg_len = records.shape
    regions = lax.axis_size("region")
    segs = lax.axis_size("seg")
    tag = jnp.broadcast_to(station_region.astype(jnp.bfloat16)[:, None, None], (local_count, 1, seg_len))
    payload = jnp.concatenate([records, tag], axis=1)
    axes = ("region", "seg")
    same_seg = [payload]
    for k in range(1, regions):
        pairs = [
            (r * segs + s, ((r + k) % regions) * segs + s) for r in range(regions) for s in range(segs)
        ]
        same_seg.append(lax.ppermute(payload, axes, pairs))
    next_seg = []
    for k in range(regions):
        pairs = [
            (r * segs + s + 1, ((r + k) % regions) * segs + s)
            for r in range(regions)
            for s in range(segs - 1)
        ]
        next_seg.append(lax.ppermute(records[:, :, :filter_taps], axes, pairs))
    me = lax.axis_index("region")
    stations = regions * local_count
    shift = jnp.arange(regions, dtype=jnp.int32)[:, None]
    local = jnp.arange(local_count, dtype=jnp.int32)[None, :]
    station_ids = (((me - shift) % regions) * local_count + local).reshape(stations)
    here = jnp.concatenate(same_seg, axis=0)
    ahead = jnp.concatenate(next_seg, axis=0)
    region_of = here[:, components, 0].astype(jnp.int32)
    rows = jnp.concatenate([here[:, :components, :], ahead], axis=2)
    earlier = (region_of[None, :] == region_of[:, None]) & (station_ids[None, :] < station_ids[:, None])
    ranks = jnp.sum(earlier.astype(jnp.int32), axis=1)
    slot_index = jnp.arange(capacity, dtype=jnp.int32)
    placing = (region_of[None, :] == me) & (ranks[None, :] == slot_index[:, None])
    owned_rows = jnp.dot(
        placing.astype(jnp.bfloat16), rows.reshape(stations, -1), preferred_element_type=jnp.float32
    ).astype(jnp.bfloat16)
    owned_rows = owned_rows.reshape(capacity, components, seg_len + filter_taps)
    filled = jnp.sum(placing.astype(jnp.float32), axis=1)
    return owned_rows, filled


def per_device(records, templates, channel_mask, station_region):
    local_batches, kept, capacity, components, filter_taps = templates.shape
    seg_len = records.shape[2]
    owned_rows, filled = gather_owned(records, station_region, capacity, filter_taps)
    flat_owned = owned_rows.reshape(capacity * components, seg_len + filter_taps)
    weight = channel_mask.astype(jnp.float32)
    widened_templates = templates.astype(jnp.float32)
    template_norm = jnp.sqrt(
        jnp.sum(widened_templates * widened_templates, axis=4, keepdims=True) + 1e-06
    )
    normed = (widened_templates * weight[..., None] / template_norm).astype(jnp.bfloat16)
    normed = normed.reshape(local_batches * kept, capacity * components, filter_taps)
    total_len = seg_len * lax.axis_size("seg")
    filled_channels = jnp.repeat(filled, components)
    stacked = ordered_sum(correlate(normed, flat_owned, filled_channels, seg_len), "region")
    power_sum = ordered_sum(jnp.sum(stacked * stacked, axis=1), "seg")
    detect = unflip(stacked) / jnp.sqrt(power_sum / total_len + 1e-06)[:, None]
    return detect.reshape(local_batches, kept, seg_len)


def solution(mesh):
    placed = (
        P(("groups", "region"), None, "seg"),
        P(("groups", "tb"), None, "region", None, None),
        P(("groups", "tb"), None, "region", None),
        P(("groups", "region")),
    )
    return jax.shard_map(
        per_device,
        mesh=mesh,
        in_specs=placed,
        out_specs=P(("groups", "tb"), None, "seg"),
        check_vma=False,
    )
```

```python
import jax
import jax.numpy as jnp
from jax import lax
from jax.sharding import PartitionSpec as P
from jax.experimental import pallas as pl
from jax.experimental.pallas import tpu as pltpu


def hankel_kernel(x_ref, n_ref, fill_ref, o_ref, h_ref):
    width = h_ref.shape[0]
    channels = n_ref.shape[1] // width
    taps_blocks = width // 128
    out_blocks = o_ref.shape[1] // 128
    blocks = taps_blocks + out_blocks
    row = lax.broadcasted_iota(jnp.int32, (128, 128), 0)
    lane = lax.broadcasted_iota(jnp.int32, (128, 128), 1)
    low = lane >= row

    def one_channel(c, acc):
        rolled = [
            pltpu.roll(x_ref[pl.ds(c * blocks + m, 128, stride=0), :], 0, 1, stride=1, stride_axis=0)
            for m in range(blocks)
        ]
        squares = []
        for m in range(blocks - 1):
            window = jnp.where(low, rolled[m], rolled[m + 1])
            squares.append(jnp.sum(window * window, axis=0, keepdims=True))
            window = window.astype(jnp.bfloat16)
            for p in range(taps_blocks):
                a = m - p
                if 0 <= a < out_blocks:
                    h_ref[p * 128 : (p + 1) * 128, a * 128 : (a + 1) * 128] = window
        energy = jnp.concatenate(
            [sum(squares[a + p] for p in range(taps_blocks)) for a in range(out_blocks)], axis=1
        )
        start = pl.multiple_of(c * width, 128)
        part = jnp.dot(n_ref[:, pl.ds(start, width)], h_ref[...], preferred_element_type=jnp.float32)
        return acc + part * (fill_ref[c] / jnp.sqrt(jnp.maximum(energy, 1.0)))

    o_ref[...] = lax.fori_loop(0, channels, one_channel, jnp.zeros(o_ref.shape, jnp.float32))


def unflip(stacked):
    rows, seg_len = stacked.shape
    return stacked.reshape(rows, seg_len // 128, 128)[..., ::-1].reshape(rows, seg_len)


def correlate(normed, flat_owned, filled, seg_len):
    rows, channels, filter_taps = normed.shape
    blocks = flat_owned.reshape(channels * (flat_owned.shape[1] // 128), 128)[:, ::-1]
    return pl.pallas_call(
        hankel_kernel,
        out_shape=jax.ShapeDtypeStruct((rows, seg_len), jnp.float32),
        in_specs=[
            pl.BlockSpec(memory_space=pltpu.VMEM),
            pl.BlockSpec(memory_space=pltpu.VMEM),
            pl.BlockSpec(memory_space=pltpu.SMEM),
        ],
        scratch_shapes=[pltpu.VMEM((filter_taps, seg_len), jnp.bfloat16)],
    )(blocks.astype(jnp.float32), normed.reshape(rows, channels * filter_taps), filled)


def ordered_sum(part, axis):
    size = lax.axis_size(axis)
    received = [part] + [
        lax.ppermute(part, axis, [(i, (i + k) % size) for i in range(size)]) for k in range(1, size)
    ]
    if size & (size - 1) == 0:
        while len(received) > 1:
            half = len(received) // 2
            received = [received[k] + received[k + half] for k in range(half)]
        return received[0]
    me = lax.axis_index(axis)
    order = (me - jnp.arange(size, dtype=jnp.int32)) % size
    return jnp.sum(jnp.take(jnp.stack(received), order, axis=0), axis=0)


def gather_owned(records, station_region, capacity, filter_taps):
    local_count, components, seg_len = records.shape
    regions = lax.axis_size("region")
    segs = lax.axis_size("seg")
    ahead = lax.ppermute(
        records[:, :, :filter_taps], "seg", [(s + 1, s) for s in range(segs - 1)]
    )
    tag = jnp.broadcast_to(station_region.astype(jnp.bfloat16)[:, None, None], (local_count, 1, seg_len + filter_taps))
    payload = jnp.concatenate(
        [jnp.concatenate([records, ahead], axis=2), tag], axis=1
    )
    gathered = [payload] + [
        lax.ppermute(payload, "region", [(r, (r + k) % regions) for r in range(regions)])
        for k in range(1, regions)
    ]
    me = lax.axis_index("region")
    stations = regions * local_count
    shift = jnp.arange(regions, dtype=jnp.int32)[:, None]
    local = jnp.arange(local_count, dtype=jnp.int32)[None, :]
    station_ids = (((me - shift) % regions) * local_count + local).reshape(stations)
    here = jnp.concatenate(gathered, axis=0)
    region_of = here[:, components, 0].astype(jnp.int32)
    rows = here[:, :components, :]
    earlier = (region_of[None, :] == region_of[:, None]) & (station_ids[None, :] < station_ids[:, None])
    ranks = jnp.sum(earlier.astype(jnp.int32), axis=1)
    slot_index = jnp.arange(capacity, dtype=jnp.int32)
    placing = (region_of[None, :] == me) & (ranks[None, :] == slot_index[:, None])
    owned_rows = jnp.dot(
        placing.astype(jnp.bfloat16), rows.reshape(stations, -1), preferred_element_type=jnp.float32
    ).astype(jnp.bfloat16)
    owned_rows = owned_rows.reshape(capacity, components, seg_len + filter_taps)
    filled = jnp.sum(placing.astype(jnp.float32), axis=1)
    return owned_rows, filled


def per_device(records, templates, channel_mask, station_region):
    local_batches, kept, capacity, components, filter_taps = templates.shape
    seg_len = records.shape[2]
    owned_rows, filled = gather_owned(records, station_region, capacity, filter_taps)
    flat_owned = owned_rows.reshape(capacity * components, seg_len + filter_taps)
    weight = channel_mask.astype(jnp.float32)
    widened_templates = templates.astype(jnp.float32)
    template_norm = jnp.sqrt(
        jnp.sum(widened_templates * widened_templates, axis=4, keepdims=True) + 1e-06
    )
    normed = (widened_templates * weight[..., None] / template_norm).astype(jnp.bfloat16)
    normed = normed.reshape(local_batches * kept, capacity * components, filter_taps)
    total_len = seg_len * lax.axis_size("seg")
    filled_channels = jnp.repeat(filled, components)
    stacked = ordered_sum(correlate(normed, flat_owned, filled_channels, seg_len), "region")
    power_sum = ordered_sum(jnp.sum(stacked * stacked, axis=1), "seg")
    detect = unflip(stacked) / jnp.sqrt(power_sum / total_len + 1e-06)[:, None]
    return detect.reshape(local_batches, kept, seg_len)


def solution(mesh):
    placed = (
        P(("groups", "region"), None, "seg"),
        P(("groups", "tb"), None, "region", None, None),
        P(("groups", "tb"), None, "region", None),
        P(("groups", "region")),
    )
    return jax.shard_map(
        per_device,
        mesh=mesh,
        in_specs=placed,
        out_specs=P(("groups", "tb"), None, "seg"),
        check_vma=False,
    )
```

```python
import jax
import jax.numpy as jnp
from jax import lax
from jax.sharding import PartitionSpec as P
from jax.experimental import pallas as pl
from jax.experimental.pallas import tpu as pltpu


def hankel_kernel(x_ref, n_ref, o_ref, h_ref):
    width = h_ref.shape[0]
    channels = n_ref.shape[1] // width
    taps_blocks = width // 128
    out_blocks = o_ref.shape[1] // 128
    blocks = taps_blocks + out_blocks
    row = lax.broadcasted_iota(jnp.int32, (128, 128), 0)
    lane = lax.broadcasted_iota(jnp.int32, (128, 128), 1)
    low = lane >= row

    def one_channel(c, acc):
        rolled = [
            pltpu.roll(x_ref[pl.ds(c * blocks + m, 128, stride=0), :], 0, 1, stride=1, stride_axis=0)
            for m in range(blocks)
        ]
        squares = []
        for m in range(blocks - 1):
            window = jnp.where(low, rolled[m], rolled[m + 1])
            squares.append(jnp.sum(window * window, axis=0, keepdims=True))
            window = window.astype(jnp.bfloat16)
            for p in range(taps_blocks):
                a = m - p
                if 0 <= a < out_blocks:
                    h_ref[p * 128 : (p + 1) * 128, a * 128 : (a + 1) * 128] = window
        energy = jnp.concatenate(
            [sum(squares[a + p] for p in range(taps_blocks)) for a in range(out_blocks)], axis=1
        )
        start = pl.multiple_of(c * width, 128)
        part = jnp.dot(n_ref[:, pl.ds(start, width)], h_ref[...], preferred_element_type=jnp.float32)
        return acc + part * (1.0 / jnp.sqrt(jnp.maximum(energy, 1.0)))

    o_ref[...] = lax.fori_loop(0, channels, one_channel, jnp.zeros(o_ref.shape, jnp.float32))


def unflip(stacked):
    rows, seg_len = stacked.shape
    return stacked.reshape(rows, seg_len // 128, 128)[..., ::-1].reshape(rows, seg_len)


def correlate(normed, flat_owned, seg_len):
    rows, channels, filter_taps = normed.shape
    blocks = flat_owned.reshape(channels * (flat_owned.shape[1] // 128), 128)[:, ::-1]
    return pl.pallas_call(
        hankel_kernel,
        out_shape=jax.ShapeDtypeStruct((rows, seg_len), jnp.float32),
        scratch_shapes=[pltpu.VMEM((filter_taps, seg_len), jnp.bfloat16)],
    )(blocks, normed.reshape(rows, channels * filter_taps))


def ordered_sum(part, axis):
    size = lax.axis_size(axis)
    received = [part] + [
        lax.ppermute(part, axis, [(i, (i + k) % size) for i in range(size)]) for k in range(1, size)
    ]
    if size & (size - 1) == 0:
        while len(received) > 1:
            half = len(received) // 2
            received = [received[k] + received[k + half] for k in range(half)]
        return received[0]
    me = lax.axis_index(axis)
    order = (me - jnp.arange(size, dtype=jnp.int32)) % size
    return jnp.sum(jnp.take(jnp.stack(received), order, axis=0), axis=0)


def gather_owned(records, station_region, capacity, filter_taps):
    local_count, components, seg_len = records.shape
    regions = lax.axis_size("region")
    segs = lax.axis_size("seg")
    ahead = lax.ppermute(
        records[:, :, :filter_taps], "seg", [(s + 1, s) for s in range(segs - 1)]
    )
    tag = jnp.broadcast_to(station_region.astype(jnp.bfloat16)[:, None, None], (local_count, 1, seg_len + filter_taps))
    payload = jnp.concatenate(
        [jnp.concatenate([records, ahead], axis=2), tag], axis=1
    )
    gathered = [payload] + [
        lax.ppermute(payload, "region", [(r, (r + k) % regions) for r in range(regions)])
        for k in range(1, regions)
    ]
    me = lax.axis_index("region")
    stations = regions * local_count
    shift = jnp.arange(regions, dtype=jnp.int32)[:, None]
    local = jnp.arange(local_count, dtype=jnp.int32)[None, :]
    station_ids = (((me - shift) % regions) * local_count + local).reshape(stations)
    here = jnp.concatenate(gathered, axis=0)
    region_of = here[:, components, 0].astype(jnp.int32)
    rows = here[:, :components, :]
    earlier = (region_of[None, :] == region_of[:, None]) & (station_ids[None, :] < station_ids[:, None])
    ranks = jnp.sum(earlier.astype(jnp.int32), axis=1)
    slot_index = jnp.arange(capacity, dtype=jnp.int32)
    placing = (region_of[None, :] == me) & (ranks[None, :] == slot_index[:, None])
    owned_rows = jnp.dot(
        placing.astype(jnp.bfloat16), rows.reshape(stations, -1), preferred_element_type=jnp.float32
    ).astype(jnp.bfloat16)
    owned_rows = owned_rows.reshape(capacity, components, seg_len + filter_taps)
    filled = jnp.sum(placing.astype(jnp.float32), axis=1)
    return owned_rows, filled


def per_device(records, templates, channel_mask, station_region):
    local_batches, kept, capacity, components, filter_taps = templates.shape
    seg_len = records.shape[2]
    owned_rows, filled = gather_owned(records, station_region, capacity, filter_taps)
    owned_rows = owned_rows.astype(jnp.float32) * filled[:, None, None]
    flat_owned = owned_rows.reshape(capacity * components, seg_len + filter_taps)
    weight = channel_mask.astype(jnp.float32)
    widened_templates = templates.astype(jnp.float32)
    template_norm = jnp.sqrt(
        jnp.sum(widened_templates * widened_templates, axis=4, keepdims=True) + 1e-06
    )
    normed = (widened_templates * weight[..., None] / template_norm).astype(jnp.bfloat16)
    normed = normed.reshape(local_batches * kept, capacity * components, filter_taps)
    total_len = seg_len * lax.axis_size("seg")
    stacked, power_sum = region_sum(correlate(normed, flat_owned, seg_len))
    power_sum = ordered_sum(power_sum, "seg")
    detect = unflip(stacked) / jnp.sqrt(power_sum / total_len + 1e-06)[:, None]
    return detect.reshape(local_batches, kept, seg_len)


def region_sum(part):
    regions = lax.axis_size("region")
    rows, width = part.shape
    chunk = width // regions
    me = lax.axis_index("region")
    chunks = part.reshape(rows, regions, chunk)

    def shifted(value, k):
        return lax.ppermute(value, "region", [(r, (r + k) % regions) for r in range(regions)])

    own = jnp.take(chunks, me, axis=1)
    for k in range(1, regions):
        own = own + shifted(jnp.take(chunks, (me + k) % regions, axis=1), k)
    power = jnp.sum(own * own, axis=1)
    power_rows = -(-rows // chunk)
    packed = jnp.pad(power, (0, power_rows * chunk - rows)).reshape(power_rows, chunk)
    bundle = jnp.concatenate([own, packed], axis=0)
    received = [bundle] + [shifted(bundle, k) for k in range(1, regions)]
    powers = [b[rows:].reshape(-1)[:rows] for b in received]
    while len(powers) > 1:
        half = len(powers) // 2
        powers = [powers[k] + powers[k + half] for k in range(half)]
    order = (me - jnp.arange(regions, dtype=jnp.int32)) % regions
    pieces = jnp.stack([b[:rows] for b in received], axis=1)
    full = jnp.take(pieces, order, axis=1).reshape(rows, width)
    return full, powers[0]


def solution(mesh):
    placed = (
        P(("groups", "region"), None, "seg"),
        P(("groups", "tb"), None, "region", None, None),
        P(("groups", "tb"), None, "region", None),
        P(("groups", "region")),
    )
    return jax.shard_map(
        per_device,
        mesh=mesh,
        in_specs=placed,
        out_specs=P(("groups", "tb"), None, "seg"),
        check_vma=False,
    )
```

```python
import jax
import jax.numpy as jnp
from jax import lax
from jax.sharding import PartitionSpec as P
from jax.experimental import pallas as pl
from jax.experimental.pallas import tpu as pltpu


def hankel_kernel(x_ref, n_ref, o_ref, h_ref):
    width = h_ref.shape[0]
    channels = n_ref.shape[1] // width
    taps_blocks = width // 128
    out_blocks = o_ref.shape[1] // 128
    blocks = taps_blocks + out_blocks
    row = lax.broadcasted_iota(jnp.int32, (128, 128), 0)
    lane = lax.broadcasted_iota(jnp.int32, (128, 128), 1)
    low = lane >= row

    def one_channel(c, acc):
        rolled = [
            pltpu.roll(x_ref[pl.ds(c * blocks + m, 128, stride=0), :], 0, 1, stride=1, stride_axis=0)
            for m in range(blocks)
        ]
        squares = []
        for m in range(blocks - 1):
            window = jnp.where(low, rolled[m], rolled[m + 1])
            squares.append(jnp.sum(window * window, axis=0, keepdims=True))
            window = window.astype(jnp.bfloat16)
            for p in range(taps_blocks):
                a = m - p
                if 0 <= a < out_blocks:
                    h_ref[p * 128 : (p + 1) * 128, a * 128 : (a + 1) * 128] = window
        energy = jnp.concatenate(
            [sum(squares[a + p] for p in range(taps_blocks)) for a in range(out_blocks)], axis=1
        )
        start = pl.multiple_of(c * width, 128)
        part = jnp.dot(n_ref[:, pl.ds(start, width)], h_ref[...], preferred_element_type=jnp.float32)
        return acc + part * (1.0 / jnp.sqrt(jnp.maximum(energy, 1.0)))

    o_ref[...] = lax.fori_loop(0, channels, one_channel, jnp.zeros(o_ref.shape, jnp.float32))


def unflip(stacked):
    rows, seg_len = stacked.shape
    return stacked.reshape(rows, seg_len // 128, 128)[..., ::-1].reshape(rows, seg_len)


def correlate(normed, flat_owned, seg_len):
    rows, channels, filter_taps = normed.shape
    blocks = flat_owned.reshape(channels * (flat_owned.shape[1] // 128), 128)[:, ::-1]
    return pl.pallas_call(
        hankel_kernel,
        out_shape=jax.ShapeDtypeStruct((rows, seg_len), jnp.float32),
        scratch_shapes=[pltpu.VMEM((filter_taps, seg_len), jnp.bfloat16)],
    )(blocks, normed.reshape(rows, channels * filter_taps))


def ordered_sum(part, axis):
    size = lax.axis_size(axis)
    if size & (size - 1) == 0:
        step = 1
        while step < size:
            part = part + lax.ppermute(part, axis, [(i, i ^ step) for i in range(size)])
            step *= 2
        return part
    me = lax.axis_index(axis)
    received = [part] + [
        lax.ppermute(part, axis, [(i, (i + k) % size) for i in range(size)]) for k in range(1, size)
    ]
    order = (me - jnp.arange(size, dtype=jnp.int32)) % size
    return jnp.sum(jnp.take(jnp.stack(received), order, axis=0), axis=0)


def gather_owned(records, station_region, capacity, filter_taps):
    local_count, components, seg_len = records.shape
    regions = lax.axis_size("region")
    segs = lax.axis_size("seg")
    ahead = lax.ppermute(
        records[:, :, :filter_taps], "seg", [(s + 1, s) for s in range(segs - 1)]
    )
    tag = jnp.broadcast_to(station_region.astype(jnp.bfloat16)[:, None, None], (local_count, 1, seg_len + filter_taps))
    payload = jnp.concatenate(
        [jnp.concatenate([records, ahead], axis=2), tag], axis=1
    )
    gathered = [payload] + [
        lax.ppermute(payload, "region", [(r, (r + k) % regions) for r in range(regions)])
        for k in range(1, regions)
    ]
    me = lax.axis_index("region")
    stations = regions * local_count
    shift = jnp.arange(regions, dtype=jnp.int32)[:, None]
    local = jnp.arange(local_count, dtype=jnp.int32)[None, :]
    station_ids = (((me - shift) % regions) * local_count + local).reshape(stations)
    here = jnp.concatenate(gathered, axis=0)
    region_of = here[:, components, 0].astype(jnp.int32)
    rows = here[:, :components, :]
    earlier = (region_of[None, :] == region_of[:, None]) & (station_ids[None, :] < station_ids[:, None])
    ranks = jnp.sum(earlier.astype(jnp.int32), axis=1)
    slot_index = jnp.arange(capacity, dtype=jnp.int32)
    placing = (region_of[None, :] == me) & (ranks[None, :] == slot_index[:, None])
    owned_rows = jnp.dot(
        placing.astype(jnp.bfloat16), rows.reshape(stations, -1), preferred_element_type=jnp.float32
    ).astype(jnp.bfloat16)
    owned_rows = owned_rows.reshape(capacity, components, seg_len + filter_taps)
    filled = jnp.sum(placing.astype(jnp.float32), axis=1)
    return owned_rows, filled


def per_device(records, templates, channel_mask, station_region):
    local_batches, kept, capacity, components, filter_taps = templates.shape
    seg_len = records.shape[2]
    owned_rows, filled = gather_owned(records, station_region, capacity, filter_taps)
    owned_rows = owned_rows.astype(jnp.float32) * filled[:, None, None]
    flat_owned = owned_rows.reshape(capacity * components, seg_len + filter_taps)
    weight = channel_mask.astype(jnp.float32)
    widened_templates = templates.astype(jnp.float32)
    template_norm = jnp.sqrt(
        jnp.sum(widened_templates * widened_templates, axis=4, keepdims=True) + 1e-06
    )
    normed = (widened_templates * weight[..., None] / template_norm).astype(jnp.bfloat16)
    normed = normed.reshape(local_batches * kept, capacity * components, filter_taps)
    total_len = seg_len * lax.axis_size("seg")
    stacked = ordered_sum(correlate(normed, flat_owned, seg_len), "region")
    power_sum = ordered_sum(jnp.sum(stacked * stacked, axis=1), "seg")
    detect = unflip(stacked) / jnp.sqrt(power_sum / total_len + 1e-06)[:, None]
    return detect.reshape(local_batches, kept, seg_len)


def solution(mesh):
    placed = (
        P(("groups", "region"), None, "seg"),
        P(("groups", "tb"), None, "region", None, None),
        P(("groups", "tb"), None, "region", None),
        P(("groups", "region")),
    )
    return jax.shard_map(
        per_device,
        mesh=mesh,
        in_specs=placed,
        out_specs=P(("groups", "tb"), None, "seg"),
        check_vma=False,
    )
```

```python
import jax
import jax.numpy as jnp
from jax import lax
from jax.sharding import PartitionSpec as P
from jax.experimental import pallas as pl
from jax.experimental.pallas import tpu as pltpu


def hankel_kernel(x_ref, n_ref, o_ref, h_ref):
    width = h_ref.shape[0]
    channels = n_ref.shape[1] // width
    taps_blocks = width // 128
    out_blocks = o_ref.shape[1] // 128
    blocks = taps_blocks + out_blocks
    row = lax.broadcasted_iota(jnp.int32, (128, 128), 0)
    lane = lax.broadcasted_iota(jnp.int32, (128, 128), 1)
    low = lane >= row

    def one_channel(c, acc):
        rolled = [
            pltpu.roll(x_ref[pl.ds(c * blocks + m, 128, stride=0), :], 0, 1, stride=1, stride_axis=0)
            for m in range(blocks)
        ]
        squares = []
        for m in range(blocks - 1):
            window = jnp.where(low, rolled[m], rolled[m + 1])
            squares.append(jnp.sum(window * window, axis=0, keepdims=True))
            window = window.astype(jnp.bfloat16)
            for p in range(taps_blocks):
                a = m - p
                if 0 <= a < out_blocks:
                    h_ref[p * 128 : (p + 1) * 128, a * 128 : (a + 1) * 128] = window
        energy = jnp.concatenate(
            [sum(squares[a + p] for p in range(taps_blocks)) for a in range(out_blocks)], axis=1
        )
        start = pl.multiple_of(c * width, 128)
        part = jnp.dot(n_ref[:, pl.ds(start, width)], h_ref[...], preferred_element_type=jnp.float32)
        return acc + part * (1.0 / jnp.sqrt(jnp.maximum(energy, 1.0)))

    o_ref[...] = lax.fori_loop(0, channels, one_channel, jnp.zeros(o_ref.shape, jnp.float32))


def unflip(stacked):
    rows, seg_len = stacked.shape
    return stacked.reshape(rows, seg_len // 128, 128)[..., ::-1].reshape(rows, seg_len)


def correlate(normed, flat_owned, seg_len):
    rows, channels, filter_taps = normed.shape
    blocks = flat_owned.reshape(channels * (flat_owned.shape[1] // 128), 128)[:, ::-1]
    return pl.pallas_call(
        hankel_kernel,
        out_shape=jax.ShapeDtypeStruct((rows, seg_len), jnp.float32),
        scratch_shapes=[pltpu.VMEM((filter_taps, seg_len), jnp.bfloat16)],
    )(blocks, normed.reshape(rows, channels * filter_taps))


def ordered_sum(part, axis):
    size = lax.axis_size(axis)
    if size & (size - 1) == 0:
        step = 1
        while step < size:
            part = part + lax.ppermute(part, axis, [(i, i ^ step) for i in range(size)])
            step *= 2
        return part
    me = lax.axis_index(axis)
    received = [part] + [
        lax.ppermute(part, axis, [(i, (i + k) % size) for i in range(size)]) for k in range(1, size)
    ]
    order = (me - jnp.arange(size, dtype=jnp.int32)) % size
    return jnp.sum(jnp.take(jnp.stack(received), order, axis=0), axis=0)


def gather_owned(records, station_region, capacity, filter_taps):
    local_count, components, seg_len = records.shape
    regions = lax.axis_size("region")
    segs = lax.axis_size("seg")
    ahead = lax.ppermute(
        records[:, :, :filter_taps], "seg", [(s + 1, s) for s in range(segs - 1)]
    )
    tag = jnp.broadcast_to(station_region.astype(jnp.bfloat16)[:, None, None], (local_count, 1, seg_len + filter_taps))
    payload = jnp.concatenate(
        [jnp.concatenate([records, ahead], axis=2), tag], axis=1
    )
    me = lax.axis_index("region")
    stations = regions * local_count
    if regions & (regions - 1) == 0:
        here = payload
        step = 1
        while step < regions:
            theirs = lax.ppermute(here, "region", [(r, r ^ step) for r in range(regions)])
            here = jnp.concatenate([here, theirs], axis=0)
            step *= 2
        source = me ^ jnp.arange(regions, dtype=jnp.int32)[:, None]
    else:
        gathered = [payload] + [
            lax.ppermute(payload, "region", [(r, (r + k) % regions) for r in range(regions)])
            for k in range(1, regions)
        ]
        here = jnp.concatenate(gathered, axis=0)
        source = (me - jnp.arange(regions, dtype=jnp.int32)[:, None]) % regions
    local = jnp.arange(local_count, dtype=jnp.int32)[None, :]
    station_ids = (source * local_count + local).reshape(stations)
    region_of = here[:, components, 0].astype(jnp.int32)
    rows = here[:, :components, :]
    earlier = (region_of[None, :] == region_of[:, None]) & (station_ids[None, :] < station_ids[:, None])
    ranks = jnp.sum(earlier.astype(jnp.int32), axis=1)
    slot_index = jnp.arange(capacity, dtype=jnp.int32)
    placing = (region_of[None, :] == me) & (ranks[None, :] == slot_index[:, None])
    owned_rows = jnp.dot(
        placing.astype(jnp.bfloat16), rows.reshape(stations, -1), preferred_element_type=jnp.float32
    ).astype(jnp.bfloat16)
    owned_rows = owned_rows.reshape(capacity, components, seg_len + filter_taps)
    filled = jnp.sum(placing.astype(jnp.float32), axis=1)
    return owned_rows, filled


def per_device(records, templates, channel_mask, station_region):
    local_batches, kept, capacity, components, filter_taps = templates.shape
    seg_len = records.shape[2]
    owned_rows, filled = gather_owned(records, station_region, capacity, filter_taps)
    owned_rows = owned_rows.astype(jnp.float32) * filled[:, None, None]
    flat_owned = owned_rows.reshape(capacity * components, seg_len + filter_taps)
    weight = channel_mask.astype(jnp.float32)
    widened_templates = templates.astype(jnp.float32)
    template_norm = jnp.sqrt(
        jnp.sum(widened_templates * widened_templates, axis=4, keepdims=True) + 1e-06
    )
    normed = (widened_templates * weight[..., None] / template_norm).astype(jnp.bfloat16)
    normed = normed.reshape(local_batches * kept, capacity * components, filter_taps)
    total_len = seg_len * lax.axis_size("seg")
    stacked = ordered_sum(correlate(normed, flat_owned, seg_len), "region")
    power_sum = ordered_sum(jnp.sum(stacked * stacked, axis=1), "seg")
    detect = unflip(stacked) / jnp.sqrt(power_sum / total_len + 1e-06)[:, None]
    return detect.reshape(local_batches, kept, seg_len)


def solution(mesh):
    placed = (
        P(("groups", "region"), None, "seg"),
        P(("groups", "tb"), None, "region", None, None),
        P(("groups", "tb"), None, "region", None),
        P(("groups", "region")),
    )
    return jax.shard_map(
        per_device,
        mesh=mesh,
        in_specs=placed,
        out_specs=P(("groups", "tb"), None, "seg"),
        check_vma=False,
    )
```

```python
import jax
import jax.numpy as jnp
from jax import lax
from jax.sharding import PartitionSpec as P
from jax.experimental import pallas as pl
from jax.experimental.pallas import tpu as pltpu


def hankel_kernel(x_ref, t_ref, m_ref, o_ref, h_ref):
    width = h_ref.shape[0]
    channels = t_ref.shape[1] // width
    taps_blocks = width // 128
    out_blocks = o_ref.shape[1] // 128
    blocks = taps_blocks + out_blocks
    row = lax.broadcasted_iota(jnp.int32, (128, 128), 0)
    lane = lax.broadcasted_iota(jnp.int32, (128, 128), 1)
    low = lane >= row

    def one_channel(c, acc):
        start = pl.multiple_of(c * width, 128)
        widened = t_ref[:, pl.ds(start, width)].astype(jnp.float32)
        norm = jnp.sqrt(jnp.sum(widened * widened, axis=1, keepdims=True) + 1e-06)
        normed = (widened * m_ref[c] / norm).astype(jnp.bfloat16)
        rolled = [
            pltpu.roll(x_ref[pl.ds(c * blocks + m, 128, stride=0), :], 0, 1, stride=1, stride_axis=0)
            for m in range(blocks)
        ]
        squares = []
        for m in range(blocks - 1):
            window = jnp.where(low, rolled[m], rolled[m + 1])
            squares.append(jnp.sum(window * window, axis=0, keepdims=True))
            window = window.astype(jnp.bfloat16)
            for p in range(taps_blocks):
                a = m - p
                if 0 <= a < out_blocks:
                    h_ref[p * 128 : (p + 1) * 128, a * 128 : (a + 1) * 128] = window
        energy = jnp.concatenate(
            [sum(squares[a + p] for p in range(taps_blocks)) for a in range(out_blocks)], axis=1
        )
        part = jnp.dot(normed, h_ref[...], preferred_element_type=jnp.float32)
        return acc + part * (1.0 / jnp.sqrt(jnp.maximum(energy, 1.0)))

    o_ref[...] = lax.fori_loop(0, channels, one_channel, jnp.zeros(o_ref.shape, jnp.float32))


def unflip(stacked):
    rows, seg_len = stacked.shape
    return stacked.reshape(rows, seg_len // 128, 128)[..., ::-1].reshape(rows, seg_len)


def correlate(templates, mask, flat_owned, seg_len):
    rows, channels, filter_taps = templates.shape
    blocks = flat_owned.reshape(channels * (flat_owned.shape[1] // 128), 128)[:, ::-1]
    return pl.pallas_call(
        hankel_kernel,
        out_shape=jax.ShapeDtypeStruct((rows, seg_len), jnp.float32),
        scratch_shapes=[pltpu.VMEM((filter_taps, seg_len), jnp.bfloat16)],
    )(blocks, templates.reshape(rows, channels * filter_taps), jnp.transpose(mask)[:, :, None])


def ordered_sum(part, axis):
    size = lax.axis_size(axis)
    if size & (size - 1) == 0:
        step = 1
        while step < size:
            part = part + lax.ppermute(part, axis, [(i, i ^ step) for i in range(size)])
            step *= 2
        return part
    me = lax.axis_index(axis)
    received = [part] + [
        lax.ppermute(part, axis, [(i, (i + k) % size) for i in range(size)]) for k in range(1, size)
    ]
    order = (me - jnp.arange(size, dtype=jnp.int32)) % size
    return jnp.sum(jnp.take(jnp.stack(received), order, axis=0), axis=0)


def gather_owned(records, station_region, capacity, filter_taps):
    local_count, components, seg_len = records.shape
    regions = lax.axis_size("region")
    segs = lax.axis_size("seg")
    ahead = lax.ppermute(
        records[:, :, :filter_taps], "seg", [(s + 1, s) for s in range(segs - 1)]
    )
    tag = jnp.broadcast_to(station_region.astype(jnp.bfloat16)[:, None, None], (local_count, 1, seg_len + filter_taps))
    payload = jnp.concatenate(
        [jnp.concatenate([records, ahead], axis=2), tag], axis=1
    )
    me = lax.axis_index("region")
    stations = regions * local_count
    if regions & (regions - 1) == 0:
        here = payload
        step = 1
        while step < regions:
            theirs = lax.ppermute(here, "region", [(r, r ^ step) for r in range(regions)])
            here = jnp.concatenate([here, theirs], axis=0)
            step *= 2
        source = me ^ jnp.arange(regions, dtype=jnp.int32)[:, None]
    else:
        gathered = [payload] + [
            lax.ppermute(payload, "region", [(r, (r + k) % regions) for r in range(regions)])
            for k in range(1, regions)
        ]
        here = jnp.concatenate(gathered, axis=0)
        source = (me - jnp.arange(regions, dtype=jnp.int32)[:, None]) % regions
    local = jnp.arange(local_count, dtype=jnp.int32)[None, :]
    station_ids = (source * local_count + local).reshape(stations)
    region_of = here[:, components, 0].astype(jnp.int32)
    rows = here[:, :components, :]
    earlier = (region_of[None, :] == region_of[:, None]) & (station_ids[None, :] < station_ids[:, None])
    ranks = jnp.sum(earlier.astype(jnp.int32), axis=1)
    slot_index = jnp.arange(capacity, dtype=jnp.int32)
    placing = (region_of[None, :] == me) & (ranks[None, :] == slot_index[:, None])
    owned_rows = jnp.dot(
        placing.astype(jnp.bfloat16), rows.reshape(stations, -1), preferred_element_type=jnp.float32
    ).astype(jnp.bfloat16)
    owned_rows = owned_rows.reshape(capacity, components, seg_len + filter_taps)
    filled = jnp.sum(placing.astype(jnp.float32), axis=1)
    return owned_rows, filled


def per_device(records, templates, channel_mask, station_region):
    local_batches, kept, capacity, components, filter_taps = templates.shape
    seg_len = records.shape[2]
    owned_rows, filled = gather_owned(records, station_region, capacity, filter_taps)
    owned_rows = owned_rows.astype(jnp.float32) * filled[:, None, None]
    flat_owned = owned_rows.reshape(capacity * components, seg_len + filter_taps)
    rows = local_batches * kept
    raw = templates.reshape(rows, capacity * components, filter_taps)
    mask = channel_mask.astype(jnp.float32).reshape(rows, capacity * components)
    total_len = seg_len * lax.axis_size("seg")
    stacked = ordered_sum(correlate(raw, mask, flat_owned, seg_len), "region")
    power_sum = ordered_sum(jnp.sum(stacked * stacked, axis=1), "seg")
    detect = unflip(stacked) / jnp.sqrt(power_sum / total_len + 1e-06)[:, None]
    return detect.reshape(local_batches, kept, seg_len)


def solution(mesh):
    placed = (
        P(("groups", "region"), None, "seg"),
        P(("groups", "tb"), None, "region", None, None),
        P(("groups", "tb"), None, "region", None),
        P(("groups", "region")),
    )
    return jax.shard_map(
        per_device,
        mesh=mesh,
        in_specs=placed,
        out_specs=P(("groups", "tb"), None, "seg"),
        check_vma=False,
    )
```

```python
import jax
import jax.numpy as jnp
from jax import lax
from jax.sharding import PartitionSpec as P
from jax.experimental import pallas as pl
from jax.experimental.pallas import tpu as pltpu


def hankel_kernel(x_ref, n_ref, o_ref, h_ref):
    width = h_ref.shape[0]
    channels = n_ref.shape[1] // width
    taps_blocks = width // 128
    out_blocks = o_ref.shape[1] // 128
    blocks = taps_blocks + out_blocks
    row = lax.broadcasted_iota(jnp.int32, (128, 128), 0)
    lane = lax.broadcasted_iota(jnp.int32, (128, 128), 1)
    low = lane >= row

    def one_channel(c, acc):
        rolled = [
            pltpu.roll(x_ref[pl.ds(c * blocks + m, 128, stride=0), :], 0, 1, stride=1, stride_axis=0)
            for m in range(blocks)
        ]
        squares = []
        for m in range(blocks - 1):
            window = jnp.where(low, rolled[m], rolled[m + 1])
            squares.append(jnp.sum(window * window, axis=0, keepdims=True))
            window = window.astype(jnp.bfloat16)
            for p in range(taps_blocks):
                a = m - p
                if 0 <= a < out_blocks:
                    h_ref[p * 128 : (p + 1) * 128, a * 128 : (a + 1) * 128] = window
        energy = jnp.concatenate(
            [sum(squares[a + p] for p in range(taps_blocks)) for a in range(out_blocks)], axis=1
        )
        start = pl.multiple_of(c * width, 128)
        part = jnp.dot(n_ref[:, pl.ds(start, width)], h_ref[...], preferred_element_type=jnp.float32)
        return acc + part * (1.0 / jnp.sqrt(jnp.maximum(energy, 1.0)))

    o_ref[...] = lax.fori_loop(0, channels, one_channel, jnp.zeros(o_ref.shape, jnp.float32))


def unflip(stacked):
    rows, seg_len = stacked.shape
    return stacked.reshape(rows, seg_len // 128, 128)[..., ::-1].reshape(rows, seg_len)


def correlate(normed, flat_owned, seg_len):
    channels = flat_owned.shape[0]
    rows = normed.shape[0]
    filter_taps = normed.shape[1] // channels
    blocks = flat_owned.reshape(channels * (flat_owned.shape[1] // 128), 128)
    return pl.pallas_call(
        hankel_kernel,
        out_shape=jax.ShapeDtypeStruct((rows, seg_len), jnp.float32),
        scratch_shapes=[pltpu.VMEM((filter_taps, seg_len), jnp.bfloat16)],
    )(blocks, normed)


def ordered_sum(part, axis):
    size = lax.axis_size(axis)
    if size & (size - 1) == 0:
        step = 1
        while step < size:
            part = part + lax.ppermute(part, axis, [(i, i ^ step) for i in range(size)])
            step *= 2
        return part
    me = lax.axis_index(axis)
    received = [part] + [
        lax.ppermute(part, axis, [(i, (i + k) % size) for i in range(size)]) for k in range(1, size)
    ]
    order = (me - jnp.arange(size, dtype=jnp.int32)) % size
    return jnp.sum(jnp.take(jnp.stack(received), order, axis=0), axis=0)


def gather_owned(records, station_region, capacity, filter_taps, prepared):
    local_count, components, seg_len = records.shape
    regions = lax.axis_size("region")
    segs = lax.axis_size("seg")
    records = records.reshape(local_count, components, seg_len // 128, 128)[..., ::-1]
    records = records.reshape(local_count, components, seg_len)
    ahead = lax.ppermute(
        records[:, :, :filter_taps], "seg", [(s + 1, s) for s in range(segs - 1)]
    )
    ahead, prepared = lax.optimization_barrier((ahead, prepared))
    tag = jnp.broadcast_to(station_region.astype(jnp.bfloat16)[:, None, None], (local_count, 1, seg_len + filter_taps))
    payload = jnp.concatenate(
        [jnp.concatenate([records, ahead], axis=2), tag], axis=1
    )
    me = lax.axis_index("region")
    stations = regions * local_count
    if regions & (regions - 1) == 0:
        here = payload
        step = 1
        while step < regions:
            theirs = lax.ppermute(here, "region", [(r, r ^ step) for r in range(regions)])
            here = jnp.concatenate([here, theirs], axis=0)
            step *= 2
        source = me ^ jnp.arange(regions, dtype=jnp.int32)[:, None]
    else:
        gathered = [payload] + [
            lax.ppermute(payload, "region", [(r, (r + k) % regions) for r in range(regions)])
            for k in range(1, regions)
        ]
        here = jnp.concatenate(gathered, axis=0)
        source = (me - jnp.arange(regions, dtype=jnp.int32)[:, None]) % regions
    local = jnp.arange(local_count, dtype=jnp.int32)[None, :]
    station_ids = (source * local_count + local).reshape(stations)
    region_of = here[:, components, 0].astype(jnp.int32)
    rows = here[:, :components, :]
    earlier = (region_of[None, :] == region_of[:, None]) & (station_ids[None, :] < station_ids[:, None])
    ranks = jnp.sum(earlier.astype(jnp.int32), axis=1)
    slot_index = jnp.arange(capacity, dtype=jnp.int32)
    placing = (region_of[None, :] == me) & (ranks[None, :] == slot_index[:, None])
    owned_rows = jnp.dot(
        placing.astype(jnp.bfloat16), rows.reshape(stations, -1), preferred_element_type=jnp.float32
    ).astype(jnp.bfloat16)
    owned_rows = owned_rows.reshape(capacity, components, seg_len + filter_taps)
    filled = jnp.sum(placing.astype(jnp.float32), axis=1)
    return owned_rows, filled, prepared


def per_device(records, templates, channel_mask, station_region):
    local_batches, kept, capacity, components, filter_taps = templates.shape
    seg_len = records.shape[2]
    weight = channel_mask.astype(jnp.float32)
    widened_templates = templates.astype(jnp.float32)
    template_norm = jnp.sqrt(
        jnp.sum(widened_templates * widened_templates, axis=4, keepdims=True) + 1e-06
    )
    normed = (widened_templates * weight[..., None] / template_norm).astype(jnp.bfloat16)
    normed = normed.reshape(local_batches * kept, capacity * components * filter_taps)
    owned_rows, filled, normed = gather_owned(records, station_region, capacity, filter_taps, normed)
    owned_rows = owned_rows.astype(jnp.float32) * filled[:, None, None]
    flat_owned = owned_rows.reshape(capacity * components, seg_len + filter_taps)
    total_len = seg_len * lax.axis_size("seg")
    stacked = ordered_sum(correlate(normed, flat_owned, seg_len), "region")
    power_sum = ordered_sum(jnp.sum(stacked * stacked, axis=1), "seg")
    detect = unflip(stacked) / jnp.sqrt(power_sum / total_len + 1e-06)[:, None]
    return detect.reshape(local_batches, kept, seg_len)


def solution(mesh):
    placed = (
        P(("groups", "region"), None, "seg"),
        P(("groups", "tb"), None, "region", None, None),
        P(("groups", "tb"), None, "region", None),
        P(("groups", "region")),
    )
    return jax.shard_map(
        per_device,
        mesh=mesh,
        in_specs=placed,
        out_specs=P(("groups", "tb"), None, "seg"),
        check_vma=False,
    )
```

```python
import jax
import jax.numpy as jnp
from jax import lax
from jax.sharding import PartitionSpec as P
from jax.experimental import pallas as pl
from jax.experimental.pallas import tpu as pltpu


def hankel_kernel(x_ref, n_ref, o_ref, h_ref):
    width = h_ref.shape[1]
    channels = n_ref.shape[1] // width
    taps_blocks = width // 128
    out_blocks = o_ref.shape[1] // 128
    blocks = taps_blocks + out_blocks
    row = lax.broadcasted_iota(jnp.int32, (128, 128), 0)
    lane = lax.broadcasted_iota(jnp.int32, (128, 128), 1)
    low = lane >= row

    def one_channel(c, slot, acc):
        rolled = [
            pltpu.roll(x_ref[pl.ds(c * blocks + m, 128, stride=0), :], 0, 1, stride=1, stride_axis=0)
            for m in range(blocks)
        ]
        squares = []
        for m in range(blocks - 1):
            window = jnp.where(low, rolled[m], rolled[m + 1])
            squares.append(jnp.sum(window * window, axis=0, keepdims=True))
            window = window.astype(jnp.bfloat16)
            for p in range(taps_blocks):
                a = m - p
                if 0 <= a < out_blocks:
                    h_ref[slot, p * 128 : (p + 1) * 128, a * 128 : (a + 1) * 128] = window
        energy = jnp.concatenate(
            [sum(squares[a + p] for p in range(taps_blocks)) for a in range(out_blocks)], axis=1
        )
        start = pl.multiple_of(c * width, 128)
        part = jnp.dot(n_ref[:, pl.ds(start, width)], h_ref[slot], preferred_element_type=jnp.float32)
        return acc + part * (1.0 / jnp.sqrt(jnp.maximum(energy, 1.0)))

    def two_channels(i, acc):
        acc = one_channel(2 * i, 0, acc)
        return one_channel(2 * i + 1, 1, acc)

    acc = jnp.zeros(o_ref.shape, jnp.float32)
    pairs = channels // 2
    acc = lax.fori_loop(0, pairs, two_channels, acc, unroll=2 if pairs % 2 == 0 else 1)
    if channels % 2:
        acc = one_channel(channels - 1, 0, acc)
    o_ref[...] = acc


def unflip(stacked):
    rows, seg_len = stacked.shape
    return stacked.reshape(rows, seg_len // 128, 128)[..., ::-1].reshape(rows, seg_len)


def correlate(normed, flat_owned, seg_len):
    rows, channels, filter_taps = normed.shape
    blocks = flat_owned.reshape(channels * (flat_owned.shape[1] // 128), 128)[:, ::-1]
    return pl.pallas_call(
        hankel_kernel,
        out_shape=jax.ShapeDtypeStruct((rows, seg_len), jnp.float32),
        scratch_shapes=[pltpu.VMEM((2, filter_taps, seg_len), jnp.bfloat16)],
    )(blocks, normed.reshape(rows, channels * filter_taps))


def ordered_sum(part, axis):
    size = lax.axis_size(axis)
    if size & (size - 1) == 0:
        step = 1
        while step < size:
            part = part + lax.ppermute(part, axis, [(i, i ^ step) for i in range(size)])
            step *= 2
        return part
    me = lax.axis_index(axis)
    received = [part] + [
        lax.ppermute(part, axis, [(i, (i + k) % size) for i in range(size)]) for k in range(1, size)
    ]
    order = (me - jnp.arange(size, dtype=jnp.int32)) % size
    return jnp.sum(jnp.take(jnp.stack(received), order, axis=0), axis=0)


def gather_owned(records, station_region, capacity, filter_taps):
    local_count, components, seg_len = records.shape
    regions = lax.axis_size("region")
    segs = lax.axis_size("seg")
    ahead = lax.ppermute(
        records[:, :, :filter_taps], "seg", [(s + 1, s) for s in range(segs - 1)]
    )
    tag = jnp.broadcast_to(station_region.astype(jnp.bfloat16)[:, None, None], (local_count, 1, seg_len + filter_taps))
    payload = jnp.concatenate(
        [jnp.concatenate([records, ahead], axis=2), tag], axis=1
    )
    me = lax.axis_index("region")
    stations = regions * local_count
    if regions & (regions - 1) == 0:
        here = payload
        step = 1
        while step < regions:
            theirs = lax.ppermute(here, "region", [(r, r ^ step) for r in range(regions)])
            here = jnp.concatenate([here, theirs], axis=0)
            step *= 2
        source = me ^ jnp.arange(regions, dtype=jnp.int32)[:, None]
    else:
        gathered = [payload] + [
            lax.ppermute(payload, "region", [(r, (r + k) % regions) for r in range(regions)])
            for k in range(1, regions)
        ]
        here = jnp.concatenate(gathered, axis=0)
        source = (me - jnp.arange(regions, dtype=jnp.int32)[:, None]) % regions
    local = jnp.arange(local_count, dtype=jnp.int32)[None, :]
    station_ids = (source * local_count + local).reshape(stations)
    region_of = here[:, components, 0].astype(jnp.int32)
    rows = here[:, :components, :]
    earlier = (region_of[None, :] == region_of[:, None]) & (station_ids[None, :] < station_ids[:, None])
    ranks = jnp.sum(earlier.astype(jnp.int32), axis=1)
    slot_index = jnp.arange(capacity, dtype=jnp.int32)
    placing = (region_of[None, :] == me) & (ranks[None, :] == slot_index[:, None])
    owned_rows = jnp.dot(
        placing.astype(jnp.bfloat16), rows.reshape(stations, -1), preferred_element_type=jnp.float32
    ).astype(jnp.bfloat16)
    owned_rows = owned_rows.reshape(capacity, components, seg_len + filter_taps)
    filled = jnp.sum(placing.astype(jnp.float32), axis=1)
    return owned_rows, filled


def per_device(records, templates, channel_mask, station_region):
    local_batches, kept, capacity, components, filter_taps = templates.shape
    seg_len = records.shape[2]
    owned_rows, filled = gather_owned(records, station_region, capacity, filter_taps)
    owned_rows = owned_rows.astype(jnp.float32) * filled[:, None, None]
    flat_owned = owned_rows.reshape(capacity * components, seg_len + filter_taps)
    weight = channel_mask.astype(jnp.float32)
    widened_templates = templates.astype(jnp.float32)
    template_norm = jnp.sqrt(
        jnp.sum(widened_templates * widened_templates, axis=4, keepdims=True) + 1e-06
    )
    normed = (widened_templates * weight[..., None] / template_norm).astype(jnp.bfloat16)
    normed = normed.reshape(local_batches * kept, capacity * components, filter_taps)
    total_len = seg_len * lax.axis_size("seg")
    stacked = ordered_sum(correlate(normed, flat_owned, seg_len), "region")
    power_sum = ordered_sum(jnp.sum(stacked * stacked, axis=1), "seg")
    detect = unflip(stacked) / jnp.sqrt(power_sum / total_len + 1e-06)[:, None]
    return detect.reshape(local_batches, kept, seg_len)


def solution(mesh):
    placed = (
        P(("groups", "region"), None, "seg"),
        P(("groups", "tb"), None, "region", None, None),
        P(("groups", "tb"), None, "region", None),
        P(("groups", "region")),
    )
    return jax.shard_map(
        per_device,
        mesh=mesh,
        in_specs=placed,
        out_specs=P(("groups", "tb"), None, "seg"),
        check_vma=False,
    )
```

```python
import jax
import jax.numpy as jnp
from jax import lax
from jax.sharding import PartitionSpec as P
from jax.experimental import pallas as pl
from jax.experimental.pallas import tpu as pltpu


def hankel_kernel(x_ref, n_ref, o_ref, h_ref, r_ref):
    width = h_ref.shape[1]
    channels = n_ref.shape[1] // width
    taps_blocks = width // 128
    out_blocks = o_ref.shape[1] // 128
    blocks = taps_blocks + out_blocks
    row = lax.broadcasted_iota(jnp.int32, (128, 128), 0)
    lane = lax.broadcasted_iota(jnp.int32, (128, 128), 1)
    low = lane >= row
    exchange = (row + lane == 127).astype(jnp.bfloat16)
    r_ref[...] = jnp.dot(x_ref[...], exchange, preferred_element_type=jnp.float32)

    def one_channel(c, slot, acc):
        rolled = [
            pltpu.roll(r_ref[pl.ds(c * blocks + m, 128, stride=0), :], 0, 1, stride=1, stride_axis=0)
            for m in range(blocks)
        ]
        squares = []
        for m in range(blocks - 1):
            window = jnp.where(low, rolled[m], rolled[m + 1])
            squares.append(jnp.sum(window * window, axis=0, keepdims=True))
            window = window.astype(jnp.bfloat16)
            for p in range(taps_blocks):
                a = m - p
                if 0 <= a < out_blocks:
                    h_ref[slot, p * 128 : (p + 1) * 128, a * 128 : (a + 1) * 128] = window
        energy = jnp.concatenate(
            [sum(squares[a + p] for p in range(taps_blocks)) for a in range(out_blocks)], axis=1
        )
        start = pl.multiple_of(c * width, 128)
        part = jnp.dot(n_ref[:, pl.ds(start, width)], h_ref[slot], preferred_element_type=jnp.float32)
        return acc + part * (1.0 / jnp.sqrt(jnp.maximum(energy, 1.0)))

    def two_channels(i, acc):
        acc = one_channel(2 * i, 0, acc)
        return one_channel(2 * i + 1, 1, acc)

    acc = jnp.zeros(o_ref.shape, jnp.float32)
    pairs = channels // 2
    acc = lax.fori_loop(0, pairs, two_channels, acc, unroll=2 if pairs % 2 == 0 else 1)
    if channels % 2:
        acc = one_channel(channels - 1, 0, acc)
    o_ref[...] = acc


def unflip(stacked):
    rows, seg_len = stacked.shape
    return stacked.reshape(rows, seg_len // 128, 128)[..., ::-1].reshape(rows, seg_len)


def correlate(normed, flat_owned, seg_len):
    rows, channels, filter_taps = normed.shape
    blocks = flat_owned.reshape(channels * (flat_owned.shape[1] // 128), 128)
    return pl.pallas_call(
        hankel_kernel,
        out_shape=jax.ShapeDtypeStruct((rows, seg_len), jnp.float32),
        scratch_shapes=[
            pltpu.VMEM((2, filter_taps, seg_len), jnp.bfloat16),
            pltpu.VMEM(blocks.shape, jnp.float32),
        ],
    )(blocks, normed.reshape(rows, channels * filter_taps))


def ordered_sum(part, axis):
    size = lax.axis_size(axis)
    if size & (size - 1) == 0:
        step = 1
        while step < size:
            part = part + lax.ppermute(part, axis, [(i, i ^ step) for i in range(size)])
            step *= 2
        return part
    me = lax.axis_index(axis)
    received = [part] + [
        lax.ppermute(part, axis, [(i, (i + k) % size) for i in range(size)]) for k in range(1, size)
    ]
    order = (me - jnp.arange(size, dtype=jnp.int32)) % size
    return jnp.sum(jnp.take(jnp.stack(received), order, axis=0), axis=0)


def gather_owned(records, station_region, capacity, filter_taps):
    local_count, components, seg_len = records.shape
    regions = lax.axis_size("region")
    segs = lax.axis_size("seg")
    ahead = lax.ppermute(
        records[:, :, :filter_taps], "seg", [(s + 1, s) for s in range(segs - 1)]
    )
    tag = jnp.broadcast_to(station_region.astype(jnp.bfloat16)[:, None, None], (local_count, 1, seg_len + filter_taps))
    payload = jnp.concatenate(
        [jnp.concatenate([records, ahead], axis=2), tag], axis=1
    )
    me = lax.axis_index("region")
    stations = regions * local_count
    if regions & (regions - 1) == 0:
        here = payload
        step = 1
        while step < regions:
            theirs = lax.ppermute(here, "region", [(r, r ^ step) for r in range(regions)])
            here = jnp.concatenate([here, theirs], axis=0)
            step *= 2
        source = me ^ jnp.arange(regions, dtype=jnp.int32)[:, None]
    else:
        gathered = [payload] + [
            lax.ppermute(payload, "region", [(r, (r + k) % regions) for r in range(regions)])
            for k in range(1, regions)
        ]
        here = jnp.concatenate(gathered, axis=0)
        source = (me - jnp.arange(regions, dtype=jnp.int32)[:, None]) % regions
    local = jnp.arange(local_count, dtype=jnp.int32)[None, :]
    station_ids = (source * local_count + local).reshape(stations)
    region_of = here[:, components, 0].astype(jnp.int32)
    rows = here[:, :components, :]
    earlier = (region_of[None, :] == region_of[:, None]) & (station_ids[None, :] < station_ids[:, None])
    ranks = jnp.sum(earlier.astype(jnp.int32), axis=1)
    slot_index = jnp.arange(capacity, dtype=jnp.int32)
    placing = (region_of[None, :] == me) & (ranks[None, :] == slot_index[:, None])
    owned_rows = jnp.dot(
        placing.astype(jnp.bfloat16), rows.reshape(stations, -1), preferred_element_type=jnp.float32
    ).astype(jnp.bfloat16)
    owned_rows = owned_rows.reshape(capacity, components, seg_len + filter_taps)
    filled = jnp.sum(placing.astype(jnp.float32), axis=1)
    return owned_rows, filled


def per_device(records, templates, channel_mask, station_region):
    local_batches, kept, capacity, components, filter_taps = templates.shape
    seg_len = records.shape[2]
    owned_rows, filled = gather_owned(records, station_region, capacity, filter_taps)
    owned_rows = owned_rows * filled.astype(jnp.bfloat16)[:, None, None]
    flat_owned = owned_rows.reshape(capacity * components, seg_len + filter_taps)
    weight = channel_mask.astype(jnp.float32)
    widened_templates = templates.astype(jnp.float32)
    template_norm = jnp.sqrt(
        jnp.sum(widened_templates * widened_templates, axis=4, keepdims=True) + 1e-06
    )
    normed = (widened_templates * weight[..., None] / template_norm).astype(jnp.bfloat16)
    normed = normed.reshape(local_batches * kept, capacity * components, filter_taps)
    total_len = seg_len * lax.axis_size("seg")
    stacked = ordered_sum(correlate(normed, flat_owned, seg_len), "region")
    power_sum = ordered_sum(jnp.sum(stacked * stacked, axis=1), "seg")
    detect = unflip(stacked) / jnp.sqrt(power_sum / total_len + 1e-06)[:, None]
    return detect.reshape(local_batches, kept, seg_len)


def solution(mesh):
    placed = (
        P(("groups", "region"), None, "seg"),
        P(("groups", "tb"), None, "region", None, None),
        P(("groups", "tb"), None, "region", None),
        P(("groups", "region")),
    )
    return jax.shard_map(
        per_device,
        mesh=mesh,
        in_specs=placed,
        out_specs=P(("groups", "tb"), None, "seg"),
        check_vma=False,
    )
```

```python
import jax
import jax.numpy as jnp
from jax import lax
from jax.sharding import PartitionSpec as P
from jax.experimental import pallas as pl
from jax.experimental.pallas import tpu as pltpu


def hankel_kernel(x_ref, n_ref, o_ref, h_ref):
    width = h_ref.shape[1]
    channels = n_ref.shape[1] // width
    taps_blocks = width // 128
    out_blocks = o_ref.shape[1] // 128
    blocks = taps_blocks + out_blocks
    row = lax.broadcasted_iota(jnp.int32, (128, 128), 0)
    lane = lax.broadcasted_iota(jnp.int32, (128, 128), 1)
    low = lane >= row

    def one_channel(c, slot, acc):
        rolled = [
            pltpu.roll(x_ref[pl.ds(c * blocks + m, 128, stride=0), :], 0, 1, stride=1, stride_axis=0)
            for m in range(blocks)
        ]
        squares = []
        for m in range(blocks - 1):
            window = jnp.where(low, rolled[m], rolled[m + 1])
            squares.append(jnp.sum(window * window, axis=0, keepdims=True))
            window = window.astype(jnp.bfloat16)
            for p in range(taps_blocks):
                a = m - p
                if 0 <= a < out_blocks:
                    h_ref[slot, p * 128 : (p + 1) * 128, a * 128 : (a + 1) * 128] = window
        energy = jnp.concatenate(
            [sum(squares[a + p] for p in range(taps_blocks)) for a in range(out_blocks)], axis=1
        )
        start = pl.multiple_of(c * width, 128)
        part = jnp.dot(n_ref[:, pl.ds(start, width)], h_ref[slot], preferred_element_type=jnp.float32)
        return acc + part * (1.0 / jnp.sqrt(jnp.maximum(energy, 1.0)))

    def two_channels(i, acc):
        acc = one_channel(2 * i, 0, acc)
        return one_channel(2 * i + 1, 1, acc)

    acc = jnp.zeros(o_ref.shape, jnp.float32)
    pairs = channels // 2
    acc = lax.fori_loop(0, pairs, two_channels, acc, unroll=2 if pairs % 2 == 0 else 1)
    if channels % 2:
        acc = one_channel(channels - 1, 0, acc)
    o_ref[...] = acc


def unflip(stacked):
    rows, seg_len = stacked.shape
    return stacked.reshape(rows, seg_len // 128, 128)[..., ::-1].reshape(rows, seg_len)


def correlate(normed, flat_owned, seg_len):
    channels = flat_owned.shape[0]
    rows = normed.shape[0]
    filter_taps = normed.shape[1] // channels
    blocks = flat_owned.reshape(channels * (flat_owned.shape[1] // 128), 128)[:, ::-1]
    return pl.pallas_call(
        hankel_kernel,
        out_shape=jax.ShapeDtypeStruct((rows, seg_len), jnp.float32),
        scratch_shapes=[pltpu.VMEM((2, filter_taps, seg_len), jnp.bfloat16)],
    )(blocks, normed)


def ordered_sum(part, axis):
    size = lax.axis_size(axis)
    if size & (size - 1) == 0:
        step = 1
        while step < size:
            part = part + lax.ppermute(part, axis, [(i, i ^ step) for i in range(size)])
            step *= 2
        return part
    me = lax.axis_index(axis)
    received = [part] + [
        lax.ppermute(part, axis, [(i, (i + k) % size) for i in range(size)]) for k in range(1, size)
    ]
    order = (me - jnp.arange(size, dtype=jnp.int32)) % size
    return jnp.sum(jnp.take(jnp.stack(received), order, axis=0), axis=0)


def gather_owned(records, station_region, capacity, filter_taps, prepared):
    local_count, components, seg_len = records.shape
    regions = lax.axis_size("region")
    segs = lax.axis_size("seg")
    ahead = lax.ppermute(
        records[:, :, :filter_taps], "seg", [(s + 1, s) for s in range(segs - 1)]
    )
    tag = jnp.broadcast_to(station_region.astype(jnp.bfloat16)[:, None, None], (local_count, 1, seg_len + filter_taps))
    payload = jnp.concatenate(
        [jnp.concatenate([records, ahead], axis=2), tag], axis=1
    )
    me = lax.axis_index("region")
    stations = regions * local_count
    if regions & (regions - 1) == 0:
        here = payload
        step = 1
        while step < regions:
            theirs = lax.ppermute(here, "region", [(r, r ^ step) for r in range(regions)])
            if step == 1:
                theirs, prepared = lax.optimization_barrier((theirs, prepared))
            here = jnp.concatenate([here, theirs], axis=0)
            step *= 2
        source = me ^ jnp.arange(regions, dtype=jnp.int32)[:, None]
    else:
        gathered = [payload] + [
            lax.ppermute(payload, "region", [(r, (r + k) % regions) for r in range(regions)])
            for k in range(1, regions)
        ]
        here = jnp.concatenate(gathered, axis=0)
        source = (me - jnp.arange(regions, dtype=jnp.int32)[:, None]) % regions
    local = jnp.arange(local_count, dtype=jnp.int32)[None, :]
    station_ids = (source * local_count + local).reshape(stations)
    region_of = here[:, components, 0].astype(jnp.int32)
    rows = here[:, :components, :]
    earlier = (region_of[None, :] == region_of[:, None]) & (station_ids[None, :] < station_ids[:, None])
    ranks = jnp.sum(earlier.astype(jnp.int32), axis=1)
    slot_index = jnp.arange(capacity, dtype=jnp.int32)
    placing = (region_of[None, :] == me) & (ranks[None, :] == slot_index[:, None])
    owned_rows = jnp.dot(
        placing.astype(jnp.bfloat16), rows.reshape(stations, -1), preferred_element_type=jnp.float32
    ).astype(jnp.bfloat16)
    owned_rows = owned_rows.reshape(capacity, components, seg_len + filter_taps)
    filled = jnp.sum(placing.astype(jnp.float32), axis=1)
    return owned_rows, filled, prepared


def per_device(records, templates, channel_mask, station_region):
    local_batches, kept, capacity, components, filter_taps = templates.shape
    seg_len = records.shape[2]
    weight = channel_mask.astype(jnp.float32)
    widened_templates = templates.astype(jnp.float32)
    template_norm = jnp.sqrt(
        jnp.sum(widened_templates * widened_templates, axis=4, keepdims=True) + 1e-06
    )
    normed = (widened_templates * weight[..., None] / template_norm).astype(jnp.bfloat16)
    normed = normed.reshape(local_batches * kept, capacity * components * filter_taps)
    owned_rows, filled, normed = gather_owned(records, station_region, capacity, filter_taps, normed)
    owned_rows = owned_rows.astype(jnp.float32) * filled[:, None, None]
    flat_owned = owned_rows.reshape(capacity * components, seg_len + filter_taps)
    total_len = seg_len * lax.axis_size("seg")
    stacked = ordered_sum(correlate(normed, flat_owned, seg_len), "region")
    power_sum = ordered_sum(jnp.sum(stacked * stacked, axis=1), "seg")
    detect = unflip(stacked) / jnp.sqrt(power_sum / total_len + 1e-06)[:, None]
    return detect.reshape(local_batches, kept, seg_len)


def solution(mesh):
    placed = (
        P(("groups", "region"), None, "seg"),
        P(("groups", "tb"), None, "region", None, None),
        P(("groups", "tb"), None, "region", None),
        P(("groups", "region")),
    )
    return jax.shard_map(
        per_device,
        mesh=mesh,
        in_specs=placed,
        out_specs=P(("groups", "tb"), None, "seg"),
        check_vma=False,
    )
```

```python
import jax
import jax.numpy as jnp
from jax import lax
from jax.sharding import PartitionSpec as P
from jax.experimental import pallas as pl
from jax.experimental.pallas import tpu as pltpu


def hankel_kernel(x_ref, n_ref, o_ref, h_ref):
    width = h_ref.shape[1]
    channels = n_ref.shape[1] // width
    taps_blocks = width // 128
    out_blocks = o_ref.shape[1] // 128
    blocks = taps_blocks + out_blocks
    row = lax.broadcasted_iota(jnp.int32, (128, 128), 0)
    lane = lax.broadcasted_iota(jnp.int32, (128, 128), 1)
    low = lane >= row

    def one_channel(c, slot, acc):
        rolled = [
            pltpu.roll(x_ref[pl.ds(c * blocks + m, 128, stride=0), :], 0, 1, stride=1, stride_axis=0)
            for m in range(blocks)
        ]
        squares = []
        for m in range(blocks - 1):
            window = jnp.where(low, rolled[m], rolled[m + 1])
            squares.append(jnp.sum(window * window, axis=0, keepdims=True))
            window = window.astype(jnp.bfloat16)
            for p in range(taps_blocks):
                a = m - p
                if 0 <= a < out_blocks:
                    h_ref[slot, p * 128 : (p + 1) * 128, a * 128 : (a + 1) * 128] = window
        energy = jnp.concatenate(
            [sum(squares[a + p] for p in range(taps_blocks)) for a in range(out_blocks)], axis=1
        )
        start = pl.multiple_of(c * width, 128)
        part = jnp.dot(n_ref[:, pl.ds(start, width)], h_ref[slot], preferred_element_type=jnp.float32)
        return acc + part * (1.0 / jnp.sqrt(jnp.maximum(energy, 1.0)))

    def two_channels(i, acc):
        acc = one_channel(2 * i, 0, acc)
        return one_channel(2 * i + 1, 1, acc)

    acc = jnp.zeros(o_ref.shape, jnp.float32)
    pairs = channels // 2
    acc = lax.fori_loop(0, pairs, two_channels, acc, unroll=2 if pairs % 2 == 0 else 1)
    if channels % 2:
        acc = one_channel(channels - 1, 0, acc)
    o_ref[...] = acc


def unflip(stacked):
    rows, seg_len = stacked.shape
    return stacked.reshape(rows, seg_len // 128, 128)[..., ::-1].reshape(rows, seg_len)


def correlate(normed, flat_owned, seg_len):
    rows, channels, filter_taps = normed.shape
    blocks = flat_owned.reshape(channels * (flat_owned.shape[1] // 128), 128)[:, ::-1]
    return pl.pallas_call(
        hankel_kernel,
        out_shape=jax.ShapeDtypeStruct((rows, seg_len), jnp.float32),
        scratch_shapes=[pltpu.VMEM((2, filter_taps, seg_len), jnp.bfloat16)],
    )(blocks, normed.reshape(rows, channels * filter_taps))


def ordered_sum(part, axis):
    size = lax.axis_size(axis)
    if size & (size - 1) == 0:
        step = 1
        while step < size:
            part = part + lax.ppermute(part, axis, [(i, i ^ step) for i in range(size)])
            step *= 2
        return part
    me = lax.axis_index(axis)
    received = [part] + [
        lax.ppermute(part, axis, [(i, (i + k) % size) for i in range(size)]) for k in range(1, size)
    ]
    order = (me - jnp.arange(size, dtype=jnp.int32)) % size
    return jnp.sum(jnp.take(jnp.stack(received), order, axis=0), axis=0)


def gather_owned(records, station_region, capacity, filter_taps):
    local_count, components, seg_len = records.shape
    regions = lax.axis_size("region")
    segs = lax.axis_size("seg")
    tag = jnp.broadcast_to(station_region.astype(jnp.bfloat16)[:, None, None], (local_count, 1, seg_len))
    payload = jnp.concatenate([records, tag], axis=1)
    everyone = regions * segs
    spread = jnp.broadcast_to(payload[None], (everyone,) + payload.shape)
    arrived = lax.all_to_all(spread, ("region", "seg"), 0, 0, tiled=True)
    arrived = arrived.reshape(regions, segs, local_count, components + 1, seg_len)
    me = lax.axis_index("region")
    seg_index = lax.axis_index("seg")
    stations = regions * local_count
    here = jnp.take(arrived, seg_index, axis=1)
    following = jnp.take(arrived, jnp.minimum(seg_index + 1, segs - 1), axis=1)[:, :, :components, :filter_taps]
    following = jnp.where(seg_index + 1 < segs, following, jnp.zeros_like(following))
    here = here.reshape(stations, components + 1, seg_len)
    following = following.reshape(stations, components, filter_taps)
    local = jnp.arange(local_count, dtype=jnp.int32)[None, :]
    source = jnp.arange(regions, dtype=jnp.int32)[:, None]
    station_ids = (source * local_count + local).reshape(stations)
    region_of = here[:, components, 0].astype(jnp.int32)
    rows = jnp.concatenate([here[:, :components, :], following], axis=2)
    earlier = (region_of[None, :] == region_of[:, None]) & (station_ids[None, :] < station_ids[:, None])
    ranks = jnp.sum(earlier.astype(jnp.int32), axis=1)
    slot_index = jnp.arange(capacity, dtype=jnp.int32)
    placing = (region_of[None, :] == me) & (ranks[None, :] == slot_index[:, None])
    owned_rows = jnp.dot(
        placing.astype(jnp.bfloat16), rows.reshape(stations, -1), preferred_element_type=jnp.float32
    ).astype(jnp.bfloat16)
    owned_rows = owned_rows.reshape(capacity, components, seg_len + filter_taps)
    filled = jnp.sum(placing.astype(jnp.float32), axis=1)
    return owned_rows, filled


def per_device(records, templates, channel_mask, station_region):
    local_batches, kept, capacity, components, filter_taps = templates.shape
    seg_len = records.shape[2]
    owned_rows, filled = gather_owned(records, station_region, capacity, filter_taps)
    owned_rows = owned_rows.astype(jnp.float32) * filled[:, None, None]
    flat_owned = owned_rows.reshape(capacity * components, seg_len + filter_taps)
    weight = channel_mask.astype(jnp.float32)
    widened_templates = templates.astype(jnp.float32)
    template_norm = jnp.sqrt(
        jnp.sum(widened_templates * widened_templates, axis=4, keepdims=True) + 1e-06
    )
    normed = (widened_templates * weight[..., None] / template_norm).astype(jnp.bfloat16)
    normed = normed.reshape(local_batches * kept, capacity * components, filter_taps)
    total_len = seg_len * lax.axis_size("seg")
    stacked = ordered_sum(correlate(normed, flat_owned, seg_len), "region")
    power_sum = ordered_sum(jnp.sum(stacked * stacked, axis=1), "seg")
    detect = unflip(stacked) / jnp.sqrt(power_sum / total_len + 1e-06)[:, None]
    return detect.reshape(local_batches, kept, seg_len)


def solution(mesh):
    placed = (
        P(("groups", "region"), None, "seg"),
        P(("groups", "tb"), None, "region", None, None),
        P(("groups", "tb"), None, "region", None),
        P(("groups", "region")),
    )
    return jax.shard_map(
        per_device,
        mesh=mesh,
        in_specs=placed,
        out_specs=P(("groups", "tb"), None, "seg"),
        check_vma=False,
    )
```

```python
import jax
import jax.numpy as jnp
from jax import lax
from jax.sharding import PartitionSpec as P
from jax.experimental import pallas as pl
from jax.experimental.pallas import tpu as pltpu


def hankel_kernel(x_ref, n_ref, o_ref, h_ref):
    width = h_ref.shape[1]
    channels = n_ref.shape[1] // width
    taps_blocks = width // 128
    out_blocks = o_ref.shape[1] // 128
    blocks = taps_blocks + out_blocks
    row = lax.broadcasted_iota(jnp.int32, (128, 128), 0)
    lane = lax.broadcasted_iota(jnp.int32, (128, 128), 1)
    low = lane >= row

    def one_channel(c, slot, acc):
        rolled = [
            pltpu.roll(x_ref[pl.ds(c * blocks + m, 128, stride=0), :], 0, 1, stride=1, stride_axis=0)
            for m in range(blocks)
        ]
        squares = []
        for m in range(blocks - 1):
            window = jnp.where(low, rolled[m], rolled[m + 1])
            squares.append(jnp.sum(window * window, axis=0, keepdims=True))
            window = window.astype(jnp.bfloat16)
            for p in range(taps_blocks):
                a = m - p
                if 0 <= a < out_blocks:
                    h_ref[slot, p * 128 : (p + 1) * 128, a * 128 : (a + 1) * 128] = window
        energy = jnp.concatenate(
            [sum(squares[a + p] for p in range(taps_blocks)) for a in range(out_blocks)], axis=1
        )
        start = pl.multiple_of(c * width, 128)
        part = jnp.dot(n_ref[:, pl.ds(start, width)], h_ref[slot], preferred_element_type=jnp.float32)
        return acc + part * (1.0 / jnp.sqrt(jnp.maximum(energy, 1.0)))

    def two_channels(i, acc):
        acc = one_channel(2 * i, 0, acc)
        return one_channel(2 * i + 1, 1, acc)

    acc = jnp.zeros(o_ref.shape, jnp.float32)
    if channels <= 16:
        for c in range(channels):
            acc = one_channel(c, c % 2, acc)
    else:
        pairs = channels // 2
        acc = lax.fori_loop(0, pairs, two_channels, acc, unroll=2 if pairs % 2 == 0 else 1)
        if channels % 2:
            acc = one_channel(channels - 1, 0, acc)
    o_ref[...] = acc


def unflip(stacked):
    rows, seg_len = stacked.shape
    return stacked.reshape(rows, seg_len // 128, 128)[..., ::-1].reshape(rows, seg_len)


def correlate(normed, flat_owned, seg_len):
    rows, channels, filter_taps = normed.shape
    blocks = flat_owned.reshape(channels * (flat_owned.shape[1] // 128), 128)[:, ::-1]
    return pl.pallas_call(
        hankel_kernel,
        out_shape=jax.ShapeDtypeStruct((rows, seg_len), jnp.float32),
        scratch_shapes=[pltpu.VMEM((2, filter_taps, seg_len), jnp.bfloat16)],
    )(blocks, normed.reshape(rows, channels * filter_taps))


def ordered_sum(part, axis):
    size = lax.axis_size(axis)
    if size & (size - 1) == 0:
        step = 1
        while step < size:
            part = part + lax.ppermute(part, axis, [(i, i ^ step) for i in range(size)])
            step *= 2
        return part
    me = lax.axis_index(axis)
    received = [part] + [
        lax.ppermute(part, axis, [(i, (i + k) % size) for i in range(size)]) for k in range(1, size)
    ]
    order = (me - jnp.arange(size, dtype=jnp.int32)) % size
    return jnp.sum(jnp.take(jnp.stack(received), order, axis=0), axis=0)


def gather_owned(records, station_region, capacity, filter_taps):
    local_count, components, seg_len = records.shape
    regions = lax.axis_size("region")
    segs = lax.axis_size("seg")
    ahead = lax.ppermute(
        records[:, :, :filter_taps], "seg", [(s + 1, s) for s in range(segs - 1)]
    )
    tag = jnp.broadcast_to(station_region.astype(jnp.bfloat16)[:, None, None], (local_count, 1, seg_len + filter_taps))
    payload = jnp.concatenate(
        [jnp.concatenate([records, ahead], axis=2), tag], axis=1
    )
    me = lax.axis_index("region")
    stations = regions * local_count
    if regions & (regions - 1) == 0:
        here = payload
        step = 1
        while step < regions:
            theirs = lax.ppermute(here, "region", [(r, r ^ step) for r in range(regions)])
            here = jnp.concatenate([here, theirs], axis=0)
            step *= 2
        source = me ^ jnp.arange(regions, dtype=jnp.int32)[:, None]
    else:
        gathered = [payload] + [
            lax.ppermute(payload, "region", [(r, (r + k) % regions) for r in range(regions)])
            for k in range(1, regions)
        ]
        here = jnp.concatenate(gathered, axis=0)
        source = (me - jnp.arange(regions, dtype=jnp.int32)[:, None]) % regions
    local = jnp.arange(local_count, dtype=jnp.int32)[None, :]
    station_ids = (source * local_count + local).reshape(stations)
    region_of = here[:, components, 0].astype(jnp.int32)
    rows = here[:, :components, :]
    earlier = (region_of[None, :] == region_of[:, None]) & (station_ids[None, :] < station_ids[:, None])
    ranks = jnp.sum(earlier.astype(jnp.int32), axis=1)
    slot_index = jnp.arange(capacity, dtype=jnp.int32)
    placing = (region_of[None, :] == me) & (ranks[None, :] == slot_index[:, None])
    owned_rows = jnp.dot(
        placing.astype(jnp.bfloat16), rows.reshape(stations, -1), preferred_element_type=jnp.float32
    ).astype(jnp.bfloat16)
    owned_rows = owned_rows.reshape(capacity, components, seg_len + filter_taps)
    filled = jnp.sum(placing.astype(jnp.float32), axis=1)
    return owned_rows, filled


def per_device(records, templates, channel_mask, station_region):
    local_batches, kept, capacity, components, filter_taps = templates.shape
    seg_len = records.shape[2]
    owned_rows, filled = gather_owned(records, station_region, capacity, filter_taps)
    owned_rows = owned_rows.astype(jnp.float32) * filled[:, None, None]
    flat_owned = owned_rows.reshape(capacity * components, seg_len + filter_taps)
    weight = channel_mask.astype(jnp.float32)
    widened_templates = templates.astype(jnp.float32)
    template_norm = jnp.sqrt(
        jnp.sum(widened_templates * widened_templates, axis=4, keepdims=True) + 1e-06
    )
    normed = (widened_templates * weight[..., None] / template_norm).astype(jnp.bfloat16)
    normed = normed.reshape(local_batches * kept, capacity * components, filter_taps)
    total_len = seg_len * lax.axis_size("seg")
    stacked = ordered_sum(correlate(normed, flat_owned, seg_len), "region")
    power_sum = ordered_sum(jnp.sum(stacked * stacked, axis=1), "seg")
    detect = unflip(stacked) / jnp.sqrt(power_sum / total_len + 1e-06)[:, None]
    return detect.reshape(local_batches, kept, seg_len)


def solution(mesh):
    placed = (
        P(("groups", "region"), None, "seg"),
        P(("groups", "tb"), None, "region", None, None),
        P(("groups", "tb"), None, "region", None),
        P(("groups", "region")),
    )
    return jax.shard_map(
        per_device,
        mesh=mesh,
        in_specs=placed,
        out_specs=P(("groups", "tb"), None, "seg"),
        check_vma=False,
    )
```

```python
import jax
import jax.numpy as jnp
from jax import lax
from jax.sharding import PartitionSpec as P
from jax.experimental import pallas as pl
from jax.experimental.pallas import tpu as pltpu


def hankel_kernel(x_ref, n_ref, o_ref, h_ref):
    width = h_ref.shape[1]
    channels = n_ref.shape[1] // width
    taps_blocks = width // 128
    out_blocks = o_ref.shape[1] // 128
    blocks = taps_blocks + out_blocks
    row = lax.broadcasted_iota(jnp.int32, (128, 128), 0)
    lane = lax.broadcasted_iota(jnp.int32, (128, 128), 1)
    low = lane >= row

    def one_channel(c, slot, acc):
        rolled = [
            pltpu.roll(x_ref[pl.ds(c * blocks + m, 128, stride=0), :], 0, 1, stride=1, stride_axis=0)
            for m in range(blocks)
        ]
        squares = []
        for m in range(blocks - 1):
            window = jnp.where(low, rolled[m], rolled[m + 1])
            squares.append(jnp.sum(window * window, axis=0, keepdims=True))
            window = window.astype(jnp.bfloat16)
            for p in range(taps_blocks):
                a = m - p
                if 0 <= a < out_blocks:
                    h_ref[slot, p * 128 : (p + 1) * 128, a * 128 : (a + 1) * 128] = window
        energy = jnp.concatenate(
            [sum(squares[a + p] for p in range(taps_blocks)) for a in range(out_blocks)], axis=1
        )
        start = pl.multiple_of(c * width, 128)
        part = jnp.dot(n_ref[:, pl.ds(start, width)], h_ref[slot], preferred_element_type=jnp.float32)
        return acc + part * (1.0 / jnp.sqrt(jnp.maximum(energy, 1.0)))

    def two_channels(i, acc):
        acc = one_channel(2 * i, 0, acc)
        return one_channel(2 * i + 1, 1, acc)

    acc = jnp.zeros(o_ref.shape, jnp.float32)
    if channels <= 16:
        for c in range(channels):
            acc = one_channel(c, c % 2, acc)
    else:
        pairs = channels // 2
        acc = lax.fori_loop(0, pairs, two_channels, acc, unroll=2 if pairs % 2 == 0 else 1)
        if channels % 2:
            acc = one_channel(channels - 1, 0, acc)
    o_ref[...] = acc


def unflip(stacked):
    rows, seg_len = stacked.shape
    return stacked.reshape(rows, seg_len // 128, 128)[..., ::-1].reshape(rows, seg_len)


def correlate(normed, flat_owned, seg_len):
    rows, channels, filter_taps = normed.shape
    blocks = flat_owned.reshape(channels * (flat_owned.shape[1] // 128), 128)[:, ::-1]
    return pl.pallas_call(
        hankel_kernel,
        out_shape=jax.ShapeDtypeStruct((rows, seg_len), jnp.float32),
        scratch_shapes=[pltpu.VMEM((2, filter_taps, seg_len), jnp.bfloat16)],
    )(blocks, normed.reshape(rows, channels * filter_taps))


def ordered_sum(part, axis):
    size = lax.axis_size(axis)
    if size & (size - 1) == 0:
        step = 1
        while step < size:
            part = part + lax.ppermute(part, axis, [(i, i ^ step) for i in range(size)])
            step *= 2
        return part
    me = lax.axis_index(axis)
    received = [part] + [
        lax.ppermute(part, axis, [(i, (i + k) % size) for i in range(size)]) for k in range(1, size)
    ]
    order = (me - jnp.arange(size, dtype=jnp.int32)) % size
    return jnp.sum(jnp.take(jnp.stack(received), order, axis=0), axis=0)


def gather_owned(records, station_region, capacity, filter_taps):
    local_count, components, seg_len = records.shape
    regions = lax.axis_size("region")
    segs = lax.axis_size("seg")
    ahead = lax.ppermute(
        records[:, :, :filter_taps], "seg", [(s + 1, s) for s in range(segs - 1)]
    )
    tag = jnp.broadcast_to(station_region.astype(jnp.bfloat16)[:, None, None], (local_count, 1, seg_len + filter_taps))
    payload = jnp.concatenate(
        [jnp.concatenate([records, ahead], axis=2), tag], axis=1
    )
    me = lax.axis_index("region")
    stations = regions * local_count
    spread = jnp.broadcast_to(payload[None], (regions,) + payload.shape)
    here = lax.all_to_all(spread, "region", 0, 0, tiled=True).reshape((stations,) + payload.shape[1:])
    source = jnp.arange(regions, dtype=jnp.int32)[:, None]
    local = jnp.arange(local_count, dtype=jnp.int32)[None, :]
    station_ids = (source * local_count + local).reshape(stations)
    region_of = here[:, components, 0].astype(jnp.int32)
    rows = here[:, :components, :]
    earlier = (region_of[None, :] == region_of[:, None]) & (station_ids[None, :] < station_ids[:, None])
    ranks = jnp.sum(earlier.astype(jnp.int32), axis=1)
    slot_index = jnp.arange(capacity, dtype=jnp.int32)
    placing = (region_of[None, :] == me) & (ranks[None, :] == slot_index[:, None])
    owned_rows = jnp.dot(
        placing.astype(jnp.bfloat16), rows.reshape(stations, -1), preferred_element_type=jnp.float32
    ).astype(jnp.bfloat16)
    owned_rows = owned_rows.reshape(capacity, components, seg_len + filter_taps)
    filled = jnp.sum(placing.astype(jnp.float32), axis=1)
    return owned_rows, filled


def per_device(records, templates, channel_mask, station_region):
    local_batches, kept, capacity, components, filter_taps = templates.shape
    seg_len = records.shape[2]
    owned_rows, filled = gather_owned(records, station_region, capacity, filter_taps)
    owned_rows = owned_rows.astype(jnp.float32) * filled[:, None, None]
    flat_owned = owned_rows.reshape(capacity * components, seg_len + filter_taps)
    weight = channel_mask.astype(jnp.float32)
    widened_templates = templates.astype(jnp.float32)
    template_norm = jnp.sqrt(
        jnp.sum(widened_templates * widened_templates, axis=4, keepdims=True) + 1e-06
    )
    normed = (widened_templates * weight[..., None] / template_norm).astype(jnp.bfloat16)
    normed = normed.reshape(local_batches * kept, capacity * components, filter_taps)
    total_len = seg_len * lax.axis_size("seg")
    stacked = ordered_sum(correlate(normed, flat_owned, seg_len), "region")
    power_sum = ordered_sum(jnp.sum(stacked * stacked, axis=1), "seg")
    detect = unflip(stacked) / jnp.sqrt(power_sum / total_len + 1e-06)[:, None]
    return detect.reshape(local_batches, kept, seg_len)


def solution(mesh):
    placed = (
        P(("groups", "region"), None, "seg"),
        P(("groups", "tb"), None, "region", None, None),
        P(("groups", "tb"), None, "region", None),
        P(("groups", "region")),
    )
    return jax.shard_map(
        per_device,
        mesh=mesh,
        in_specs=placed,
        out_specs=P(("groups", "tb"), None, "seg"),
        check_vma=False,
    )
```

```python
import jax
import jax.numpy as jnp
from jax import lax
from jax.sharding import PartitionSpec as P
from jax.experimental import pallas as pl
from jax.experimental.pallas import tpu as pltpu


def hankel_kernel(x_ref, n_ref, o_ref, h_ref):
    width = h_ref.shape[1]
    channels = n_ref.shape[1] // width
    taps_blocks = width // 128
    out_blocks = o_ref.shape[1] // 128
    blocks = taps_blocks + out_blocks
    row = lax.broadcasted_iota(jnp.int32, (128, 128), 0)
    lane = lax.broadcasted_iota(jnp.int32, (128, 128), 1)
    low = lane >= row

    def one_channel(c, slot, acc):
        rolled = [
            pltpu.roll(x_ref[pl.ds(c * blocks + m, 128, stride=0), :], 0, 1, stride=1, stride_axis=0)
            for m in range(blocks)
        ]
        squares = []
        for m in range(blocks - 1):
            window = jnp.where(low, rolled[m], rolled[m + 1])
            squares.append(jnp.sum(window * window, axis=0, keepdims=True))
            window = window.astype(jnp.bfloat16)
            for p in range(taps_blocks):
                a = m - p
                if 0 <= a < out_blocks:
                    h_ref[slot, p * 128 : (p + 1) * 128, a * 128 : (a + 1) * 128] = window
        energy = jnp.concatenate(
            [sum(squares[a + p] for p in range(taps_blocks)) for a in range(out_blocks)], axis=1
        )
        start = pl.multiple_of(c * width, 128)
        part = jnp.dot(n_ref[:, pl.ds(start, width)], h_ref[slot], preferred_element_type=jnp.float32)
        return acc + part * (1.0 / jnp.sqrt(jnp.maximum(energy, 1.0)))

    def two_channels(i, acc):
        acc = one_channel(2 * i, 0, acc)
        return one_channel(2 * i + 1, 1, acc)

    acc = jnp.zeros(o_ref.shape, jnp.float32)
    if channels <= 16:
        for c in range(channels):
            acc = one_channel(c, c % 2, acc)
    else:
        pairs = channels // 2
        acc = lax.fori_loop(0, pairs, two_channels, acc, unroll=2 if pairs % 2 == 0 else 1)
        if channels % 2:
            acc = one_channel(channels - 1, 0, acc)
    o_ref[...] = acc


def reverse_blocks(rows):
    shape = rows.shape
    return rows.reshape(shape[:-1] + (shape[-1] // 128, 128))[..., ::-1].reshape(shape)


def unflip(stacked):
    rows, seg_len = stacked.shape
    return stacked.reshape(rows, seg_len // 128, 128)[..., ::-1].reshape(rows, seg_len)


def correlate(normed, flat_owned, seg_len):
    rows, channels, filter_taps = normed.shape
    blocks = flat_owned.reshape(channels * (flat_owned.shape[1] // 128), 128)
    return pl.pallas_call(
        hankel_kernel,
        out_shape=jax.ShapeDtypeStruct((rows, seg_len), jnp.float32),
        scratch_shapes=[pltpu.VMEM((2, filter_taps, seg_len), jnp.bfloat16)],
    )(blocks, normed.reshape(rows, channels * filter_taps))


def ordered_sum(part, axis):
    size = lax.axis_size(axis)
    if size & (size - 1) == 0:
        step = 1
        while step < size:
            part = part + lax.ppermute(part, axis, [(i, i ^ step) for i in range(size)])
            step *= 2
        return part
    me = lax.axis_index(axis)
    received = [part] + [
        lax.ppermute(part, axis, [(i, (i + k) % size) for i in range(size)]) for k in range(1, size)
    ]
    order = (me - jnp.arange(size, dtype=jnp.int32)) % size
    return jnp.sum(jnp.take(jnp.stack(received), order, axis=0), axis=0)


def gather_owned(records, station_region, capacity, filter_taps):
    local_count, components, seg_len = records.shape
    regions = lax.axis_size("region")
    segs = lax.axis_size("seg")
    ahead = lax.ppermute(
        records[:, :, :filter_taps], "seg", [(s + 1, s) for s in range(segs - 1)]
    )
    tag = jnp.broadcast_to(station_region.astype(jnp.bfloat16)[:, None, None], (local_count, 1, seg_len + filter_taps))
    window = jnp.concatenate([reverse_blocks(records), reverse_blocks(ahead)], axis=2)
    payload = jnp.concatenate([window, tag], axis=1)
    me = lax.axis_index("region")
    stations = regions * local_count
    if regions & (regions - 1) == 0:
        here = payload
        step = 1
        while step < regions:
            theirs = lax.ppermute(here, "region", [(r, r ^ step) for r in range(regions)])
            here = jnp.concatenate([here, theirs], axis=0)
            step *= 2
        source = me ^ jnp.arange(regions, dtype=jnp.int32)[:, None]
    else:
        gathered = [payload] + [
            lax.ppermute(payload, "region", [(r, (r + k) % regions) for r in range(regions)])
            for k in range(1, regions)
        ]
        here = jnp.concatenate(gathered, axis=0)
        source = (me - jnp.arange(regions, dtype=jnp.int32)[:, None]) % regions
    local = jnp.arange(local_count, dtype=jnp.int32)[None, :]
    station_ids = (source * local_count + local).reshape(stations)
    region_of = here[:, components, 0].astype(jnp.int32)
    rows = here[:, :components, :]
    earlier = (region_of[None, :] == region_of[:, None]) & (station_ids[None, :] < station_ids[:, None])
    ranks = jnp.sum(earlier.astype(jnp.int32), axis=1)
    slot_index = jnp.arange(capacity, dtype=jnp.int32)
    placing = (region_of[None, :] == me) & (ranks[None, :] == slot_index[:, None])
    owned_rows = jnp.dot(
        placing.astype(jnp.bfloat16), rows.reshape(stations, -1), preferred_element_type=jnp.float32
    ).astype(jnp.bfloat16)
    owned_rows = owned_rows.reshape(capacity, components, seg_len + filter_taps)
    filled = jnp.sum(placing.astype(jnp.float32), axis=1)
    return owned_rows, filled


def per_device(records, templates, channel_mask, station_region):
    local_batches, kept, capacity, components, filter_taps = templates.shape
    seg_len = records.shape[2]
    owned_rows, filled = gather_owned(records, station_region, capacity, filter_taps)
    owned_rows = owned_rows.astype(jnp.float32) * filled[:, None, None]
    flat_owned = owned_rows.reshape(capacity * components, seg_len + filter_taps)
    weight = channel_mask.astype(jnp.float32)
    widened_templates = templates.astype(jnp.float32)
    template_norm = jnp.sqrt(
        jnp.sum(widened_templates * widened_templates, axis=4, keepdims=True) + 1e-06
    )
    normed = (widened_templates * weight[..., None] / template_norm).astype(jnp.bfloat16)
    normed = normed.reshape(local_batches * kept, capacity * components, filter_taps)
    total_len = seg_len * lax.axis_size("seg")
    stacked = ordered_sum(correlate(normed, flat_owned, seg_len), "region")
    power_sum = ordered_sum(jnp.sum(stacked * stacked, axis=1), "seg")
    detect = unflip(stacked) / jnp.sqrt(power_sum / total_len + 1e-06)[:, None]
    return detect.reshape(local_batches, kept, seg_len)


def solution(mesh):
    placed = (
        P(("groups", "region"), None, "seg"),
        P(("groups", "tb"), None, "region", None, None),
        P(("groups", "tb"), None, "region", None),
        P(("groups", "region")),
    )
    return jax.shard_map(
        per_device,
        mesh=mesh,
        in_specs=placed,
        out_specs=P(("groups", "tb"), None, "seg"),
        check_vma=False,
    )
```

```python
import jax
import jax.numpy as jnp
from jax import lax
from jax.sharding import PartitionSpec as P
from jax.experimental import pallas as pl
from jax.experimental.pallas import tpu as pltpu


def hankel_kernel(x_ref, n_ref, o_ref, h_ref):
    width = h_ref.shape[1]
    channels = n_ref.shape[1] // width
    taps_blocks = width // 128
    out_blocks = o_ref.shape[1] // 128
    blocks = taps_blocks + out_blocks
    row = lax.broadcasted_iota(jnp.int32, (128, 128), 0)
    lane = lax.broadcasted_iota(jnp.int32, (128, 128), 1)
    low = lane >= row

    def one_channel(c, slot, acc):
        rolled = [
            pltpu.roll(x_ref[pl.ds(c * blocks + m, 128, stride=0), :], 0, 1, stride=1, stride_axis=0)
            for m in range(blocks)
        ]
        squares = []
        for m in range(blocks - 1):
            window = jnp.where(low, rolled[m], rolled[m + 1])
            squares.append(jnp.sum(window * window, axis=0, keepdims=True))
            window = window.astype(jnp.bfloat16)
            for p in range(taps_blocks):
                a = m - p
                if 0 <= a < out_blocks:
                    h_ref[slot, p * 128 : (p + 1) * 128, a * 128 : (a + 1) * 128] = window
        energy = jnp.concatenate(
            [sum(squares[a + p] for p in range(taps_blocks)) for a in range(out_blocks)], axis=1
        )
        start = pl.multiple_of(c * width, 128)
        part = jnp.dot(n_ref[:, pl.ds(start, width)], h_ref[slot], preferred_element_type=jnp.float32)
        return acc + part * (1.0 / jnp.sqrt(jnp.maximum(energy, 1.0)))

    def two_channels(i, acc):
        acc = one_channel(2 * i, 0, acc)
        return one_channel(2 * i + 1, 1, acc)

    acc = jnp.zeros(o_ref.shape, jnp.float32)
    if channels <= 16:
        for c in range(channels):
            acc = one_channel(c, c % 2, acc)
    else:
        pairs = channels // 2
        acc = lax.fori_loop(0, pairs, two_channels, acc, unroll=2 if pairs % 2 == 0 else 1)
        if channels % 2:
            acc = one_channel(channels - 1, 0, acc)
    o_ref[...] = acc


def unflip(stacked):
    rows, seg_len = stacked.shape
    return stacked.reshape(rows, seg_len // 128, 128)[..., ::-1].reshape(rows, seg_len)


def correlate(normed, flat_owned, seg_len):
    rows, channels, filter_taps = normed.shape
    blocks = flat_owned.reshape(channels * (flat_owned.shape[1] // 128), 128)[:, ::-1]
    return pl.pallas_call(
        hankel_kernel,
        out_shape=jax.ShapeDtypeStruct((rows, seg_len), jnp.float32),
        scratch_shapes=[pltpu.VMEM((2, filter_taps, seg_len), jnp.bfloat16)],
    )(blocks, normed.reshape(rows, channels * filter_taps))


def ordered_sum(part, axis):
    size = lax.axis_size(axis)
    if size & (size - 1) == 0:
        step = 1
        while step < size:
            part = part + lax.ppermute(part, axis, [(i, i ^ step) for i in range(size)])
            step *= 2
        return part
    me = lax.axis_index(axis)
    received = [part] + [
        lax.ppermute(part, axis, [(i, (i + k) % size) for i in range(size)]) for k in range(1, size)
    ]
    order = (me - jnp.arange(size, dtype=jnp.int32)) % size
    return jnp.sum(jnp.take(jnp.stack(received), order, axis=0), axis=0)


def region_sum(part):
    regions = lax.axis_size("region")
    cores = lax.axis_size("tb")
    if regions & (regions - 1) or cores != 2:
        return ordered_sum(part, "region")
    steps = []
    step = 1
    while step < regions:
        steps.append(step)
        step *= 2
    for first, second in zip(steps, steps[::-1]):
        pairs = [(r * 2, (r ^ first) * 2) for r in range(regions)]
        pairs += [(r * 2 + 1, (r ^ second) * 2 + 1) for r in range(regions)]
        part = part + lax.ppermute(part, ("region", "tb"), pairs)
    return part


def gather_owned(records, station_region, capacity, filter_taps):
    local_count, components, seg_len = records.shape
    regions = lax.axis_size("region")
    segs = lax.axis_size("seg")
    ahead = lax.ppermute(
        records[:, :, :filter_taps], "seg", [(s + 1, s) for s in range(segs - 1)]
    )
    tag = jnp.broadcast_to(station_region.astype(jnp.bfloat16)[:, None, None], (local_count, 1, seg_len + filter_taps))
    payload = jnp.concatenate(
        [jnp.concatenate([records, ahead], axis=2), tag], axis=1
    )
    me = lax.axis_index("region")
    stations = regions * local_count
    if regions & (regions - 1) == 0:
        here = payload
        step = 1
        while step < regions:
            theirs = lax.ppermute(here, "region", [(r, r ^ step) for r in range(regions)])
            here = jnp.concatenate([here, theirs], axis=0)
            step *= 2
        source = me ^ jnp.arange(regions, dtype=jnp.int32)[:, None]
    else:
        gathered = [payload] + [
            lax.ppermute(payload, "region", [(r, (r + k) % regions) for r in range(regions)])
            for k in range(1, regions)
        ]
        here = jnp.concatenate(gathered, axis=0)
        source = (me - jnp.arange(regions, dtype=jnp.int32)[:, None]) % regions
    local = jnp.arange(local_count, dtype=jnp.int32)[None, :]
    station_ids = (source * local_count + local).reshape(stations)
    region_of = here[:, components, 0].astype(jnp.int32)
    rows = here[:, :components, :]
    earlier = (region_of[None, :] == region_of[:, None]) & (station_ids[None, :] < station_ids[:, None])
    ranks = jnp.sum(earlier.astype(jnp.int32), axis=1)
    slot_index = jnp.arange(capacity, dtype=jnp.int32)
    placing = (region_of[None, :] == me) & (ranks[None, :] == slot_index[:, None])
    owned_rows = jnp.dot(
        placing.astype(jnp.bfloat16), rows.reshape(stations, -1), preferred_element_type=jnp.float32
    ).astype(jnp.bfloat16)
    owned_rows = owned_rows.reshape(capacity, components, seg_len + filter_taps)
    filled = jnp.sum(placing.astype(jnp.float32), axis=1)
    return owned_rows, filled


def per_device(records, templates, channel_mask, station_region):
    local_batches, kept, capacity, components, filter_taps = templates.shape
    seg_len = records.shape[2]
    owned_rows, filled = gather_owned(records, station_region, capacity, filter_taps)
    owned_rows = owned_rows.astype(jnp.float32) * filled[:, None, None]
    flat_owned = owned_rows.reshape(capacity * components, seg_len + filter_taps)
    weight = channel_mask.astype(jnp.float32)
    widened_templates = templates.astype(jnp.float32)
    template_norm = jnp.sqrt(
        jnp.sum(widened_templates * widened_templates, axis=4, keepdims=True) + 1e-06
    )
    normed = (widened_templates * weight[..., None] / template_norm).astype(jnp.bfloat16)
    normed = normed.reshape(local_batches * kept, capacity * components, filter_taps)
    total_len = seg_len * lax.axis_size("seg")
    stacked = region_sum(correlate(normed, flat_owned, seg_len))
    power_sum = ordered_sum(jnp.sum(stacked * stacked, axis=1), "seg")
    detect = unflip(stacked) / jnp.sqrt(power_sum / total_len + 1e-06)[:, None]
    return detect.reshape(local_batches, kept, seg_len)


def solution(mesh):
    placed = (
        P(("groups", "region"), None, "seg"),
        P(("groups", "tb"), None, "region", None, None),
        P(("groups", "tb"), None, "region", None),
        P(("groups", "region")),
    )
    return jax.shard_map(
        per_device,
        mesh=mesh,
        in_specs=placed,
        out_specs=P(("groups", "tb"), None, "seg"),
        check_vma=False,
    )
```

```python
import jax
import jax.numpy as jnp
from jax import lax
from jax.sharding import PartitionSpec as P
from jax.experimental import pallas as pl
from jax.experimental.pallas import tpu as pltpu


def hankel_kernel(x_ref, n_ref, o_ref, h_ref):
    width = h_ref.shape[1]
    channels = n_ref.shape[1] // width
    taps_blocks = width // 128
    out_blocks = o_ref.shape[1] // 128
    blocks = taps_blocks + out_blocks
    row = lax.broadcasted_iota(jnp.int32, (128, 128), 0)
    lane = lax.broadcasted_iota(jnp.int32, (128, 128), 1)
    low = lane >= row

    def one_channel(c, slot, acc):
        rolled = [
            pltpu.roll(x_ref[pl.ds(c * blocks + m, 128, stride=0), :], 0, 1, stride=1, stride_axis=0)
            for m in range(blocks)
        ]
        squares = []
        for m in range(blocks - 1):
            window = jnp.where(low, rolled[m], rolled[m + 1])
            squares.append(jnp.sum(window * window, axis=0, keepdims=True))
            window = window.astype(jnp.bfloat16)
            for p in range(taps_blocks):
                a = m - p
                if 0 <= a < out_blocks:
                    h_ref[slot, p * 128 : (p + 1) * 128, a * 128 : (a + 1) * 128] = window
        energy = jnp.concatenate(
            [sum(squares[a + p] for p in range(taps_blocks)) for a in range(out_blocks)], axis=1
        )
        start = pl.multiple_of(c * width, 128)
        part = jnp.dot(n_ref[:, pl.ds(start, width)], h_ref[slot], preferred_element_type=jnp.float32)
        return acc + part * (1.0 / jnp.sqrt(jnp.maximum(energy, 1.0)))

    def two_channels(i, acc):
        acc = one_channel(2 * i, 0, acc)
        return one_channel(2 * i + 1, 1, acc)

    acc = jnp.zeros(o_ref.shape, jnp.float32)
    if channels <= 16:
        for c in range(channels):
            acc = one_channel(c, c % 2, acc)
    else:
        pairs = channels // 2
        acc = lax.fori_loop(0, pairs, two_channels, acc, unroll=2 if pairs % 2 == 0 else 1)
        if channels % 2:
            acc = one_channel(channels - 1, 0, acc)
    o_ref[...] = acc


def unflip(stacked):
    rows, seg_len = stacked.shape
    return stacked.reshape(rows, seg_len // 128, 128)[..., ::-1].reshape(rows, seg_len)


def correlate(normed, flat_owned, seg_len):
    rows, channels, filter_taps = normed.shape
    blocks = flat_owned.reshape(channels * (flat_owned.shape[1] // 128), 128)[:, ::-1]
    return pl.pallas_call(
        hankel_kernel,
        out_shape=jax.ShapeDtypeStruct((rows, seg_len), jnp.float32),
        scratch_shapes=[pltpu.VMEM((2, filter_taps, seg_len), jnp.bfloat16)],
    )(blocks, normed.reshape(rows, channels * filter_taps))


def ordered_sum(part, axis):
    size = lax.axis_size(axis)
    if size & (size - 1) == 0:
        step = 1
        while step < size:
            pairs = [(i, i ^ step) for i in range(size)]
            if part.ndim == 2 and part.shape[1] % 256 == 0:
                half = part.shape[1] // 2
                theirs = jnp.concatenate(
                    [lax.ppermute(part[:, :half], axis, pairs), lax.ppermute(part[:, half:], axis, pairs)],
                    axis=1,
                )
            else:
                theirs = lax.ppermute(part, axis, pairs)
            part = part + theirs
            step *= 2
        return part
    me = lax.axis_index(axis)
    received = [part] + [
        lax.ppermute(part, axis, [(i, (i + k) % size) for i in range(size)]) for k in range(1, size)
    ]
    order = (me - jnp.arange(size, dtype=jnp.int32)) % size
    return jnp.sum(jnp.take(jnp.stack(received), order, axis=0), axis=0)


def gather_owned(records, station_region, capacity, filter_taps):
    local_count, components, seg_len = records.shape
    regions = lax.axis_size("region")
    segs = lax.axis_size("seg")
    ahead = lax.ppermute(
        records[:, :, :filter_taps], "seg", [(s + 1, s) for s in range(segs - 1)]
    )
    tag = jnp.broadcast_to(station_region.astype(jnp.bfloat16)[:, None, None], (local_count, 1, seg_len + filter_taps))
    payload = jnp.concatenate(
        [jnp.concatenate([records, ahead], axis=2), tag], axis=1
    )
    me = lax.axis_index("region")
    stations = regions * local_count
    if regions & (regions - 1) == 0:
        here = payload
        step = 1
        while step < regions:
            theirs = lax.ppermute(here, "region", [(r, r ^ step) for r in range(regions)])
            here = jnp.concatenate([here, theirs], axis=0)
            step *= 2
        source = me ^ jnp.arange(regions, dtype=jnp.int32)[:, None]
    else:
        gathered = [payload] + [
            lax.ppermute(payload, "region", [(r, (r + k) % regions) for r in range(regions)])
            for k in range(1, regions)
        ]
        here = jnp.concatenate(gathered, axis=0)
        source = (me - jnp.arange(regions, dtype=jnp.int32)[:, None]) % regions
    local = jnp.arange(local_count, dtype=jnp.int32)[None, :]
    station_ids = (source * local_count + local).reshape(stations)
    region_of = here[:, components, 0].astype(jnp.int32)
    rows = here[:, :components, :]
    earlier = (region_of[None, :] == region_of[:, None]) & (station_ids[None, :] < station_ids[:, None])
    ranks = jnp.sum(earlier.astype(jnp.int32), axis=1)
    slot_index = jnp.arange(capacity, dtype=jnp.int32)
    placing = (region_of[None, :] == me) & (ranks[None, :] == slot_index[:, None])
    owned_rows = jnp.dot(
        placing.astype(jnp.bfloat16), rows.reshape(stations, -1), preferred_element_type=jnp.float32
    ).astype(jnp.bfloat16)
    owned_rows = owned_rows.reshape(capacity, components, seg_len + filter_taps)
    filled = jnp.sum(placing.astype(jnp.float32), axis=1)
    return owned_rows, filled


def per_device(records, templates, channel_mask, station_region):
    local_batches, kept, capacity, components, filter_taps = templates.shape
    seg_len = records.shape[2]
    owned_rows, filled = gather_owned(records, station_region, capacity, filter_taps)
    owned_rows = owned_rows.astype(jnp.float32) * filled[:, None, None]
    flat_owned = owned_rows.reshape(capacity * components, seg_len + filter_taps)
    weight = channel_mask.astype(jnp.float32)
    widened_templates = templates.astype(jnp.float32)
    template_norm = jnp.sqrt(
        jnp.sum(widened_templates * widened_templates, axis=4, keepdims=True) + 1e-06
    )
    normed = (widened_templates * weight[..., None] / template_norm).astype(jnp.bfloat16)
    normed = normed.reshape(local_batches * kept, capacity * components, filter_taps)
    total_len = seg_len * lax.axis_size("seg")
    stacked = ordered_sum(correlate(normed, flat_owned, seg_len), "region")
    power_sum = ordered_sum(jnp.sum(stacked * stacked, axis=1), "seg")
    detect = unflip(stacked) / jnp.sqrt(power_sum / total_len + 1e-06)[:, None]
    return detect.reshape(local_batches, kept, seg_len)


def solution(mesh):
    placed = (
        P(("groups", "region"), None, "seg"),
        P(("groups", "tb"), None, "region", None, None),
        P(("groups", "tb"), None, "region", None),
        P(("groups", "region")),
    )
    return jax.shard_map(
        per_device,
        mesh=mesh,
        in_specs=placed,
        out_specs=P(("groups", "tb"), None, "seg"),
        check_vma=False,
    )
```

```python
import jax
import jax.numpy as jnp
from jax import lax
from jax.sharding import PartitionSpec as P
from jax.experimental import pallas as pl
from jax.experimental.pallas import tpu as pltpu


def hankel_kernel(x_ref, n_ref, o_ref, h_ref):
    width = h_ref.shape[1]
    channels = n_ref.shape[1] // width
    taps_blocks = width // 128
    out_blocks = o_ref.shape[1] // 128
    blocks = taps_blocks + out_blocks
    row = lax.broadcasted_iota(jnp.int32, (128, 128), 0)
    lane = lax.broadcasted_iota(jnp.int32, (128, 128), 1)
    low = lane >= row

    def one_channel(c, slot, acc):
        rolled = [
            pltpu.roll(x_ref[pl.ds(c * blocks + m, 128, stride=0), :], 0, 1, stride=1, stride_axis=0)
            for m in range(blocks)
        ]
        windows = [jnp.where(low, rolled[m], rolled[m + 1]) for m in range(blocks - 1)]
        squares = [jnp.sum(w * w, axis=0, keepdims=True) for w in windows]
        scale = [
            1.0 / jnp.sqrt(jnp.maximum(sum(squares[a + p] for p in range(taps_blocks)), 1.0))
            for a in range(out_blocks)
        ]
        for p in range(taps_blocks):
            for a in range(out_blocks):
                h_ref[slot, p * 128 : (p + 1) * 128, a * 128 : (a + 1) * 128] = (
                    windows[a + p] * scale[a]
                ).astype(jnp.bfloat16)
        start = pl.multiple_of(c * width, 128)
        return acc + jnp.dot(n_ref[:, pl.ds(start, width)], h_ref[slot], preferred_element_type=jnp.float32)

    def two_channels(i, acc):
        acc = one_channel(2 * i, 0, acc)
        return one_channel(2 * i + 1, 1, acc)

    acc = jnp.zeros(o_ref.shape, jnp.float32)
    if channels <= 16:
        for c in range(channels):
            acc = one_channel(c, c % 2, acc)
    else:
        pairs = channels // 2
        acc = lax.fori_loop(0, pairs, two_channels, acc, unroll=2 if pairs % 2 == 0 else 1)
        if channels % 2:
            acc = one_channel(channels - 1, 0, acc)
    o_ref[...] = acc


def unflip(stacked):
    rows, seg_len = stacked.shape
    return stacked.reshape(rows, seg_len // 128, 128)[..., ::-1].reshape(rows, seg_len)


def correlate(normed, flat_owned, seg_len):
    rows, channels, filter_taps = normed.shape
    blocks = flat_owned.reshape(channels * (flat_owned.shape[1] // 128), 128)[:, ::-1]
    return pl.pallas_call(
        hankel_kernel,
        out_shape=jax.ShapeDtypeStruct((rows, seg_len), jnp.float32),
        scratch_shapes=[pltpu.VMEM((2, filter_taps, seg_len), jnp.bfloat16)],
    )(blocks, normed.reshape(rows, channels * filter_taps))


def ordered_sum(part, axis):
    size = lax.axis_size(axis)
    if size & (size - 1) == 0:
        step = 1
        while step < size:
            part = part + lax.ppermute(part, axis, [(i, i ^ step) for i in range(size)])
            step *= 2
        return part
    me = lax.axis_index(axis)
    received = [part] + [
        lax.ppermute(part, axis, [(i, (i + k) % size) for i in range(size)]) for k in range(1, size)
    ]
    order = (me - jnp.arange(size, dtype=jnp.int32)) % size
    return jnp.sum(jnp.take(jnp.stack(received), order, axis=0), axis=0)


def gather_owned(records, station_region, capacity, filter_taps):
    local_count, components, seg_len = records.shape
    regions = lax.axis_size("region")
    segs = lax.axis_size("seg")
    ahead = lax.ppermute(
        records[:, :, :filter_taps], "seg", [(s + 1, s) for s in range(segs - 1)]
    )
    tag = jnp.broadcast_to(station_region.astype(jnp.bfloat16)[:, None, None], (local_count, 1, seg_len + filter_taps))
    payload = jnp.concatenate(
        [jnp.concatenate([records, ahead], axis=2), tag], axis=1
    )
    me = lax.axis_index("region")
    stations = regions * local_count
    if regions & (regions - 1) == 0:
        here = payload
        step = 1
        while step < regions:
            theirs = lax.ppermute(here, "region", [(r, r ^ step) for r in range(regions)])
            here = jnp.concatenate([here, theirs], axis=0)
            step *= 2
        source = me ^ jnp.arange(regions, dtype=jnp.int32)[:, None]
    else:
        gathered = [payload] + [
            lax.ppermute(payload, "region", [(r, (r + k) % regions) for r in range(regions)])
            for k in range(1, regions)
        ]
        here = jnp.concatenate(gathered, axis=0)
        source = (me - jnp.arange(regions, dtype=jnp.int32)[:, None]) % regions
    local = jnp.arange(local_count, dtype=jnp.int32)[None, :]
    station_ids = (source * local_count + local).reshape(stations)
    region_of = here[:, components, 0].astype(jnp.int32)
    rows = here[:, :components, :]
    earlier = (region_of[None, :] == region_of[:, None]) & (station_ids[None, :] < station_ids[:, None])
    ranks = jnp.sum(earlier.astype(jnp.int32), axis=1)
    slot_index = jnp.arange(capacity, dtype=jnp.int32)
    placing = (region_of[None, :] == me) & (ranks[None, :] == slot_index[:, None])
    owned_rows = jnp.dot(
        placing.astype(jnp.bfloat16), rows.reshape(stations, -1), preferred_element_type=jnp.float32
    ).astype(jnp.bfloat16)
    owned_rows = owned_rows.reshape(capacity, components, seg_len + filter_taps)
    filled = jnp.sum(placing.astype(jnp.float32), axis=1)
    return owned_rows, filled


def per_device(records, templates, channel_mask, station_region):
    local_batches, kept, capacity, components, filter_taps = templates.shape
    seg_len = records.shape[2]
    owned_rows, filled = gather_owned(records, station_region, capacity, filter_taps)
    owned_rows = owned_rows.astype(jnp.float32) * filled[:, None, None]
    flat_owned = owned_rows.reshape(capacity * components, seg_len + filter_taps)
    weight = channel_mask.astype(jnp.float32)
    widened_templates = templates.astype(jnp.float32)
    template_norm = jnp.sqrt(
        jnp.sum(widened_templates * widened_templates, axis=4, keepdims=True) + 1e-06
    )
    normed = (widened_templates * weight[..., None] / template_norm).astype(jnp.bfloat16)
    normed = normed.reshape(local_batches * kept, capacity * components, filter_taps)
    total_len = seg_len * lax.axis_size("seg")
    stacked = ordered_sum(correlate(normed, flat_owned, seg_len), "region")
    power_sum = ordered_sum(jnp.sum(stacked * stacked, axis=1), "seg")
    detect = unflip(stacked) / jnp.sqrt(power_sum / total_len + 1e-06)[:, None]
    return detect.reshape(local_batches, kept, seg_len)


def solution(mesh):
    placed = (
        P(("groups", "region"), None, "seg"),
        P(("groups", "tb"), None, "region", None, None),
        P(("groups", "tb"), None, "region", None),
        P(("groups", "region")),
    )
    return jax.shard_map(
        per_device,
        mesh=mesh,
        in_specs=placed,
        out_specs=P(("groups", "tb"), None, "seg"),
        check_vma=False,
    )
```

```python
import jax
import jax.numpy as jnp
from jax import lax
from jax.sharding import PartitionSpec as P
from jax.experimental import pallas as pl
from jax.experimental.pallas import tpu as pltpu


def hankel_kernel(x_ref, n_hbm, o_ref, h_ref, n_ref, copies):
    width = h_ref.shape[1]
    channels = n_hbm.shape[1] // width

    def fetch(c):
        return pltpu.make_async_copy(
            n_hbm.at[:, pl.ds(c * width, width)], n_ref.at[c % 2], copies.at[c % 2]
        )

    taps_blocks = width // 128
    out_blocks = o_ref.shape[1] // 128
    blocks = taps_blocks + out_blocks
    row = lax.broadcasted_iota(jnp.int32, (128, 128), 0)
    lane = lax.broadcasted_iota(jnp.int32, (128, 128), 1)
    low = lane >= row

    def one_channel(c, slot, acc):
        rolled = [
            pltpu.roll(x_ref[pl.ds(c * blocks + m, 128, stride=0), :], 0, 1, stride=1, stride_axis=0)
            for m in range(blocks)
        ]
        windows = [jnp.where(low, rolled[m], rolled[m + 1]) for m in range(blocks - 1)]
        squares = [jnp.sum(w * w, axis=0, keepdims=True) for w in windows]
        scale = [
            1.0 / jnp.sqrt(jnp.maximum(sum(squares[a + p] for p in range(taps_blocks)), 1.0))
            for a in range(out_blocks)
        ]
        for p in range(taps_blocks):
            for a in range(out_blocks):
                h_ref[slot, p * 128 : (p + 1) * 128, a * 128 : (a + 1) * 128] = (
                    windows[a + p] * scale[a]
                ).astype(jnp.bfloat16)
        fetch(c).wait()
        if c + 1 < channels:
            fetch(c + 1).start()
        return acc + jnp.dot(n_ref[c % 2], h_ref[slot], preferred_element_type=jnp.float32)

    acc = jnp.zeros(o_ref.shape, jnp.float32)
    fetch(0).start()
    for c in range(channels):
        acc = one_channel(c, c % 2, acc)
    o_ref[...] = acc


def unflip(stacked):
    rows, seg_len = stacked.shape
    return stacked.reshape(rows, seg_len // 128, 128)[..., ::-1].reshape(rows, seg_len)


def correlate(normed, flat_owned, seg_len):
    rows, channels, filter_taps = normed.shape
    blocks = flat_owned.reshape(channels * (flat_owned.shape[1] // 128), 128)[:, ::-1]
    return pl.pallas_call(
        hankel_kernel,
        out_shape=jax.ShapeDtypeStruct((rows, seg_len), jnp.float32),
        in_specs=[pl.BlockSpec(memory_space=pltpu.VMEM), pl.BlockSpec(memory_space=pl.ANY)],
        scratch_shapes=[
            pltpu.VMEM((2, filter_taps, seg_len), jnp.bfloat16),
            pltpu.VMEM((2, rows, filter_taps), jnp.bfloat16),
            pltpu.SemaphoreType.DMA((2,)),
        ],
    )(blocks, normed.reshape(rows, channels * filter_taps))


def ordered_sum(part, axis):
    size = lax.axis_size(axis)
    if size & (size - 1) == 0:
        step = 1
        while step < size:
            part = part + lax.ppermute(part, axis, [(i, i ^ step) for i in range(size)])
            step *= 2
        return part
    me = lax.axis_index(axis)
    received = [part] + [
        lax.ppermute(part, axis, [(i, (i + k) % size) for i in range(size)]) for k in range(1, size)
    ]
    order = (me - jnp.arange(size, dtype=jnp.int32)) % size
    return jnp.sum(jnp.take(jnp.stack(received), order, axis=0), axis=0)


def gather_owned(records, station_region, capacity, filter_taps):
    local_count, components, seg_len = records.shape
    regions = lax.axis_size("region")
    segs = lax.axis_size("seg")
    ahead = lax.ppermute(
        records[:, :, :filter_taps], "seg", [(s + 1, s) for s in range(segs - 1)]
    )
    tag = jnp.broadcast_to(station_region.astype(jnp.bfloat16)[:, None, None], (local_count, 1, seg_len + filter_taps))
    payload = jnp.concatenate(
        [jnp.concatenate([records, ahead], axis=2), tag], axis=1
    )
    me = lax.axis_index("region")
    stations = regions * local_count
    if regions & (regions - 1) == 0:
        here = payload
        step = 1
        while step < regions:
            theirs = lax.ppermute(here, "region", [(r, r ^ step) for r in range(regions)])
            here = jnp.concatenate([here, theirs], axis=0)
            step *= 2
        source = me ^ jnp.arange(regions, dtype=jnp.int32)[:, None]
    else:
        gathered = [payload] + [
            lax.ppermute(payload, "region", [(r, (r + k) % regions) for r in range(regions)])
            for k in range(1, regions)
        ]
        here = jnp.concatenate(gathered, axis=0)
        source = (me - jnp.arange(regions, dtype=jnp.int32)[:, None]) % regions
    local = jnp.arange(local_count, dtype=jnp.int32)[None, :]
    station_ids = (source * local_count + local).reshape(stations)
    region_of = here[:, components, 0].astype(jnp.int32)
    rows = here[:, :components, :]
    earlier = (region_of[None, :] == region_of[:, None]) & (station_ids[None, :] < station_ids[:, None])
    ranks = jnp.sum(earlier.astype(jnp.int32), axis=1)
    slot_index = jnp.arange(capacity, dtype=jnp.int32)
    placing = (region_of[None, :] == me) & (ranks[None, :] == slot_index[:, None])
    owned_rows = jnp.dot(
        placing.astype(jnp.bfloat16), rows.reshape(stations, -1), preferred_element_type=jnp.float32
    ).astype(jnp.bfloat16)
    owned_rows = owned_rows.reshape(capacity, components, seg_len + filter_taps)
    filled = jnp.sum(placing.astype(jnp.float32), axis=1)
    return owned_rows, filled


def per_device(records, templates, channel_mask, station_region):
    local_batches, kept, capacity, components, filter_taps = templates.shape
    seg_len = records.shape[2]
    owned_rows, filled = gather_owned(records, station_region, capacity, filter_taps)
    owned_rows = owned_rows.astype(jnp.float32) * filled[:, None, None]
    flat_owned = owned_rows.reshape(capacity * components, seg_len + filter_taps)
    weight = channel_mask.astype(jnp.float32)
    widened_templates = templates.astype(jnp.float32)
    template_norm = jnp.sqrt(
        jnp.sum(widened_templates * widened_templates, axis=4, keepdims=True) + 1e-06
    )
    normed = (widened_templates * weight[..., None] / template_norm).astype(jnp.bfloat16)
    normed = normed.reshape(local_batches * kept, capacity * components, filter_taps)
    total_len = seg_len * lax.axis_size("seg")
    stacked = ordered_sum(correlate(normed, flat_owned, seg_len), "region")
    power_sum = ordered_sum(jnp.sum(stacked * stacked, axis=1), "seg")
    detect = unflip(stacked) / jnp.sqrt(power_sum / total_len + 1e-06)[:, None]
    return detect.reshape(local_batches, kept, seg_len)


def solution(mesh):
    placed = (
        P(("groups", "region"), None, "seg"),
        P(("groups", "tb"), None, "region", None, None),
        P(("groups", "tb"), None, "region", None),
        P(("groups", "region")),
    )
    return jax.shard_map(
        per_device,
        mesh=mesh,
        in_specs=placed,
        out_specs=P(("groups", "tb"), None, "seg"),
        check_vma=False,
    )
```

```python
import jax
import jax.numpy as jnp
from jax import lax
from jax.sharding import PartitionSpec as P
from jax.experimental import pallas as pl
from jax.experimental.pallas import tpu as pltpu


def hankel_kernel(x_ref, n_ref, o_ref, h_ref):
    width = h_ref.shape[1]
    channels = n_ref.shape[1] // width
    taps_blocks = width // 128
    out_blocks = o_ref.shape[1] // 128
    blocks = taps_blocks + out_blocks
    row = lax.broadcasted_iota(jnp.int32, (128, 128), 0)
    lane = lax.broadcasted_iota(jnp.int32, (128, 128), 1)
    low = lane >= row

    components = x_ref.shape[1] // (blocks * 128)

    def one_channel(c, slot, acc):
        station, component = divmod(c, components)
        base = component * blocks * 128
        rolled = [
            pltpu.roll(
                jnp.broadcast_to(x_ref[pl.ds(station, 1), pl.ds(base + m * 128, 128)], (128, 128)),
                0,
                1,
                stride=1,
                stride_axis=0,
            )
            for m in range(blocks)
        ]
        windows = [jnp.where(low, rolled[m], rolled[m + 1]) for m in range(blocks - 1)]
        squares = [jnp.sum(w * w, axis=0, keepdims=True) for w in windows]
        scale = [
            1.0 / jnp.sqrt(jnp.maximum(sum(squares[a + p] for p in range(taps_blocks)), 1.0))
            for a in range(out_blocks)
        ]
        for p in range(taps_blocks):
            for a in range(out_blocks):
                h_ref[slot, p * 128 : (p + 1) * 128, a * 128 : (a + 1) * 128] = (
                    windows[a + p] * scale[a]
                ).astype(jnp.bfloat16)
        start = pl.multiple_of(c * width, 128)
        return acc + jnp.dot(n_ref[:, pl.ds(start, width)], h_ref[slot], preferred_element_type=jnp.float32)

    acc = jnp.zeros(o_ref.shape, jnp.float32)
    for c in range(channels):
        acc = one_channel(c, c % 2, acc)
    o_ref[...] = acc


def reverse_blocks(rows):
    shape = rows.shape
    return rows.reshape(shape[:-1] + (shape[-1] // 128, 128))[..., ::-1].reshape(shape)


def unflip(stacked):
    rows, seg_len = stacked.shape
    return stacked.reshape(rows, seg_len // 128, 128)[..., ::-1].reshape(rows, seg_len)


def correlate(normed, owned, seg_len):
    rows, channels, filter_taps = normed.shape
    return pl.pallas_call(
        hankel_kernel,
        out_shape=jax.ShapeDtypeStruct((rows, seg_len), jnp.float32),
        scratch_shapes=[pltpu.VMEM((2, filter_taps, seg_len), jnp.bfloat16)],
    )(owned, normed.reshape(rows, channels * filter_taps))


def ordered_sum(part, axis):
    size = lax.axis_size(axis)
    if size & (size - 1) == 0:
        step = 1
        while step < size:
            part = part + lax.ppermute(part, axis, [(i, i ^ step) for i in range(size)])
            step *= 2
        return part
    me = lax.axis_index(axis)
    received = [part] + [
        lax.ppermute(part, axis, [(i, (i + k) % size) for i in range(size)]) for k in range(1, size)
    ]
    order = (me - jnp.arange(size, dtype=jnp.int32)) % size
    return jnp.sum(jnp.take(jnp.stack(received), order, axis=0), axis=0)


def gather_owned(records, station_region, capacity, filter_taps):
    local_count, components, seg_len = records.shape
    regions = lax.axis_size("region")
    segs = lax.axis_size("seg")
    ahead = lax.ppermute(
        records[:, :, :filter_taps], "seg", [(s + 1, s) for s in range(segs - 1)]
    )
    tag = jnp.broadcast_to(station_region.astype(jnp.bfloat16)[:, None, None], (local_count, 1, seg_len + filter_taps))
    window = jnp.concatenate([reverse_blocks(records), reverse_blocks(ahead)], axis=2)
    payload = jnp.concatenate([window, tag], axis=1)
    me = lax.axis_index("region")
    stations = regions * local_count
    if regions & (regions - 1) == 0:
        here = payload
        step = 1
        while step < regions:
            theirs = lax.ppermute(here, "region", [(r, r ^ step) for r in range(regions)])
            here = jnp.concatenate([here, theirs], axis=0)
            step *= 2
        source = me ^ jnp.arange(regions, dtype=jnp.int32)[:, None]
    else:
        gathered = [payload] + [
            lax.ppermute(payload, "region", [(r, (r + k) % regions) for r in range(regions)])
            for k in range(1, regions)
        ]
        here = jnp.concatenate(gathered, axis=0)
        source = (me - jnp.arange(regions, dtype=jnp.int32)[:, None]) % regions
    local = jnp.arange(local_count, dtype=jnp.int32)[None, :]
    station_ids = (source * local_count + local).reshape(stations)
    region_of = here[:, components, 0].astype(jnp.int32)
    rows = here[:, :components, :]
    earlier = (region_of[None, :] == region_of[:, None]) & (station_ids[None, :] < station_ids[:, None])
    ranks = jnp.sum(earlier.astype(jnp.int32), axis=1)
    slot_index = jnp.arange(capacity, dtype=jnp.int32)
    placing = (region_of[None, :] == me) & (ranks[None, :] == slot_index[:, None])
    owned_rows = jnp.dot(
        placing.astype(jnp.bfloat16), rows.reshape(stations, -1), preferred_element_type=jnp.float32
    ).astype(jnp.bfloat16)
    owned_rows = owned_rows.reshape(capacity, components, seg_len + filter_taps)
    filled = jnp.sum(placing.astype(jnp.float32), axis=1)
    return owned_rows, filled


def per_device(records, templates, channel_mask, station_region):
    local_batches, kept, capacity, components, filter_taps = templates.shape
    seg_len = records.shape[2]
    owned_rows, filled = gather_owned(records, station_region, capacity, filter_taps)
    owned_rows = owned_rows.astype(jnp.float32) * filled[:, None, None]
    flat_owned = owned_rows.reshape(capacity, components * (seg_len + filter_taps))
    weight = channel_mask.astype(jnp.float32)
    widened_templates = templates.astype(jnp.float32)
    template_norm = jnp.sqrt(
        jnp.sum(widened_templates * widened_templates, axis=4, keepdims=True) + 1e-06
    )
    normed = (widened_templates * weight[..., None] / template_norm).astype(jnp.bfloat16)
    normed = normed.reshape(local_batches * kept, capacity * components, filter_taps)
    total_len = seg_len * lax.axis_size("seg")
    stacked = ordered_sum(correlate(normed, flat_owned, seg_len), "region")
    power_sum = ordered_sum(jnp.sum(stacked * stacked, axis=1), "seg")
    detect = unflip(stacked) / jnp.sqrt(power_sum / total_len + 1e-06)[:, None]
    return detect.reshape(local_batches, kept, seg_len)


def solution(mesh):
    placed = (
        P(("groups", "region"), None, "seg"),
        P(("groups", "tb"), None, "region", None, None),
        P(("groups", "tb"), None, "region", None),
        P(("groups", "region")),
    )
    return jax.shard_map(
        per_device,
        mesh=mesh,
        in_specs=placed,
        out_specs=P(("groups", "tb"), None, "seg"),
        check_vma=False,
    )
```

```python
import jax
import jax.numpy as jnp
from jax import lax
from jax.sharding import PartitionSpec as P
from jax.experimental import pallas as pl
from jax.experimental.pallas import tpu as pltpu


def hankel_kernel(x_ref, n_ref, o_ref, h_ref):
    width = h_ref.shape[1]
    channels = n_ref.shape[1] // width
    taps_blocks = width // 128
    out_blocks = o_ref.shape[1] // 128
    blocks = taps_blocks + out_blocks
    row = lax.broadcasted_iota(jnp.int32, (128, 128), 0)
    lane = lax.broadcasted_iota(jnp.int32, (128, 128), 1)
    low = lane >= row

    def one_channel(c, slot, acc):
        rolled = [
            pltpu.roll(x_ref[pl.ds(c * blocks + m, 128, stride=0), :], 0, 1, stride=1, stride_axis=0)
            for m in range(blocks)
        ]
        windows = [jnp.where(low, rolled[m], rolled[m + 1]) for m in range(blocks - 1)]
        squares = [jnp.sum(w * w, axis=0, keepdims=True) for w in windows]
        scale = [
            1.0 / jnp.sqrt(jnp.maximum(sum(squares[a + p] for p in range(taps_blocks)), 1.0))
            for a in range(out_blocks)
        ]
        for p in range(taps_blocks):
            for a in range(out_blocks):
                h_ref[slot, p * 128 : (p + 1) * 128, a * 128 : (a + 1) * 128] = (
                    windows[a + p] * scale[a]
                ).astype(jnp.bfloat16)
        start = pl.multiple_of(c * width, 128)
        return acc + jnp.dot(n_ref[:, pl.ds(start, width)], h_ref[slot], preferred_element_type=jnp.float32)

    def two_channels(i, acc):
        acc = one_channel(2 * i, 0, acc)
        return one_channel(2 * i + 1, 1, acc)

    acc = jnp.zeros(o_ref.shape, jnp.float32)
    if channels <= 16:
        for c in range(channels):
            acc = one_channel(c, c % 2, acc)
    else:
        pairs = channels // 2
        acc = lax.fori_loop(0, pairs, two_channels, acc, unroll=2 if pairs % 2 == 0 else 1)
        if channels % 2:
            acc = one_channel(channels - 1, 0, acc)
    o_ref[...] = acc


def unflip(stacked):
    rows, seg_len = stacked.shape
    return stacked.reshape(rows, seg_len // 128, 128)[..., ::-1].reshape(rows, seg_len)


def correlate(normed, flat_owned, seg_len):
    rows, channels, filter_taps = normed.shape
    blocks = flat_owned.reshape(channels * (flat_owned.shape[1] // 128), 128)[:, ::-1]
    return pl.pallas_call(
        hankel_kernel,
        out_shape=jax.ShapeDtypeStruct((rows, seg_len), jnp.float32),
        scratch_shapes=[pltpu.VMEM((2, filter_taps, seg_len), jnp.bfloat16)],
    )(blocks, normed.reshape(rows, channels * filter_taps))


def ordered_sum(part, axis):
    size = lax.axis_size(axis)
    if size & (size - 1) == 0:
        step = 1
        while step < size:
            part = part + lax.ppermute(part, axis, [(i, i ^ step) for i in range(size)])
            step *= 2
        return part
    me = lax.axis_index(axis)
    received = [part] + [
        lax.ppermute(part, axis, [(i, (i + k) % size) for i in range(size)]) for k in range(1, size)
    ]
    order = (me - jnp.arange(size, dtype=jnp.int32)) % size
    return jnp.sum(jnp.take(jnp.stack(received), order, axis=0), axis=0)


def sum_and_power(part):
    regions = lax.axis_size("region")
    segs = lax.axis_size("seg")
    if regions & (regions - 1) or regions < 2 or segs != 2:
        stacked = ordered_sum(part, "region")
        return stacked, ordered_sum(jnp.sum(stacked * stacked, axis=1), "seg")
    step = 1
    while step < regions // 2:
        part = part + lax.ppermute(part, "region", [(r, r ^ step) for r in range(regions)])
        step *= 2
    partner = lax.ppermute(part, "region", [(r, r ^ step) for r in range(regions)])
    other = lax.ppermute(part, "seg", [(0, 1), (1, 0)])
    other_partner = lax.ppermute(
        part, ("region", "seg"), [(r * 2 + s, (r ^ step) * 2 + 1 - s) for r in range(regions) for s in range(2)]
    )
    stacked = part + partner
    stacked_other = other + other_partner
    power = jnp.sum(stacked * stacked, axis=1) + jnp.sum(stacked_other * stacked_other, axis=1)
    return stacked, power


def gather_owned(records, station_region, capacity, filter_taps):
    local_count, components, seg_len = records.shape
    regions = lax.axis_size("region")
    segs = lax.axis_size("seg")
    ahead = lax.ppermute(
        records[:, :, :filter_taps], "seg", [(s + 1, s) for s in range(segs - 1)]
    )
    tag = jnp.broadcast_to(station_region.astype(jnp.bfloat16)[:, None, None], (local_count, 1, seg_len + filter_taps))
    payload = jnp.concatenate(
        [jnp.concatenate([records, ahead], axis=2), tag], axis=1
    )
    me = lax.axis_index("region")
    stations = regions * local_count
    if regions & (regions - 1) == 0:
        here = payload
        step = 1
        while step < regions:
            theirs = lax.ppermute(here, "region", [(r, r ^ step) for r in range(regions)])
            here = jnp.concatenate([here, theirs], axis=0)
            step *= 2
        source = me ^ jnp.arange(regions, dtype=jnp.int32)[:, None]
    else:
        gathered = [payload] + [
            lax.ppermute(payload, "region", [(r, (r + k) % regions) for r in range(regions)])
            for k in range(1, regions)
        ]
        here = jnp.concatenate(gathered, axis=0)
        source = (me - jnp.arange(regions, dtype=jnp.int32)[:, None]) % regions
    local = jnp.arange(local_count, dtype=jnp.int32)[None, :]
    station_ids = (source * local_count + local).reshape(stations)
    region_of = here[:, components, 0].astype(jnp.int32)
    rows = here[:, :components, :]
    earlier = (region_of[None, :] == region_of[:, None]) & (station_ids[None, :] < station_ids[:, None])
    ranks = jnp.sum(earlier.astype(jnp.int32), axis=1)
    slot_index = jnp.arange(capacity, dtype=jnp.int32)
    placing = (region_of[None, :] == me) & (ranks[None, :] == slot_index[:, None])
    owned_rows = jnp.dot(
        placing.astype(jnp.bfloat16), rows.reshape(stations, -1), preferred_element_type=jnp.float32
    ).astype(jnp.bfloat16)
    owned_rows = owned_rows.reshape(capacity, components, seg_len + filter_taps)
    filled = jnp.sum(placing.astype(jnp.float32), axis=1)
    return owned_rows, filled


def per_device(records, templates, channel_mask, station_region):
    local_batches, kept, capacity, components, filter_taps = templates.shape
    seg_len = records.shape[2]
    owned_rows, filled = gather_owned(records, station_region, capacity, filter_taps)
    owned_rows = owned_rows.astype(jnp.float32) * filled[:, None, None]
    flat_owned = owned_rows.reshape(capacity * components, seg_len + filter_taps)
    weight = channel_mask.astype(jnp.float32)
    widened_templates = templates.astype(jnp.float32)
    template_norm = jnp.sqrt(
        jnp.sum(widened_templates * widened_templates, axis=4, keepdims=True) + 1e-06
    )
    normed = (widened_templates * weight[..., None] / template_norm).astype(jnp.bfloat16)
    normed = normed.reshape(local_batches * kept, capacity * components, filter_taps)
    total_len = seg_len * lax.axis_size("seg")
    stacked, power_sum = sum_and_power(correlate(normed, flat_owned, seg_len))
    detect = unflip(stacked) / jnp.sqrt(power_sum / total_len + 1e-06)[:, None]
    return detect.reshape(local_batches, kept, seg_len)


def solution(mesh):
    placed = (
        P(("groups", "region"), None, "seg"),
        P(("groups", "tb"), None, "region", None, None),
        P(("groups", "tb"), None, "region", None),
        P(("groups", "region")),
    )
    return jax.shard_map(
        per_device,
        mesh=mesh,
        in_specs=placed,
        out_specs=P(("groups", "tb"), None, "seg"),
        check_vma=False,
    )
```

```python
import jax
import jax.numpy as jnp
from jax import lax
from jax.sharding import PartitionSpec as P
from jax.experimental import pallas as pl
from jax.experimental.pallas import tpu as pltpu


def hankel_kernel(x_ref, n_ref, o_ref, h_ref):
    width = h_ref.shape[1]
    channels = n_ref.shape[1] // width
    taps_blocks = width // 128
    out_blocks = o_ref.shape[1] // 128
    blocks = taps_blocks + out_blocks
    row = lax.broadcasted_iota(jnp.int32, (128, 128), 0)
    lane = lax.broadcasted_iota(jnp.int32, (128, 128), 1)
    low = lane >= row

    def one_channel(c, slot, acc):
        rolled = [
            pltpu.roll(x_ref[pl.ds(c * blocks + m, 128, stride=0), :], 0, 1, stride=1, stride_axis=0)
            for m in range(blocks)
        ]
        windows = [jnp.where(low, rolled[m], rolled[m + 1]) for m in range(blocks - 1)]
        squares = [jnp.sum(w * w, axis=0, keepdims=True) for w in windows]
        scale = [
            1.0 / jnp.sqrt(jnp.maximum(sum(squares[a + p] for p in range(taps_blocks)), 1.0))
            for a in range(out_blocks)
        ]
        for p in range(taps_blocks):
            for a in range(out_blocks):
                h_ref[slot, p * 128 : (p + 1) * 128, a * 128 : (a + 1) * 128] = (
                    windows[a + p] * scale[a]
                ).astype(jnp.bfloat16)
        start = pl.multiple_of(c * width, 128)
        return acc + jnp.dot(n_ref[:, pl.ds(start, width)], h_ref[slot], preferred_element_type=jnp.float32)

    def two_channels(i, acc):
        acc = one_channel(2 * i, 0, acc)
        return one_channel(2 * i + 1, 1, acc)

    acc = jnp.zeros(o_ref.shape, jnp.float32)
    if channels <= 16:
        for c in range(channels):
            acc = one_channel(c, c % 2, acc)
    else:
        pairs = channels // 2
        acc = lax.fori_loop(0, pairs, two_channels, acc, unroll=2 if pairs % 2 == 0 else 1)
        if channels % 2:
            acc = one_channel(channels - 1, 0, acc)
    exchange = (row + lane == 127).astype(jnp.bfloat16)
    high = acc.astype(jnp.bfloat16)
    rest = acc - high.astype(jnp.float32)
    middle = rest.astype(jnp.bfloat16)
    low_part = (rest - middle.astype(jnp.float32)).astype(jnp.bfloat16)
    for a in range(out_blocks):
        cols = slice(a * 128, (a + 1) * 128)
        flipped = jnp.dot(high[:, cols], exchange, preferred_element_type=jnp.float32)
        flipped = flipped + jnp.dot(middle[:, cols], exchange, preferred_element_type=jnp.float32)
        flipped = flipped + jnp.dot(low_part[:, cols], exchange, preferred_element_type=jnp.float32)
        o_ref[:, cols] = flipped


def correlate(normed, flat_owned, seg_len):
    rows, channels, filter_taps = normed.shape
    blocks = flat_owned.reshape(channels * (flat_owned.shape[1] // 128), 128)[:, ::-1]
    return pl.pallas_call(
        hankel_kernel,
        out_shape=jax.ShapeDtypeStruct((rows, seg_len), jnp.float32),
        scratch_shapes=[pltpu.VMEM((2, filter_taps, seg_len), jnp.bfloat16)],
    )(blocks, normed.reshape(rows, channels * filter_taps))


def ordered_sum(part, axis):
    size = lax.axis_size(axis)
    if size & (size - 1) == 0:
        step = 1
        while step < size:
            part = part + lax.ppermute(part, axis, [(i, i ^ step) for i in range(size)])
            step *= 2
        return part
    me = lax.axis_index(axis)
    received = [part] + [
        lax.ppermute(part, axis, [(i, (i + k) % size) for i in range(size)]) for k in range(1, size)
    ]
    order = (me - jnp.arange(size, dtype=jnp.int32)) % size
    return jnp.sum(jnp.take(jnp.stack(received), order, axis=0), axis=0)


def gather_owned(records, station_region, capacity, filter_taps):
    local_count, components, seg_len = records.shape
    regions = lax.axis_size("region")
    segs = lax.axis_size("seg")
    ahead = lax.ppermute(
        records[:, :, :filter_taps], "seg", [(s + 1, s) for s in range(segs - 1)]
    )
    tag = jnp.broadcast_to(station_region.astype(jnp.bfloat16)[:, None, None], (local_count, 1, seg_len + filter_taps))
    payload = jnp.concatenate(
        [jnp.concatenate([records, ahead], axis=2), tag], axis=1
    )
    me = lax.axis_index("region")
    stations = regions * local_count
    if regions & (regions - 1) == 0:
        here = payload
        step = 1
        while step < regions:
            theirs = lax.ppermute(here, "region", [(r, r ^ step) for r in range(regions)])
            here = jnp.concatenate([here, theirs], axis=0)
            step *= 2
        source = me ^ jnp.arange(regions, dtype=jnp.int32)[:, None]
    else:
        gathered = [payload] + [
            lax.ppermute(payload, "region", [(r, (r + k) % regions) for r in range(regions)])
            for k in range(1, regions)
        ]
        here = jnp.concatenate(gathered, axis=0)
        source = (me - jnp.arange(regions, dtype=jnp.int32)[:, None]) % regions
    local = jnp.arange(local_count, dtype=jnp.int32)[None, :]
    station_ids = (source * local_count + local).reshape(stations)
    region_of = here[:, components, 0].astype(jnp.int32)
    rows = here[:, :components, :]
    earlier = (region_of[None, :] == region_of[:, None]) & (station_ids[None, :] < station_ids[:, None])
    ranks = jnp.sum(earlier.astype(jnp.int32), axis=1)
    slot_index = jnp.arange(capacity, dtype=jnp.int32)
    placing = (region_of[None, :] == me) & (ranks[None, :] == slot_index[:, None])
    owned_rows = jnp.dot(
        placing.astype(jnp.bfloat16), rows.reshape(stations, -1), preferred_element_type=jnp.float32
    ).astype(jnp.bfloat16)
    owned_rows = owned_rows.reshape(capacity, components, seg_len + filter_taps)
    filled = jnp.sum(placing.astype(jnp.float32), axis=1)
    return owned_rows, filled


def per_device(records, templates, channel_mask, station_region):
    local_batches, kept, capacity, components, filter_taps = templates.shape
    seg_len = records.shape[2]
    owned_rows, filled = gather_owned(records, station_region, capacity, filter_taps)
    owned_rows = owned_rows.astype(jnp.float32) * filled[:, None, None]
    flat_owned = owned_rows.reshape(capacity * components, seg_len + filter_taps)
    weight = channel_mask.astype(jnp.float32)
    widened_templates = templates.astype(jnp.float32)
    template_norm = jnp.sqrt(
        jnp.sum(widened_templates * widened_templates, axis=4, keepdims=True) + 1e-06
    )
    normed = (widened_templates * weight[..., None] / template_norm).astype(jnp.bfloat16)
    normed = normed.reshape(local_batches * kept, capacity * components, filter_taps)
    total_len = seg_len * lax.axis_size("seg")
    stacked = ordered_sum(correlate(normed, flat_owned, seg_len), "region")
    power_sum = ordered_sum(jnp.sum(stacked * stacked, axis=1), "seg")
    detect = stacked / jnp.sqrt(power_sum / total_len + 1e-06)[:, None]
    return detect.reshape(local_batches, kept, seg_len)


def solution(mesh):
    placed = (
        P(("groups", "region"), None, "seg"),
        P(("groups", "tb"), None, "region", None, None),
        P(("groups", "tb"), None, "region", None),
        P(("groups", "region")),
    )
    return jax.shard_map(
        per_device,
        mesh=mesh,
        in_specs=placed,
        out_specs=P(("groups", "tb"), None, "seg"),
        check_vma=False,
    )
```

```python
import jax
import jax.numpy as jnp
from jax import lax
from jax.sharding import PartitionSpec as P
from jax.experimental import pallas as pl
from jax.experimental.pallas import tpu as pltpu


def hankel_kernel(x_ref, n_ref, o_ref, h_ref):
    width = h_ref.shape[1]
    channels = n_ref.shape[1] // width
    taps_blocks = width // 128
    out_blocks = o_ref.shape[1] // 128
    blocks = taps_blocks + out_blocks
    row = lax.broadcasted_iota(jnp.int32, (128, 128), 0)
    lane = lax.broadcasted_iota(jnp.int32, (128, 128), 1)
    low = lane >= row

    def one_channel(c, slot, acc):
        rolled = [
            pltpu.roll(x_ref[pl.ds(c * blocks + m, 128, stride=0), :], 0, 1, stride=1, stride_axis=0)
            for m in range(blocks)
        ]
        windows = [jnp.where(low, rolled[m], rolled[m + 1]) for m in range(blocks - 1)]
        squares = [jnp.sum(w * w, axis=0, keepdims=True) for w in windows]
        scale = [
            1.0 / jnp.sqrt(jnp.maximum(sum(squares[a + p] for p in range(taps_blocks)), 1.0))
            for a in range(out_blocks)
        ]
        for p in range(taps_blocks):
            for a in range(out_blocks):
                h_ref[slot, p * 128 : (p + 1) * 128, a * 128 : (a + 1) * 128] = (
                    windows[a + p] * scale[a]
                ).astype(jnp.bfloat16)
        start = pl.multiple_of(c * width, 128)
        return acc + jnp.dot(n_ref[:, pl.ds(start, width)], h_ref[slot], preferred_element_type=jnp.float32)

    def two_channels(i, acc):
        acc = one_channel(2 * i, 0, acc)
        return one_channel(2 * i + 1, 1, acc)

    acc = jnp.zeros(o_ref.shape, jnp.float32)
    if channels <= 16:
        for c in range(channels):
            acc = one_channel(c, c % 2, acc)
    else:
        pairs = channels // 2
        acc = lax.fori_loop(0, pairs, two_channels, acc, unroll=2 if pairs % 2 == 0 else 1)
        if channels % 2:
            acc = one_channel(channels - 1, 0, acc)
    o_ref[...] = acc


def unflip(stacked):
    rows, seg_len = stacked.shape
    return stacked.reshape(rows, seg_len // 128, 128)[..., ::-1].reshape(rows, seg_len)


def correlate(normed, flat_owned, seg_len):
    rows, channels, filter_taps = normed.shape
    blocks = flat_owned.reshape(channels * (flat_owned.shape[1] // 128), 128)[:, ::-1]
    return pl.pallas_call(
        hankel_kernel,
        out_shape=jax.ShapeDtypeStruct((rows, seg_len), jnp.float32),
        scratch_shapes=[pltpu.VMEM((2, filter_taps, seg_len), jnp.bfloat16)],
    )(blocks, normed.reshape(rows, channels * filter_taps))


def ordered_sum(part, axis):
    size = lax.axis_size(axis)
    if size & (size - 1) == 0:
        step = 1
        while step < size:
            part = part + lax.ppermute(part, axis, [(i, i ^ step) for i in range(size)])
            step *= 2
        return part
    me = lax.axis_index(axis)
    received = [part] + [
        lax.ppermute(part, axis, [(i, (i + k) % size) for i in range(size)]) for k in range(1, size)
    ]
    order = (me - jnp.arange(size, dtype=jnp.int32)) % size
    return jnp.sum(jnp.take(jnp.stack(received), order, axis=0), axis=0)


def gather_owned(records, station_region, capacity, filter_taps):
    local_count, components, seg_len = records.shape
    regions = lax.axis_size("region")
    segs = lax.axis_size("seg")
    ahead = lax.ppermute(
        records[:, :, :filter_taps], "seg", [(s + 1, s) for s in range(segs - 1)]
    )
    tag = jnp.broadcast_to(station_region.astype(jnp.bfloat16)[:, None, None], (local_count, 1, seg_len + filter_taps))
    payload = jnp.concatenate(
        [jnp.concatenate([records, ahead], axis=2), tag], axis=1
    )
    me = lax.axis_index("region")
    stations = regions * local_count
    if regions & (regions - 1) == 0:
        here = payload
        step = 1
        while step < regions:
            theirs = lax.ppermute(here, "region", [(r, r ^ step) for r in range(regions)])
            here = jnp.concatenate([here, theirs], axis=0)
            step *= 2
        source = me ^ jnp.arange(regions, dtype=jnp.int32)[:, None]
    else:
        gathered = [payload] + [
            lax.ppermute(payload, "region", [(r, (r + k) % regions) for r in range(regions)])
            for k in range(1, regions)
        ]
        here = jnp.concatenate(gathered, axis=0)
        source = (me - jnp.arange(regions, dtype=jnp.int32)[:, None]) % regions
    local = jnp.arange(local_count, dtype=jnp.int32)[None, :]
    station_ids = (source * local_count + local).reshape(stations)
    region_of = here[:, components, 0].astype(jnp.int32)
    rows = here[:, :components, :]
    earlier = (region_of[None, :] == region_of[:, None]) & (station_ids[None, :] < station_ids[:, None])
    ranks = jnp.sum(earlier.astype(jnp.int32), axis=1)
    slot_index = jnp.arange(capacity, dtype=jnp.int32)
    placing = (region_of[None, :] == me) & (ranks[None, :] == slot_index[:, None])
    owned_rows = jnp.dot(
        placing.astype(jnp.bfloat16), rows.reshape(stations, -1), preferred_element_type=jnp.float32
    ).astype(jnp.bfloat16)
    owned_rows = owned_rows.reshape(capacity, components, seg_len + filter_taps)
    filled = jnp.sum(placing.astype(jnp.float32), axis=1)
    return owned_rows, filled


def per_device(records, templates, channel_mask, station_region):
    local_batches, kept, capacity, components, filter_taps = templates.shape
    seg_len = records.shape[2]
    owned_rows, filled = gather_owned(records, station_region, capacity, filter_taps)
    owned_rows = owned_rows.astype(jnp.float32) * filled[:, None, None]
    flat_owned = owned_rows.reshape(capacity * components, seg_len + filter_taps)
    weight = channel_mask.astype(jnp.float32)
    widened_templates = templates.astype(jnp.float32)
    template_norm = jnp.sqrt(
        jnp.sum(widened_templates * widened_templates, axis=4, keepdims=True) + 1e-06
    )
    normed = (widened_templates * weight[..., None] / template_norm).astype(jnp.bfloat16)
    normed = normed.reshape(local_batches * kept, capacity * components, filter_taps)
    total_len = seg_len * lax.axis_size("seg")
    stacked = ordered_sum(correlate(normed, flat_owned, seg_len), "region")
    power_sum = ordered_sum(jnp.sum(stacked * stacked, axis=1), "seg")
    ordered = lax.optimization_barrier(unflip(stacked))
    detect = ordered / jnp.sqrt(power_sum / total_len + 1e-06)[:, None]
    return detect.reshape(local_batches, kept, seg_len)


def solution(mesh):
    placed = (
        P(("groups", "region"), None, "seg"),
        P(("groups", "tb"), None, "region", None, None),
        P(("groups", "tb"), None, "region", None),
        P(("groups", "region")),
    )
    return jax.shard_map(
        per_device,
        mesh=mesh,
        in_specs=placed,
        out_specs=P(("groups", "tb"), None, "seg"),
        check_vma=False,
    )
```

```python
import jax
import jax.numpy as jnp
from jax import lax
from jax.sharding import PartitionSpec as P
from jax.experimental import pallas as pl
from jax.experimental.pallas import tpu as pltpu


def hankel_kernel(x_ref, n_ref, o_ref, h_ref):
    width = h_ref.shape[1]
    channels = n_ref.shape[1] // width
    taps_blocks = width // 128
    out_blocks = o_ref.shape[1] // 128
    blocks = taps_blocks + out_blocks
    row = lax.broadcasted_iota(jnp.int32, (128, 128), 0)
    lane = lax.broadcasted_iota(jnp.int32, (128, 128), 1)
    low = lane >= row

    def one_channel(c, slot, acc):
        def window(m):
            rolled = [
                pltpu.roll(x_ref[pl.ds(c * blocks + k, 128, stride=0), :], 0, 1, stride=1, stride_axis=0)
                for k in (m, m + 1)
            ]
            return jnp.where(low, rolled[0], rolled[1])

        squares = []
        for m in range(blocks - 1):
            w = window(m)
            squares.append(jnp.sum(w * w, axis=0, keepdims=True))
        scale = [
            1.0 / jnp.sqrt(jnp.maximum(sum(squares[a + p] for p in range(taps_blocks)), 1.0))
            for a in range(out_blocks)
        ]
        for m in range(blocks - 1):
            w = window(m)
            for p in range(taps_blocks):
                a = m - p
                if 0 <= a < out_blocks:
                    h_ref[slot, p * 128 : (p + 1) * 128, a * 128 : (a + 1) * 128] = (w * scale[a]).astype(
                        jnp.bfloat16
                    )
        start = pl.multiple_of(c * width, 128)
        return acc + jnp.dot(n_ref[:, pl.ds(start, width)], h_ref[slot], preferred_element_type=jnp.float32)

    def two_channels(i, acc):
        acc = one_channel(2 * i, 0, acc)
        return one_channel(2 * i + 1, 1, acc)

    acc = jnp.zeros(o_ref.shape, jnp.float32)
    if channels <= 16:
        for c in range(channels):
            acc = one_channel(c, c % 2, acc)
    else:
        pairs = channels // 2
        acc = lax.fori_loop(0, pairs, two_channels, acc, unroll=2 if pairs % 2 == 0 else 1)
        if channels % 2:
            acc = one_channel(channels - 1, 0, acc)
    o_ref[...] = acc


def unflip(stacked):
    rows, seg_len = stacked.shape
    return stacked.reshape(rows, seg_len // 128, 128)[..., ::-1].reshape(rows, seg_len)


def correlate(normed, flat_owned, seg_len):
    rows, channels, filter_taps = normed.shape
    blocks = flat_owned.reshape(channels * (flat_owned.shape[1] // 128), 128)[:, ::-1]
    return pl.pallas_call(
        hankel_kernel,
        out_shape=jax.ShapeDtypeStruct((rows, seg_len), jnp.float32),
        scratch_shapes=[pltpu.VMEM((2, filter_taps, seg_len), jnp.bfloat16)],
    )(blocks, normed.reshape(rows, channels * filter_taps))


def ordered_sum(part, axis):
    size = lax.axis_size(axis)
    if size & (size - 1) == 0:
        step = 1
        while step < size:
            part = part + lax.ppermute(part, axis, [(i, i ^ step) for i in range(size)])
            step *= 2
        return part
    me = lax.axis_index(axis)
    received = [part] + [
        lax.ppermute(part, axis, [(i, (i + k) % size) for i in range(size)]) for k in range(1, size)
    ]
    order = (me - jnp.arange(size, dtype=jnp.int32)) % size
    return jnp.sum(jnp.take(jnp.stack(received), order, axis=0), axis=0)


def gather_owned(records, station_region, capacity, filter_taps):
    local_count, components, seg_len = records.shape
    regions = lax.axis_size("region")
    segs = lax.axis_size("seg")
    ahead = lax.ppermute(
        records[:, :, :filter_taps], "seg", [(s + 1, s) for s in range(segs - 1)]
    )
    tag = jnp.broadcast_to(station_region.astype(jnp.bfloat16)[:, None, None], (local_count, 1, seg_len + filter_taps))
    payload = jnp.concatenate(
        [jnp.concatenate([records, ahead], axis=2), tag], axis=1
    )
    me = lax.axis_index("region")
    stations = regions * local_count
    if regions & (regions - 1) == 0:
        here = payload
        step = 1
        while step < regions:
            theirs = lax.ppermute(here, "region", [(r, r ^ step) for r in range(regions)])
            here = jnp.concatenate([here, theirs], axis=0)
            step *= 2
        source = me ^ jnp.arange(regions, dtype=jnp.int32)[:, None]
    else:
        gathered = [payload] + [
            lax.ppermute(payload, "region", [(r, (r + k) % regions) for r in range(regions)])
            for k in range(1, regions)
        ]
        here = jnp.concatenate(gathered, axis=0)
        source = (me - jnp.arange(regions, dtype=jnp.int32)[:, None]) % regions
    local = jnp.arange(local_count, dtype=jnp.int32)[None, :]
    station_ids = (source * local_count + local).reshape(stations)
    region_of = here[:, components, 0].astype(jnp.int32)
    rows = here[:, :components, :]
    earlier = (region_of[None, :] == region_of[:, None]) & (station_ids[None, :] < station_ids[:, None])
    ranks = jnp.sum(earlier.astype(jnp.int32), axis=1)
    slot_index = jnp.arange(capacity, dtype=jnp.int32)
    placing = (region_of[None, :] == me) & (ranks[None, :] == slot_index[:, None])
    owned_rows = jnp.dot(
        placing.astype(jnp.bfloat16), rows.reshape(stations, -1), preferred_element_type=jnp.float32
    ).astype(jnp.bfloat16)
    owned_rows = owned_rows.reshape(capacity, components, seg_len + filter_taps)
    filled = jnp.sum(placing.astype(jnp.float32), axis=1)
    return owned_rows, filled


def per_device(records, templates, channel_mask, station_region):
    local_batches, kept, capacity, components, filter_taps = templates.shape
    seg_len = records.shape[2]
    owned_rows, filled = gather_owned(records, station_region, capacity, filter_taps)
    owned_rows = owned_rows.astype(jnp.float32) * filled[:, None, None]
    flat_owned = owned_rows.reshape(capacity * components, seg_len + filter_taps)
    weight = channel_mask.astype(jnp.float32)
    widened_templates = templates.astype(jnp.float32)
    template_norm = jnp.sqrt(
        jnp.sum(widened_templates * widened_templates, axis=4, keepdims=True) + 1e-06
    )
    normed = (widened_templates * weight[..., None] / template_norm).astype(jnp.bfloat16)
    normed = normed.reshape(local_batches * kept, capacity * components, filter_taps)
    total_len = seg_len * lax.axis_size("seg")
    stacked = ordered_sum(correlate(normed, flat_owned, seg_len), "region")
    power_sum = ordered_sum(jnp.sum(stacked * stacked, axis=1), "seg")
    detect = unflip(stacked) / jnp.sqrt(power_sum / total_len + 1e-06)[:, None]
    return detect.reshape(local_batches, kept, seg_len)


def solution(mesh):
    placed = (
        P(("groups", "region"), None, "seg"),
        P(("groups", "tb"), None, "region", None, None),
        P(("groups", "tb"), None, "region", None),
        P(("groups", "region")),
    )
    return jax.shard_map(
        per_device,
        mesh=mesh,
        in_specs=placed,
        out_specs=P(("groups", "tb"), None, "seg"),
        check_vma=False,
    )
```

```python
import jax
import jax.numpy as jnp
from jax import lax
from jax.sharding import PartitionSpec as P
from jax.experimental import pallas as pl
from jax.experimental.pallas import tpu as pltpu


def hankel_kernel(x_ref, n_ref, o_ref, h_ref):
    width = h_ref.shape[1]
    channels = n_ref.shape[1] // width
    taps_blocks = width // 128
    out_blocks = o_ref.shape[1] // 128
    blocks = taps_blocks + out_blocks
    row = lax.broadcasted_iota(jnp.int32, (128, 128), 0)
    lane = lax.broadcasted_iota(jnp.int32, (128, 128), 1)
    low = lane >= row

    def one_channel(c, slot, acc):
        rolled = [
            pltpu.roll(x_ref[pl.ds(c * blocks + m, 128, stride=0), :], 0, 1, stride=1, stride_axis=0)
            for m in range(blocks)
        ]
        windows = [jnp.where(low, rolled[m], rolled[m + 1]) for m in range(blocks - 1)]
        squares = [jnp.sum(w * w, axis=0, keepdims=True) for w in windows]
        scale = [
            1.0 / jnp.sqrt(jnp.maximum(sum(squares[a + p] for p in range(taps_blocks)), 1.0))
            for a in range(out_blocks)
        ]
        for p in range(taps_blocks):
            for a in range(out_blocks):
                h_ref[slot, p * 128 : (p + 1) * 128, a * 128 : (a + 1) * 128] = (
                    windows[a + p] * scale[a]
                ).astype(jnp.bfloat16)
        start = pl.multiple_of(c * width, 128)
        return acc + jnp.dot(n_ref[:, pl.ds(start, width)], h_ref[slot], preferred_element_type=jnp.float32)

    def two_channels(i, acc):
        acc = one_channel(2 * i, 0, acc)
        return one_channel(2 * i + 1, 1, acc)

    acc = jnp.zeros(o_ref.shape, jnp.float32)
    if channels <= 2:
        for c in range(channels):
            acc = one_channel(c, c % 2, acc)
    else:
        pairs = channels // 2
        acc = lax.fori_loop(0, pairs, two_channels, acc, unroll=2 if pairs % 2 == 0 else 1)
        if channels % 2:
            acc = one_channel(channels - 1, 0, acc)
    o_ref[...] = acc


def unflip(stacked):
    rows, seg_len = stacked.shape
    return stacked.reshape(rows, seg_len // 128, 128)[..., ::-1].reshape(rows, seg_len)


def correlate(normed, flat_owned, seg_len):
    rows, channels, filter_taps = normed.shape
    blocks = flat_owned.reshape(channels * (flat_owned.shape[1] // 128), 128)[:, ::-1]
    return pl.pallas_call(
        hankel_kernel,
        out_shape=jax.ShapeDtypeStruct((rows, seg_len), jnp.float32),
        scratch_shapes=[pltpu.VMEM((2, filter_taps, seg_len), jnp.bfloat16)],
    )(blocks, normed.reshape(rows, channels * filter_taps))


def ordered_sum(part, axis):
    size = lax.axis_size(axis)
    if size & (size - 1) == 0:
        step = 1
        while step < size:
            part = part + lax.ppermute(part, axis, [(i, i ^ step) for i in range(size)])
            step *= 2
        return part
    me = lax.axis_index(axis)
    received = [part] + [
        lax.ppermute(part, axis, [(i, (i + k) % size) for i in range(size)]) for k in range(1, size)
    ]
    order = (me - jnp.arange(size, dtype=jnp.int32)) % size
    return jnp.sum(jnp.take(jnp.stack(received), order, axis=0), axis=0)


def gather_owned(records, station_region, capacity, filter_taps):
    local_count, components, seg_len = records.shape
    regions = lax.axis_size("region")
    segs = lax.axis_size("seg")
    ahead = lax.ppermute(
        records[:, :, :filter_taps], "seg", [(s + 1, s) for s in range(segs - 1)]
    )
    tag = jnp.broadcast_to(station_region.astype(jnp.bfloat16)[:, None, None], (local_count, 1, seg_len + filter_taps))
    payload = jnp.concatenate(
        [jnp.concatenate([records, ahead], axis=2), tag], axis=1
    )
    me = lax.axis_index("region")
    stations = regions * local_count
    if regions & (regions - 1) == 0:
        here = payload
        step = 1
        while step < regions:
            theirs = lax.ppermute(here, "region", [(r, r ^ step) for r in range(regions)])
            here = jnp.concatenate([here, theirs], axis=0)
            step *= 2
        source = me ^ jnp.arange(regions, dtype=jnp.int32)[:, None]
    else:
        gathered = [payload] + [
            lax.ppermute(payload, "region", [(r, (r + k) % regions) for r in range(regions)])
            for k in range(1, regions)
        ]
        here = jnp.concatenate(gathered, axis=0)
        source = (me - jnp.arange(regions, dtype=jnp.int32)[:, None]) % regions
    local = jnp.arange(local_count, dtype=jnp.int32)[None, :]
    station_ids = (source * local_count + local).reshape(stations)
    region_of = here[:, components, 0].astype(jnp.int32)
    rows = here[:, :components, :]
    earlier = (region_of[None, :] == region_of[:, None]) & (station_ids[None, :] < station_ids[:, None])
    ranks = jnp.sum(earlier.astype(jnp.int32), axis=1)
    slot_index = jnp.arange(capacity, dtype=jnp.int32)
    placing = (region_of[None, :] == me) & (ranks[None, :] == slot_index[:, None])
    owned_rows = jnp.dot(
        placing.astype(jnp.bfloat16), rows.reshape(stations, -1), preferred_element_type=jnp.float32
    ).astype(jnp.bfloat16)
    owned_rows = owned_rows.reshape(capacity, components, seg_len + filter_taps)
    filled = jnp.sum(placing.astype(jnp.float32), axis=1)
    return owned_rows, filled


def per_device(records, templates, channel_mask, station_region):
    local_batches, kept, capacity, components, filter_taps = templates.shape
    seg_len = records.shape[2]
    owned_rows, filled = gather_owned(records, station_region, capacity, filter_taps)
    owned_rows = owned_rows.astype(jnp.float32) * filled[:, None, None]
    flat_owned = owned_rows.reshape(capacity * components, seg_len + filter_taps)
    weight = channel_mask.astype(jnp.float32)
    widened_templates = templates.astype(jnp.float32)
    template_norm = jnp.sqrt(
        jnp.sum(widened_templates * widened_templates, axis=4, keepdims=True) + 1e-06
    )
    normed = (widened_templates * weight[..., None] / template_norm).astype(jnp.bfloat16)
    normed = normed.reshape(local_batches * kept, capacity * components, filter_taps)
    total_len = seg_len * lax.axis_size("seg")
    stacked = ordered_sum(correlate(normed, flat_owned, seg_len), "region")
    power_sum = ordered_sum(jnp.sum(stacked * stacked, axis=1), "seg")
    detect = unflip(stacked) / jnp.sqrt(power_sum / total_len + 1e-06)[:, None]
    return detect.reshape(local_batches, kept, seg_len)


def solution(mesh):
    placed = (
        P(("groups", "region"), None, "seg"),
        P(("groups", "tb"), None, "region", None, None),
        P(("groups", "tb"), None, "region", None),
        P(("groups", "region")),
    )
    return jax.shard_map(
        per_device,
        mesh=mesh,
        in_specs=placed,
        out_specs=P(("groups", "tb"), None, "seg"),
        check_vma=False,
    )
```

```python
import jax
import jax.numpy as jnp
from jax import lax
from jax.sharding import PartitionSpec as P
from jax.experimental import pallas as pl
from jax.experimental.pallas import tpu as pltpu


def hankel_kernel(x_ref, n_ref, o_ref, h_ref):
    width = h_ref.shape[1]
    channels = n_ref.shape[1] // width
    taps_blocks = width // 128
    out_blocks = o_ref.shape[1] // 128
    blocks = taps_blocks + out_blocks
    row = lax.broadcasted_iota(jnp.int32, (128, 128), 0)
    lane = lax.broadcasted_iota(jnp.int32, (128, 128), 1)
    low = lane >= row

    def one_channel(c, slot, acc):
        rolled = [
            pltpu.roll(x_ref[pl.ds(c * blocks + m, 128, stride=0), :], 0, 1, stride=1, stride_axis=0)
            for m in range(blocks)
        ]
        windows = [jnp.where(low, rolled[m], rolled[m + 1]) for m in range(blocks - 1)]
        squares = [jnp.sum(w * w, axis=0, keepdims=True) for w in windows]
        scale = [
            1.0 / jnp.sqrt(jnp.maximum(sum(squares[a + p] for p in range(taps_blocks)), 1.0))
            for a in range(out_blocks)
        ]
        for p in range(taps_blocks):
            for a in range(out_blocks):
                h_ref[slot, p * 128 : (p + 1) * 128, a * 128 : (a + 1) * 128] = (
                    windows[a + p] * scale[a]
                ).astype(jnp.bfloat16)
        start = pl.multiple_of(c * width, 128)
        return acc + jnp.dot(n_ref[:, pl.ds(start, width)], h_ref[slot], preferred_element_type=jnp.float32)

    def two_channels(i, acc):
        acc = one_channel(2 * i, 0, acc)
        return one_channel(2 * i + 1, 1, acc)

    acc = jnp.zeros(o_ref.shape, jnp.float32)
    if channels <= 16:
        for c in range(channels):
            acc = one_channel(c, c % 3, acc)
    else:
        pairs = channels // 2
        acc = lax.fori_loop(0, pairs, two_channels, acc, unroll=2 if pairs % 2 == 0 else 1)
        if channels % 2:
            acc = one_channel(channels - 1, 0, acc)
    o_ref[...] = acc


def unflip(stacked):
    rows, seg_len = stacked.shape
    return stacked.reshape(rows, seg_len // 128, 128)[..., ::-1].reshape(rows, seg_len)


def correlate(normed, flat_owned, seg_len):
    rows, channels, filter_taps = normed.shape
    blocks = flat_owned.reshape(channels * (flat_owned.shape[1] // 128), 128)[:, ::-1]
    return pl.pallas_call(
        hankel_kernel,
        out_shape=jax.ShapeDtypeStruct((rows, seg_len), jnp.float32),
        scratch_shapes=[pltpu.VMEM((3, filter_taps, seg_len), jnp.bfloat16)],
    )(blocks, normed.reshape(rows, channels * filter_taps))


def ordered_sum(part, axis):
    size = lax.axis_size(axis)
    if size & (size - 1) == 0:
        step = 1
        while step < size:
            part = part + lax.ppermute(part, axis, [(i, i ^ step) for i in range(size)])
            step *= 2
        return part
    me = lax.axis_index(axis)
    received = [part] + [
        lax.ppermute(part, axis, [(i, (i + k) % size) for i in range(size)]) for k in range(1, size)
    ]
    order = (me - jnp.arange(size, dtype=jnp.int32)) % size
    return jnp.sum(jnp.take(jnp.stack(received), order, axis=0), axis=0)


def gather_owned(records, station_region, capacity, filter_taps):
    local_count, components, seg_len = records.shape
    regions = lax.axis_size("region")
    segs = lax.axis_size("seg")
    ahead = lax.ppermute(
        records[:, :, :filter_taps], "seg", [(s + 1, s) for s in range(segs - 1)]
    )
    tag = jnp.broadcast_to(station_region.astype(jnp.bfloat16)[:, None, None], (local_count, 1, seg_len + filter_taps))
    payload = jnp.concatenate(
        [jnp.concatenate([records, ahead], axis=2), tag], axis=1
    )
    me = lax.axis_index("region")
    stations = regions * local_count
    if regions & (regions - 1) == 0:
        here = payload
        step = 1
        while step < regions:
            theirs = lax.ppermute(here, "region", [(r, r ^ step) for r in range(regions)])
            here = jnp.concatenate([here, theirs], axis=0)
            step *= 2
        source = me ^ jnp.arange(regions, dtype=jnp.int32)[:, None]
    else:
        gathered = [payload] + [
            lax.ppermute(payload, "region", [(r, (r + k) % regions) for r in range(regions)])
            for k in range(1, regions)
        ]
        here = jnp.concatenate(gathered, axis=0)
        source = (me - jnp.arange(regions, dtype=jnp.int32)[:, None]) % regions
    local = jnp.arange(local_count, dtype=jnp.int32)[None, :]
    station_ids = (source * local_count + local).reshape(stations)
    region_of = here[:, components, 0].astype(jnp.int32)
    rows = here[:, :components, :]
    earlier = (region_of[None, :] == region_of[:, None]) & (station_ids[None, :] < station_ids[:, None])
    ranks = jnp.sum(earlier.astype(jnp.int32), axis=1)
    slot_index = jnp.arange(capacity, dtype=jnp.int32)
    placing = (region_of[None, :] == me) & (ranks[None, :] == slot_index[:, None])
    owned_rows = jnp.dot(
        placing.astype(jnp.bfloat16), rows.reshape(stations, -1), preferred_element_type=jnp.float32
    ).astype(jnp.bfloat16)
    owned_rows = owned_rows.reshape(capacity, components, seg_len + filter_taps)
    filled = jnp.sum(placing.astype(jnp.float32), axis=1)
    return owned_rows, filled


def per_device(records, templates, channel_mask, station_region):
    local_batches, kept, capacity, components, filter_taps = templates.shape
    seg_len = records.shape[2]
    owned_rows, filled = gather_owned(records, station_region, capacity, filter_taps)
    owned_rows = owned_rows.astype(jnp.float32) * filled[:, None, None]
    flat_owned = owned_rows.reshape(capacity * components, seg_len + filter_taps)
    weight = channel_mask.astype(jnp.float32)
    widened_templates = templates.astype(jnp.float32)
    template_norm = jnp.sqrt(
        jnp.sum(widened_templates * widened_templates, axis=4, keepdims=True) + 1e-06
    )
    normed = (widened_templates * weight[..., None] / template_norm).astype(jnp.bfloat16)
    normed = normed.reshape(local_batches * kept, capacity * components, filter_taps)
    total_len = seg_len * lax.axis_size("seg")
    stacked = ordered_sum(correlate(normed, flat_owned, seg_len), "region")
    power_sum = ordered_sum(jnp.sum(stacked * stacked, axis=1), "seg")
    detect = unflip(stacked) / jnp.sqrt(power_sum / total_len + 1e-06)[:, None]
    return detect.reshape(local_batches, kept, seg_len)


def solution(mesh):
    placed = (
        P(("groups", "region"), None, "seg"),
        P(("groups", "tb"), None, "region", None, None),
        P(("groups", "tb"), None, "region", None),
        P(("groups", "region")),
    )
    return jax.shard_map(
        per_device,
        mesh=mesh,
        in_specs=placed,
        out_specs=P(("groups", "tb"), None, "seg"),
        check_vma=False,
    )
```

```python
import jax
import jax.numpy as jnp
from jax import lax
from jax.sharding import PartitionSpec as P
from jax.experimental import pallas as pl
from jax.experimental.pallas import tpu as pltpu


def hankel_kernel(x_ref, n_ref, o_ref, h_ref):
    width = h_ref.shape[1]
    channels = n_ref.shape[1] // width
    taps_blocks = width // 128
    out_blocks = o_ref.shape[1] // 128
    blocks = taps_blocks + out_blocks
    row = lax.broadcasted_iota(jnp.int32, (128, 128), 0)
    lane = lax.broadcasted_iota(jnp.int32, (128, 128), 1)
    low = lane >= row

    def one_channel(c, slot, acc):
        rolled = [
            pltpu.roll(x_ref[pl.ds(c * blocks + m, 128, stride=0), :], 0, 1, stride=1, stride_axis=0)
            for m in range(blocks)
        ]
        windows = [jnp.where(low, rolled[m], rolled[m + 1]) for m in range(blocks - 1)]
        squares = [jnp.sum(w * w, axis=0, keepdims=True) for w in windows]
        scale = [
            1.0 / jnp.sqrt(jnp.maximum(sum(squares[a + p] for p in range(taps_blocks)), 1.0))
            for a in range(out_blocks)
        ]
        for p in range(taps_blocks):
            for a in range(out_blocks):
                h_ref[slot, p * 128 : (p + 1) * 128, a * 128 : (a + 1) * 128] = (
                    windows[a + p] * scale[a]
                ).astype(jnp.bfloat16)
        start = pl.multiple_of(c * width, 128)
        return acc + jnp.dot(n_ref[:, pl.ds(start, width)], h_ref[slot], preferred_element_type=jnp.float32)

    def two_channels(i, acc):
        acc = one_channel(2 * i, 0, acc)
        return one_channel(2 * i + 1, 1, acc)

    acc = jnp.zeros(o_ref.shape, jnp.float32)
    if channels <= 16:
        for c in range(channels):
            acc = one_channel(c, c % 2, acc)
    else:
        pairs = channels // 2
        acc = lax.fori_loop(0, pairs, two_channels, acc, unroll=2 if pairs % 2 == 0 else 1)
        if channels % 2:
            acc = one_channel(channels - 1, 0, acc)
    o_ref[...] = acc


def unflip(stacked):
    rows, seg_len = stacked.shape
    return stacked.reshape(rows, seg_len // 128, 128)[..., ::-1].reshape(rows, seg_len)


def correlate(normed, flat_owned, seg_len):
    rows, channels, filter_taps = normed.shape
    blocks = flat_owned.reshape(channels * (flat_owned.shape[1] // 128), 128)[:, ::-1]
    return pl.pallas_call(
        hankel_kernel,
        out_shape=jax.ShapeDtypeStruct((rows, seg_len), jnp.float32),
        scratch_shapes=[pltpu.VMEM((2, filter_taps, seg_len), jnp.bfloat16)],
    )(blocks, normed.reshape(rows, channels * filter_taps))


def ordered_sum(part, axis):
    size = lax.axis_size(axis)
    if size & (size - 1) == 0:
        step = 1
        while step < size:
            part = part + lax.ppermute(part, axis, [(i, i ^ step) for i in range(size)])
            step *= 2
        return part
    me = lax.axis_index(axis)
    received = [part] + [
        lax.ppermute(part, axis, [(i, (i + k) % size) for i in range(size)]) for k in range(1, size)
    ]
    order = (me - jnp.arange(size, dtype=jnp.int32)) % size
    return jnp.sum(jnp.take(jnp.stack(received), order, axis=0), axis=0)


def gather_owned(records, station_region, capacity, filter_taps):
    local_count, components, seg_len = records.shape
    regions = lax.axis_size("region")
    segs = lax.axis_size("seg")
    ahead = lax.ppermute(
        records[:, :, :filter_taps], "seg", [(s + 1, s) for s in range(segs - 1)]
    )
    tag = jnp.broadcast_to(station_region.astype(jnp.bfloat16)[:, None, None], (local_count, 1, seg_len + filter_taps))
    payload = jnp.concatenate(
        [jnp.concatenate([records, ahead], axis=2), tag], axis=1
    )
    me = lax.axis_index("region")
    stations = regions * local_count
    if regions & (regions - 1) == 0:
        here = payload
        step = 1
        while step < regions:
            theirs = lax.ppermute(here, "region", [(r, r ^ step) for r in range(regions)])
            here = jnp.concatenate([here, theirs], axis=0)
            step *= 2
        source = me ^ jnp.arange(regions, dtype=jnp.int32)[:, None]
    else:
        gathered = [payload] + [
            lax.ppermute(payload, "region", [(r, (r + k) % regions) for r in range(regions)])
            for k in range(1, regions)
        ]
        here = jnp.concatenate(gathered, axis=0)
        source = (me - jnp.arange(regions, dtype=jnp.int32)[:, None]) % regions
    local = jnp.arange(local_count, dtype=jnp.int32)[None, :]
    station_ids = (source * local_count + local).reshape(stations)
    region_of = here[:, components, 0].astype(jnp.int32)
    rows = here[:, :components, :]
    earlier = (region_of[None, :] == region_of[:, None]) & (station_ids[None, :] < station_ids[:, None])
    ranks = jnp.sum(earlier.astype(jnp.int32), axis=1)
    slot_index = jnp.arange(capacity, dtype=jnp.int32)
    placing = (region_of[None, :] == me) & (ranks[None, :] == slot_index[:, None])
    filled = jnp.sum(placing.astype(jnp.float32), axis=1)
    weights = (placing.astype(jnp.float32) * filled[:, None]).astype(jnp.bfloat16)
    owned_rows = jnp.dot(weights, rows.reshape(stations, -1), preferred_element_type=jnp.float32)
    owned_rows = owned_rows.reshape(capacity, components, seg_len + filter_taps)
    return owned_rows, filled


def per_device(records, templates, channel_mask, station_region):
    local_batches, kept, capacity, components, filter_taps = templates.shape
    seg_len = records.shape[2]
    owned_rows, filled = gather_owned(records, station_region, capacity, filter_taps)
    flat_owned = owned_rows.reshape(capacity * components, seg_len + filter_taps)
    weight = channel_mask.astype(jnp.float32)
    widened_templates = templates.astype(jnp.float32)
    template_norm = jnp.sqrt(
        jnp.sum(widened_templates * widened_templates, axis=4, keepdims=True) + 1e-06
    )
    normed = (widened_templates * weight[..., None] / template_norm).astype(jnp.bfloat16)
    normed = normed.reshape(local_batches * kept, capacity * components, filter_taps)
    total_len = seg_len * lax.axis_size("seg")
    stacked = ordered_sum(correlate(normed, flat_owned, seg_len), "region")
    power_sum = ordered_sum(jnp.sum(stacked * stacked, axis=1), "seg")
    detect = unflip(stacked) / jnp.sqrt(power_sum / total_len + 1e-06)[:, None]
    return detect.reshape(local_batches, kept, seg_len)


def solution(mesh):
    placed = (
        P(("groups", "region"), None, "seg"),
        P(("groups", "tb"), None, "region", None, None),
        P(("groups", "tb"), None, "region", None),
        P(("groups", "region")),
    )
    return jax.shard_map(
        per_device,
        mesh=mesh,
        in_specs=placed,
        out_specs=P(("groups", "tb"), None, "seg"),
        check_vma=False,
    )
```
